32 devices in a mesh: parts: 2 (over x), chan: 8 (over z, y), tm: 2 (over core).
Axes of the slice: x: 2, y: 2, z: 4, core: 2. Of those that a mesh axis runs over, the one named last changes fastest.
Arguments:
- records: bfloat16 [8192, 6144], P(('chan', 'tm'), 'parts'), parts along dimension 1, may hold values from -500 to 500
- fir_taps: float32 [32], replicated, may hold values from -1 to 1
- channel_map: int32 [6144], P('parts'), parts along dimension 0, may hold values from 0 to 3071, each once
- source_owner: int32 [4], P('parts'), parts along dimension 0, may hold values from 0 to 7
- source_offset: int32 [4], P('parts'), parts along dimension 0, may hold values from 0 to 368
Outputs:
- correlations: float32 [2, 16, 6144, 512], P(None, None, ('parts', 'chan'), 'tm'), parts along dimension 2
The draws below stay inside these ranges and needn't reach their ends.
There are 2 independent parts, one for each index of `parts`. The reference program is written for one: setup_inputs(seed, part) draws one part's arguments, and reference() takes and returns one part's arrays. A program takes and returns all parts, laid end to end along the dimension named above; an argument that names none is the same for every part. Nothing has to cross between parts.
All inputs are finite; a program needn't handle non-finite values.
Results may differ from the reference program's by a relative error of at most 0.014.
Values may be sent and summed in bfloat16 or wider, within the bound.
No kernel may reach another device: no remote copies, remote signals or barrier semaphores. Data moves between devices by JAX's collectives and lax.ppermute only.
A program may use at most 128 MiB of HBM per device.

```python
import math
import jax
import jax.numpy as jnp
from jax import lax

CB = 384
SRC = 16
STEPS = 2
LAGS = 512
TAPS = 32
STRIDE = 8
HALF_BAND = 32
SAMPLES = 1024
BINS = 512
RAW_LEN = 8192
CHANNELS = 3072
N_CHAN = 8


def draw_records(key, part):
    first_key, column_key, row_key = jax.random.split(key, 3)
    shape = (RAW_LEN, CHANNELS)
    column_scale = jnp.exp(jax.random.uniform(column_key, (1, CHANNELS), jnp.float32, 0.0, math.log(10.0)))
    row_scale = jnp.exp(jax.random.uniform(row_key, (RAW_LEN, 1), jnp.float32, 0.0, math.log(10.0)))
    base_values = jnp.clip(jax.random.normal(first_key, shape, jnp.float32), -4.0, 4.0)
    return (base_values * column_scale * row_scale).astype(jnp.bfloat16)


def normal_values(key, shape, width, limit, kind=jnp.bfloat16):
    entries = jax.random.normal(key, shape, jnp.float32) * width
    return jnp.minimum(jnp.maximum(entries, -limit), limit).astype(kind)


def setup_inputs(seed: int = 0, part: int = 0) -> dict:
    seeds = jax.random.split(jax.random.key(seed), 6)
    part_splits = jax.random.split(jax.random.fold_in(seeds[5], part), 6)
    return {
        "records": draw_records(jax.random.fold_in(jax.random.fold_in(seeds[5], part), 71), part),
        "fir_taps": normal_values(seeds[1], (TAPS,), TAPS ** -0.5, 1.0, jnp.float32),
        "channel_map": jax.random.permutation(part_splits[2], CHANNELS).astype(jnp.int32),
        "source_owner": jax.random.randint(part_splits[3], (STEPS,), 0, N_CHAN).astype(jnp.int32),
        "source_offset": jax.random.randint(part_splits[4], (STEPS,), 0, CB - SRC + 1).astype(jnp.int32),
    }


two_pi = 2.0 * math.pi
epsilon = 1e-06

def decimate(extended, fir_taps, out_rows):
    column_count = extended.shape[1]
    lead_blocks = TAPS // STRIDE
    blocks = extended[:(out_rows + lead_blocks) * STRIDE].astype(jnp.float32)
    blocks = blocks.reshape(out_rows + lead_blocks, STRIDE, column_count)
    summed = jnp.zeros((out_rows, column_count), jnp.float32)
    for lead in range(lead_blocks):
        kernel = fir_taps[lead * STRIDE:(lead + 1) * STRIDE]
        summed = summed + jnp.einsum('nrc,r->nc', blocks[lead:lead + out_rows], kernel, precision=lax.Precision.HIGHEST)
    return summed.astype(jnp.bfloat16)

def spectrum(series):
    samples = series.shape[0]
    bin_count = samples // 2
    block_bins = min(256, bin_count)
    values = series.astype(jnp.float32)
    time_index = jnp.arange(samples, dtype=jnp.int32)

    def one_block(first_bin):
        frequency = first_bin + jnp.arange(block_bins, dtype=jnp.int32)
        phases = time_index[:, None] * frequency[None, :] % samples
        angles = phases.astype(jnp.float32) * (two_pi / samples)
        dims = (((0,), (0,)), ((), ()))
        cosine = lax.dot_general(values, jnp.cos(angles), dims, precision=lax.Precision.HIGHEST)
        sine = lax.dot_general(values, jnp.sin(angles), dims, precision=lax.Precision.HIGHEST)
        return (cosine, -sine)
    firsts = jnp.arange(bin_count // block_bins, dtype=jnp.int32) * block_bins
    real_blocks, imag_blocks = lax.map(one_block, firsts)
    channel_count = series.shape[1]
    real_part = jnp.moveaxis(real_blocks, 0, 1).reshape(channel_count, bin_count)
    imag_part = jnp.moveaxis(imag_blocks, 0, 1).reshape(channel_count, bin_count)
    return (real_part, imag_part)

def whiten(real_part, imag_part):
    powers = real_part * real_part + imag_part * imag_part
    window_span = 2 * HALF_BAND + 1
    window = lax.reduce_window(powers, jnp.array(0.0, powers.dtype), lax.add, (1, window_span), (1, 1), ((0, 0), (HALF_BAND, HALF_BAND)))
    factor = 1.0 / jnp.sqrt(window / window_span + epsilon)
    return jnp.concatenate([real_part * factor, imag_part * factor], axis=1).astype(jnp.bfloat16)

def lag_kernel(samples, first_lag, lag_count):
    bin_count = samples // 2
    frequency = jnp.arange(bin_count, dtype=jnp.int32)
    shifts = first_lag + jnp.arange(lag_count, dtype=jnp.int32) - LAGS // 2
    phases = jnp.mod(frequency[:, None] * shifts[None, :], samples)
    angles = phases.astype(jnp.float32) * (two_pi / samples)
    return jnp.concatenate([jnp.cos(angles), -jnp.sin(angles)], axis=0).astype(jnp.bfloat16)

def reference(records, fir_taps, channel_map, source_owner, source_offset):
    relaid = jnp.take(records, channel_map, axis=1)
    padded = jnp.concatenate([relaid, jnp.zeros((TAPS, CHANNELS), relaid.dtype)], axis=0)
    decimated = decimate(padded, fir_taps, SAMPLES)
    real_part, imag_part = spectrum(decimated)
    whitened = whiten(real_part, imag_part)
    first_rows = source_owner * CB + source_offset
    picked = (first_rows[:, None] + jnp.arange(SRC, dtype=jnp.int32)[None, :]).reshape(-1)
    sources = jnp.take(whitened, picked, axis=0)
    white_values = whitened.astype(jnp.float32)
    kernel_values = lag_kernel(SAMPLES, 0, LAGS).astype(jnp.float32)
    factor = 1.0 / math.sqrt(BINS)

    def per_source(source_row):
        row_values = source_row.astype(jnp.float32)
        real_src = row_values[:BINS][None, :]
        imag_src = row_values[BINS:][None, :]
        real_rcv = white_values[:, :BINS]
        imag_rcv = white_values[:, BINS:]
        cross = jnp.concatenate([real_src * real_rcv + imag_src * imag_rcv, imag_src * real_rcv - real_src * imag_rcv], axis=1).astype(jnp.bfloat16)
        return jnp.dot(cross.astype(jnp.float32), kernel_values, precision=lax.Precision.HIGHEST) * factor
    results = lax.map(per_source, sources)
    return results.reshape(STEPS, SRC, CHANNELS, LAGS)
```

```python
import math

import jax
import jax.numpy as jnp
from jax import lax
from jax.sharding import PartitionSpec as P

SRC = 16
STEPS = 2
LAGS = 512
TAPS = 32
STRIDE = 8
HALF_BAND = 32

two_pi = 2.0 * math.pi
epsilon = 1e-06


def split_bf16(x, parts):
    pieces = []
    rest = x
    for _ in range(parts):
        piece = rest.astype(jnp.bfloat16)
        pieces.append(piece)
        rest = rest - piece.astype(jnp.float32)
    return pieces


def decimation_matrix(fir_taps, out_rows, in_rows):
    rows = jnp.arange(out_rows, dtype=jnp.int32)[:, None]
    cols = jnp.arange(in_rows, dtype=jnp.int32)[None, :]
    tap = cols - rows * STRIDE
    inside = (tap >= 0) & (tap < TAPS)
    picked = jnp.take(fir_taps, jnp.clip(tap, 0, TAPS - 1), mode="clip")
    return jnp.where(inside, picked, 0.0)


def dft_table(samples, bins):
    inner = 32
    outer = samples // inner
    frequency = jnp.arange(bins, dtype=jnp.int32)[None, :]
    low = jnp.arange(inner, dtype=jnp.int32)[:, None]
    high = jnp.arange(outer, dtype=jnp.int32)[:, None] * inner
    scale = two_pi / samples
    low_angle = ((low * frequency) % samples).astype(jnp.float32) * scale
    high_angle = ((high * frequency) % samples).astype(jnp.float32) * scale
    cl, sl = jnp.cos(low_angle)[None], jnp.sin(low_angle)[None]
    ch, sh = jnp.cos(high_angle)[:, None], jnp.sin(high_angle)[:, None]
    cosine = (ch * cl - sh * sl).reshape(samples, bins)
    sine = (sh * cl + ch * sl).reshape(samples, bins)
    return jnp.concatenate([cosine, -sine], axis=1)


def band_matrix(bins):
    g = jnp.arange(bins, dtype=jnp.int32)
    near = jnp.abs(g[:, None] - g[None, :]) <= HALF_BAND
    return near.astype(jnp.bfloat16)


def lag_kernel(samples, first_lag, lag_count):
    bin_count = samples // 2
    frequency = jnp.arange(bin_count, dtype=jnp.int32)
    shifts = first_lag + jnp.arange(lag_count, dtype=jnp.int32) - LAGS // 2
    phases = jnp.mod(frequency[:, None] * shifts[None, :], samples)
    angles = phases.astype(jnp.float32) * (two_pi / samples)
    return jnp.concatenate([jnp.cos(angles), -jnp.sin(angles)], axis=0).astype(jnp.bfloat16)


def whiten_series(series):
    samples = series.shape[0]
    bins = samples // 2
    table = dft_table(samples, bins)
    hi, lo = split_bf16(table, 2)
    dims = (((0,), (0,)), ((), ()))
    both = lax.dot_general(
        series, jnp.concatenate([hi, lo], axis=1), dims, preferred_element_type=jnp.float32
    )
    spectrum = both[:, : 2 * bins] + both[:, 2 * bins :]
    real_part = spectrum[:, :bins]
    imag_part = spectrum[:, bins:]
    powers = real_part * real_part + imag_part * imag_part
    pieces = split_bf16(powers, 3)
    band = band_matrix(bins)
    window = jnp.dot(
        jnp.concatenate(pieces, axis=1),
        jnp.concatenate([band] * 3, axis=0),
        preferred_element_type=jnp.float32,
    )
    window_span = 2 * HALF_BAND + 1
    factor = 1.0 / jnp.sqrt(window / window_span + epsilon)
    return jnp.concatenate([real_part * factor, imag_part * factor], axis=1).astype(jnp.bfloat16)


def local(records, fir_taps, channel_map, source_owner, source_offset):
    n_chan = lax.axis_size("chan")
    n_tm = lax.axis_size("tm")
    n_dev = n_chan * n_tm
    raw_rows, channels = records.shape
    block = channels // n_chan
    out_rows = raw_rows // STRIDE
    halo_rows = TAPS - STRIDE
    samples = out_rows * n_dev

    shift = [(b, b - 1) for b in range(1, n_dev)]
    halo = lax.ppermute(records[:halo_rows], ("chan", "tm"), perm=shift)

    taps_matrix = decimation_matrix(fir_taps, out_rows, raw_rows + halo_rows)
    parts = split_bf16(taps_matrix, 3)
    stacked = jnp.concatenate(parts, axis=0)
    main = jnp.dot(stacked[:, :raw_rows], records, preferred_element_type=jnp.float32)
    tail = jnp.dot(stacked[:, raw_rows:], halo, preferred_element_type=jnp.float32)
    summed = main + tail
    decimated = (
        summed[:out_rows] + summed[out_rows : 2 * out_rows] + summed[2 * out_rows :]
    ).astype(jnp.bfloat16)

    first_rows = source_owner * block + source_offset
    picked = (first_rows[:, None] + jnp.arange(SRC, dtype=jnp.int32)[None, :]).reshape(-1)
    source_raw = jnp.take(channel_map, picked, mode="clip")
    block_raw = channel_map.reshape(n_chan, 1, block)
    block_raw = jnp.broadcast_to(block_raw, (n_chan, n_tm, block)).reshape(n_dev, block)
    index = jnp.concatenate(
        [block_raw, jnp.broadcast_to(source_raw[None], (n_dev, source_raw.shape[0]))], axis=1
    )
    width = index.shape[1]
    columns = jnp.take(decimated, index.reshape(-1), axis=1, mode="clip")
    series = lax.all_to_all(columns, ("chan", "tm"), 1, 0, tiled=True)

    white = whiten_series(series)
    receivers = white[:block]
    sources = white[block:].astype(jnp.float32)
    bins = samples // 2
    real_src = sources[:, :bins][:, :, None]
    imag_src = sources[:, bins:][:, :, None]

    lag_share = LAGS // n_tm
    kernel = lag_kernel(samples, lax.axis_index("tm") * lag_share, lag_share).astype(jnp.float32)
    cosine = kernel[:bins][None]
    sine = kernel[bins:][None]
    mixed = jnp.concatenate(
        [real_src * cosine + imag_src * sine, imag_src * cosine - real_src * sine], axis=1
    ).astype(jnp.bfloat16)
    factor = 1.0 / math.sqrt(bins)
    result = jnp.einsum("jf,sfl->sjl", receivers, mixed, preferred_element_type=jnp.float32) * factor
    return result.reshape(STEPS, SRC, block, lag_share)


def solution(mesh):
    return jax.shard_map(
        local,
        mesh=mesh,
        in_specs=(P(("chan", "tm"), "parts"), P(), P("parts"), P("parts"), P("parts")),
        out_specs=P(None, None, ("parts", "chan"), "tm"),
        check_vma=False,
    )
```

```python
import functools
import math

import jax
import jax.numpy as jnp
from jax import lax
from jax.experimental import pallas as pl
from jax.experimental.pallas import tpu as pltpu
from jax.sharding import PartitionSpec as P

SRC = 16
STEPS = 2
LAGS = 512
TAPS = 32
STRIDE = 8
HALF_BAND = 32

two_pi = 2.0 * math.pi
epsilon = 1e-06


def split_bf16(x, parts):
    pieces = []
    rest = x
    for _ in range(parts):
        piece = rest.astype(jnp.bfloat16)
        pieces.append(piece)
        rest = rest - piece.astype(jnp.float32)
    return pieces


def decimation_matrix(fir_taps, out_rows, in_rows):
    rows = jnp.arange(out_rows, dtype=jnp.int32)[:, None, None]
    groups = jnp.arange(in_rows // STRIDE, dtype=jnp.int32)[None, :, None]
    lead = groups - rows
    matrix = jnp.zeros((out_rows, in_rows // STRIDE, STRIDE), jnp.float32)
    for lead_index in range(TAPS // STRIDE):
        taps = fir_taps[lead_index * STRIDE : (lead_index + 1) * STRIDE][None, None, :]
        matrix = matrix + jnp.where(lead == lead_index, taps, 0.0)
    return matrix.reshape(out_rows, in_rows)


def dft_table(samples, bins):
    inner = 32
    outer = samples // inner
    frequency = jnp.arange(bins, dtype=jnp.int32)[None, :]
    low = jnp.arange(inner, dtype=jnp.int32)[:, None]
    high = jnp.arange(outer, dtype=jnp.int32)[:, None] * inner
    scale = two_pi / samples
    low_angle = ((low * frequency) % samples).astype(jnp.float32) * scale
    high_angle = ((high * frequency) % samples).astype(jnp.float32) * scale
    cl, sl = jnp.cos(low_angle)[None], jnp.sin(low_angle)[None]
    ch, sh = jnp.cos(high_angle)[:, None], jnp.sin(high_angle)[:, None]
    cosine = (ch * cl - sh * sl).reshape(samples, bins)
    sine = (sh * cl + ch * sl).reshape(samples, bins)
    return jnp.concatenate([cosine, -sine], axis=1)


def band_matrix(bins):
    g = jnp.arange(bins, dtype=jnp.int32)
    near = jnp.abs(g[:, None] - g[None, :]) <= HALF_BAND
    return near.astype(jnp.bfloat16)


def lag_kernel(samples, first_lag, lag_count):
    bin_count = samples // 2
    frequency = jnp.arange(bin_count, dtype=jnp.int32)
    shifts = first_lag + jnp.arange(lag_count, dtype=jnp.int32) - LAGS // 2
    phases = jnp.mod(frequency[:, None] * shifts[None, :], samples)
    angles = phases.astype(jnp.float32) * (two_pi / samples)
    return jnp.concatenate([jnp.cos(angles), -jnp.sin(angles)], axis=0).astype(jnp.bfloat16)


def whiten_series(series):
    samples = series.shape[0]
    bins = samples // 2
    table = dft_table(samples, bins)
    hi, lo = split_bf16(table, 2)
    dims = (((0,), (0,)), ((), ()))
    both = lax.dot_general(
        series, jnp.concatenate([hi, lo], axis=1), dims, preferred_element_type=jnp.float32
    )
    spectrum = both[:, : 2 * bins] + both[:, 2 * bins :]
    real_part = spectrum[:, :bins]
    imag_part = spectrum[:, bins:]
    powers = real_part * real_part + imag_part * imag_part
    pieces = split_bf16(powers, 3)
    band = band_matrix(bins)
    window = jnp.dot(
        jnp.concatenate(pieces, axis=1),
        jnp.concatenate([band] * 3, axis=0),
        preferred_element_type=jnp.float32,
    )
    window_span = 2 * HALF_BAND + 1
    factor = 1.0 / jnp.sqrt(window / window_span + epsilon)
    return jnp.concatenate([real_part * factor, imag_part * factor], axis=1).astype(jnp.bfloat16)


def correlate_kernel(factor, bins, white_ref, src_ref, cos_ref, sin_ref, out_ref):
    step = pl.program_id(0)
    row = src_ref[pl.ds(step, 1), :]
    real_src = row[:, :bins]
    imag_src = row[:, bins:]
    cosine = cos_ref[...]
    sine = sin_ref[...]
    top = (cosine * real_src + sine * imag_src).astype(jnp.bfloat16)
    bottom = (cosine * imag_src - sine * real_src).astype(jnp.bfloat16)
    nt = (((1,), (1,)), ((), ()))
    total = lax.dot_general(white_ref[:, :bins], top, nt, preferred_element_type=jnp.float32)
    total = total + lax.dot_general(
        white_ref[:, bins:], bottom, nt, preferred_element_type=jnp.float32
    )
    out_ref[0] = total * factor


def correlate(receivers, sources, cosine_t, sine_t):
    block, width = receivers.shape
    bins = width // 2
    count = sources.shape[0]
    lags = cosine_t.shape[0]
    factor = 1.0 / math.sqrt(bins)
    flops = 2 * count * block * width * lags + 6 * count * bins * lags
    moved = 2 * block * width + 4 * count * width + 8 * lags * bins + 4 * count * block * lags
    return pl.pallas_call(
        functools.partial(correlate_kernel, factor, bins),
        out_shape=jax.ShapeDtypeStruct((count, block, lags), jnp.float32),
        grid=(count,),
        in_specs=[
            pl.BlockSpec((block, width), lambda s: (0, 0)),
            pl.BlockSpec((count, width), lambda s: (0, 0)),
            pl.BlockSpec((lags, bins), lambda s: (0, 0)),
            pl.BlockSpec((lags, bins), lambda s: (0, 0)),
        ],
        out_specs=pl.BlockSpec((1, block, lags), lambda s: (s, 0, 0)),
        compiler_params=pltpu.CompilerParams(dimension_semantics=("arbitrary",)),
        cost_estimate=pl.CostEstimate(flops=flops, bytes_accessed=moved, transcendentals=0),
    )(receivers, sources, cosine_t, sine_t)


def local(records, fir_taps, channel_map, source_owner, source_offset):
    n_chan = lax.axis_size("chan")
    n_tm = lax.axis_size("tm")
    n_dev = n_chan * n_tm
    raw_rows, channels = records.shape
    block = channels // n_chan
    out_rows = raw_rows // STRIDE
    halo_rows = TAPS - STRIDE
    samples = out_rows * n_dev

    shift = [(b, b - 1) for b in range(1, n_dev)]
    halo = lax.ppermute(records[:halo_rows], ("chan", "tm"), perm=shift)

    taps_matrix = decimation_matrix(fir_taps, out_rows, raw_rows + halo_rows)
    parts = split_bf16(taps_matrix, 3)
    stacked = jnp.concatenate(parts, axis=0)
    main = jnp.dot(stacked[:, :raw_rows], records, preferred_element_type=jnp.float32)
    tail = jnp.dot(stacked[:, raw_rows:], halo, preferred_element_type=jnp.float32)
    summed = main + tail
    decimated = (
        summed[:out_rows] + summed[out_rows : 2 * out_rows] + summed[2 * out_rows :]
    ).astype(jnp.bfloat16)

    first_rows = source_owner * block + source_offset
    picked = (first_rows[:, None] + jnp.arange(SRC, dtype=jnp.int32)[None, :]).reshape(-1)
    source_raw = jnp.take(channel_map, picked, mode="clip")
    block_raw = channel_map.reshape(n_chan, 1, block)
    block_raw = jnp.broadcast_to(block_raw, (n_chan, n_tm, block)).reshape(n_dev, block)
    index = jnp.concatenate(
        [block_raw, jnp.broadcast_to(source_raw[None], (n_dev, source_raw.shape[0]))], axis=1
    )
    width = index.shape[1]
    columns = jnp.take(decimated, index.reshape(-1), axis=1, mode="clip")
    series = lax.all_to_all(columns, ("chan", "tm"), 1, 0, tiled=True)

    white = whiten_series(series)
    receivers = white[:block]
    sources = white[block:].astype(jnp.float32)
    bins = samples // 2
    lag_share = LAGS // n_tm
    kernel = lag_kernel(samples, lax.axis_index("tm") * lag_share, lag_share).astype(jnp.float32)
    cosine_t = kernel[:bins].T
    sine_t = kernel[bins:].T
    result = correlate(receivers, sources, cosine_t, sine_t)
    return result.reshape(STEPS, SRC, block, lag_share)


def solution(mesh):
    return jax.shard_map(
        local,
        mesh=mesh,
        in_specs=(P(("chan", "tm"), "parts"), P(), P("parts"), P("parts"), P("parts")),
        out_specs=P(None, None, ("parts", "chan"), "tm"),
        check_vma=False,
    )
```

```python
import functools
import math

import jax
import jax.numpy as jnp
from jax import lax
from jax.experimental import pallas as pl
from jax.experimental.pallas import tpu as pltpu
from jax.sharding import PartitionSpec as P

SRC = 16
STEPS = 2
LAGS = 512
TAPS = 32
STRIDE = 8
HALF_BAND = 32

two_pi = 2.0 * math.pi
epsilon = 1e-06


def split_bf16(x, parts):
    pieces = []
    rest = x
    for _ in range(parts):
        piece = rest.astype(jnp.bfloat16)
        pieces.append(piece)
        rest = rest - piece.astype(jnp.float32)
    return pieces


def decimation_matrix(fir_taps, out_rows, in_rows):
    rows = jnp.arange(out_rows, dtype=jnp.int32)[:, None, None]
    groups = jnp.arange(in_rows // STRIDE, dtype=jnp.int32)[None, :, None]
    lead = groups - rows
    matrix = jnp.zeros((out_rows, in_rows // STRIDE, STRIDE), jnp.float32)
    for lead_index in range(TAPS // STRIDE):
        taps = fir_taps[lead_index * STRIDE : (lead_index + 1) * STRIDE][None, None, :]
        matrix = matrix + jnp.where(lead == lead_index, taps, 0.0)
    return matrix.reshape(out_rows, in_rows)


def dft_table(samples, bins):
    inner = 32
    outer = samples // inner
    frequency = jnp.arange(bins, dtype=jnp.int32)[None, :]
    low = jnp.arange(inner, dtype=jnp.int32)[:, None]
    high = jnp.arange(outer, dtype=jnp.int32)[:, None] * inner
    scale = two_pi / samples
    low_angle = ((low * frequency) % samples).astype(jnp.float32) * scale
    high_angle = ((high * frequency) % samples).astype(jnp.float32) * scale
    cl, sl = jnp.cos(low_angle)[None], jnp.sin(low_angle)[None]
    ch, sh = jnp.cos(high_angle)[:, None], jnp.sin(high_angle)[:, None]
    cosine = (ch * cl - sh * sl).reshape(samples, bins)
    sine = (sh * cl + ch * sl).reshape(samples, bins)
    return jnp.concatenate([cosine, -sine], axis=1)


def band_matrix(bins):
    g = jnp.arange(bins, dtype=jnp.int32)
    near = jnp.abs(g[:, None] - g[None, :]) <= HALF_BAND
    return near.astype(jnp.bfloat16)


def lag_kernel(samples, first_lag, lag_count):
    bin_count = samples // 2
    frequency = jnp.arange(bin_count, dtype=jnp.int32)
    shifts = first_lag + jnp.arange(lag_count, dtype=jnp.int32) - LAGS // 2
    phases = jnp.mod(frequency[:, None] * shifts[None, :], samples)
    angles = phases.astype(jnp.float32) * (two_pi / samples)
    return jnp.concatenate([jnp.cos(angles), -jnp.sin(angles)], axis=0).astype(jnp.bfloat16)


def whiten_series(series):
    samples = series.shape[1]
    bins = samples // 2
    table = dft_table(samples, bins)
    hi, lo = split_bf16(table, 2)
    both = jnp.dot(series, jnp.concatenate([hi, lo], axis=1), preferred_element_type=jnp.float32)
    spectrum = both[:, : 2 * bins] + both[:, 2 * bins :]
    real_part = spectrum[:, :bins]
    imag_part = spectrum[:, bins:]
    powers = real_part * real_part + imag_part * imag_part
    pieces = split_bf16(powers, 3)
    band = band_matrix(bins)
    window = jnp.dot(
        jnp.concatenate(pieces, axis=1),
        jnp.concatenate([band] * 3, axis=0),
        preferred_element_type=jnp.float32,
    )
    window_span = 2 * HALF_BAND + 1
    factor = 1.0 / jnp.sqrt(window / window_span + epsilon)
    return jnp.concatenate([real_part * factor, imag_part * factor], axis=1).astype(jnp.bfloat16)


def correlate_kernel(factor, bins, group, white_ref, src_ref, cos_ref, sin_ref, out_ref):
    cosine = cos_ref[...]
    sine = sin_ref[...]
    for k in range(group):
        real_src = src_ref[0, :bins, k : k + 1]
        imag_src = src_ref[0, bins:, k : k + 1]
        top = (cosine * real_src + sine * imag_src).astype(jnp.bfloat16)
        bottom = (cosine * imag_src - sine * real_src).astype(jnp.bfloat16)
        total = jnp.dot(white_ref[:, :bins], top, preferred_element_type=jnp.float32)
        total = total + jnp.dot(white_ref[:, bins:], bottom, preferred_element_type=jnp.float32)
        out_ref[k] = total * factor


def correlate(receivers, sources, cosine, sine):
    block, width = receivers.shape
    bins = width // 2
    count = sources.shape[0]
    lags = cosine.shape[1]
    group = 8
    grouped = sources.reshape(count // group, group, width).transpose(0, 2, 1)
    factor = 1.0 / math.sqrt(bins)
    flops = 2 * count * block * width * lags + 6 * count * bins * lags
    moved = 2 * block * width + 4 * count * width + 8 * lags * bins + 4 * count * block * lags
    return pl.pallas_call(
        functools.partial(correlate_kernel, factor, bins, group),
        out_shape=jax.ShapeDtypeStruct((count, block, lags), jnp.float32),
        grid=(count // group,),
        in_specs=[
            pl.BlockSpec((block, width), lambda s: (0, 0)),
            pl.BlockSpec((1, width, group), lambda s: (s, 0, 0)),
            pl.BlockSpec((bins, lags), lambda s: (0, 0)),
            pl.BlockSpec((bins, lags), lambda s: (0, 0)),
        ],
        out_specs=pl.BlockSpec((group, block, lags), lambda s: (s, 0, 0)),
        compiler_params=pltpu.CompilerParams(dimension_semantics=("arbitrary",)),
        cost_estimate=pl.CostEstimate(flops=flops, bytes_accessed=moved, transcendentals=0),
    )(receivers, grouped, cosine, sine)


def swap_tm(x):
    other = lax.ppermute(x, "tm", perm=[(0, 1), (1, 0)])
    first = lax.axis_index("tm") == 0
    return jnp.where(first, x, other), jnp.where(first, other, x)


def local(records, fir_taps, channel_map, source_owner, source_offset):
    n_chan = lax.axis_size("chan")
    n_tm = lax.axis_size("tm")
    assert n_tm == 2
    n_dev = n_chan * n_tm
    raw_rows, channels = records.shape
    block = channels // n_chan
    half = block // n_tm
    out_rows = raw_rows // STRIDE
    halo_rows = TAPS - STRIDE
    samples = out_rows * n_dev
    bins = samples // 2
    tm = lax.axis_index("tm")

    shift = [(b, b - 1) for b in range(1, n_dev)]
    halo = lax.ppermute(records[:halo_rows], ("chan", "tm"), perm=shift)

    taps_matrix = decimation_matrix(fir_taps, out_rows, raw_rows + halo_rows)
    parts = split_bf16(taps_matrix, 3)
    stacked = jnp.concatenate(parts, axis=0)
    dims = (((0,), (1,)), ((), ()))
    main = lax.dot_general(records, stacked[:, :raw_rows], dims, preferred_element_type=jnp.float32)
    tail = lax.dot_general(halo, stacked[:, raw_rows:], dims, preferred_element_type=jnp.float32)
    summed = main + tail
    decimated = (
        summed[:, :out_rows] + summed[:, out_rows : 2 * out_rows] + summed[:, 2 * out_rows :]
    ).astype(jnp.bfloat16)

    first, second = swap_tm(decimated)
    paired = jnp.concatenate([first, second], axis=1)

    first_rows = source_owner * block + source_offset
    own_first = lax.dynamic_index_in_dim(first_rows, tm, keepdims=False)
    source_raw = jnp.take(channel_map, own_first + jnp.arange(SRC, dtype=jnp.int32), mode="clip")
    halves = channel_map.reshape(n_chan, n_tm, half)
    half_raw = lax.dynamic_index_in_dim(halves, tm, axis=1, keepdims=False)
    index = jnp.concatenate(
        [half_raw, jnp.broadcast_to(source_raw[None], (n_chan, SRC))], axis=1
    )
    width = index.shape[1]
    rows = jnp.take(paired, index.reshape(-1), axis=0, mode="clip").reshape(n_chan, width, -1)
    series = lax.all_to_all(rows, "chan", 0, 2, tiled=True).reshape(width, samples)

    white = whiten_series(series)
    low, high = swap_tm(white)
    receivers = jnp.concatenate([low[:half], high[:half]], axis=0)
    sources = jnp.concatenate([low[half:], high[half:]], axis=0).astype(jnp.float32)

    lag_share = LAGS // n_tm
    kernel = lag_kernel(samples, tm * lag_share, lag_share).astype(jnp.float32)
    result = correlate(receivers, sources, kernel[:bins], kernel[bins:])
    return result.reshape(STEPS, SRC, block, lag_share)


def solution(mesh):
    return jax.shard_map(
        local,
        mesh=mesh,
        in_specs=(P(("chan", "tm"), "parts"), P(), P("parts"), P("parts"), P("parts")),
        out_specs=P(None, None, ("parts", "chan"), "tm"),
        check_vma=False,
    )
```

```python
import functools
import math

import jax
import jax.numpy as jnp
from jax import lax
from jax.experimental import pallas as pl
from jax.experimental.pallas import tpu as pltpu
from jax.sharding import PartitionSpec as P

SRC = 16
STEPS = 2
LAGS = 512
TAPS = 32
STRIDE = 8
HALF_BAND = 32

two_pi = 2.0 * math.pi
epsilon = 1e-06


def split_bf16(x, parts):
    pieces = []
    rest = x
    for _ in range(parts):
        piece = rest.astype(jnp.bfloat16)
        pieces.append(piece)
        rest = rest - piece.astype(jnp.float32)
    return pieces


def decimation_matrix(fir_taps, out_rows, in_rows):
    rows = jnp.arange(out_rows, dtype=jnp.int32)[:, None, None]
    groups = jnp.arange(in_rows // STRIDE, dtype=jnp.int32)[None, :, None]
    lead = groups - rows
    matrix = jnp.zeros((out_rows, in_rows // STRIDE, STRIDE), jnp.float32)
    for lead_index in range(TAPS // STRIDE):
        taps = fir_taps[lead_index * STRIDE : (lead_index + 1) * STRIDE][None, None, :]
        matrix = matrix + jnp.where(lead == lead_index, taps, 0.0)
    return matrix.reshape(out_rows, in_rows)


def dft_table(samples, bins, time_index):
    inner = 32
    outer = samples // inner
    frequency = jnp.arange(bins, dtype=jnp.int32)[None, :]
    low = jnp.arange(inner, dtype=jnp.int32)[:, None]
    high = time_index.reshape(outer, inner)[:, :1]
    scale = two_pi / samples
    low_angle = ((low * frequency) % samples).astype(jnp.float32) * scale
    high_angle = ((high * frequency) % samples).astype(jnp.float32) * scale
    cl, sl = jnp.cos(low_angle)[None], jnp.sin(low_angle)[None]
    ch, sh = jnp.cos(high_angle)[:, None], jnp.sin(high_angle)[:, None]
    cosine = (ch * cl - sh * sl).reshape(samples, bins)
    sine = (sh * cl + ch * sl).reshape(samples, bins)
    return jnp.concatenate([cosine, -sine], axis=1)


def band_matrix(bins):
    g = jnp.arange(bins, dtype=jnp.int32)
    near = jnp.abs(g[:, None] - g[None, :]) <= HALF_BAND
    return near.astype(jnp.bfloat16)


def lag_kernel(samples, first_lag, lag_count):
    bin_count = samples // 2
    frequency = jnp.arange(bin_count, dtype=jnp.int32)
    shifts = first_lag + jnp.arange(lag_count, dtype=jnp.int32) - LAGS // 2
    phases = jnp.mod(frequency[:, None] * shifts[None, :], samples)
    angles = phases.astype(jnp.float32) * (two_pi / samples)
    return jnp.concatenate([jnp.cos(angles), -jnp.sin(angles)], axis=0).astype(jnp.bfloat16)


def whiten_series(series, time_index):
    samples = series.shape[1]
    bins = samples // 2
    table = dft_table(samples, bins, time_index)
    hi, lo = split_bf16(table, 2)
    both = jnp.dot(series, jnp.concatenate([hi, lo], axis=1), preferred_element_type=jnp.float32)
    spectrum = both[:, : 2 * bins] + both[:, 2 * bins :]
    real_part = spectrum[:, :bins]
    imag_part = spectrum[:, bins:]
    powers = real_part * real_part + imag_part * imag_part
    pieces = split_bf16(powers, 3)
    band = band_matrix(bins)
    window = jnp.dot(
        jnp.concatenate(pieces, axis=1),
        jnp.concatenate([band] * 3, axis=0),
        preferred_element_type=jnp.float32,
    )
    window_span = 2 * HALF_BAND + 1
    factor = 1.0 / jnp.sqrt(window / window_span + epsilon)
    return jnp.concatenate([real_part * factor, imag_part * factor], axis=1).astype(jnp.bfloat16)


def correlate_kernel(factor, bins, group, white_ref, src_ref, cos_ref, sin_ref, out_ref):
    cosine = cos_ref[...]
    sine = sin_ref[...]
    count = src_ref.shape[1]
    lags = cosine.shape[1]
    lanes = 128
    which = lax.broadcasted_iota(jnp.int32, (count, lanes), 0)
    for k in range(group):
        pick = (which == pl.program_id(0) * group + k).astype(jnp.bfloat16)
        real_src = jnp.dot(src_ref[:bins, :], pick, preferred_element_type=jnp.float32)
        imag_src = jnp.dot(src_ref[bins:, :], pick, preferred_element_type=jnp.float32)
        real_src = jnp.concatenate([real_src] * (lags // lanes), axis=1)
        imag_src = jnp.concatenate([imag_src] * (lags // lanes), axis=1)
        top = (cosine * real_src + sine * imag_src).astype(jnp.bfloat16)
        bottom = (cosine * imag_src - sine * real_src).astype(jnp.bfloat16)
        total = jnp.dot(white_ref[:, :bins], top, preferred_element_type=jnp.float32)
        total = total + jnp.dot(white_ref[:, bins:], bottom, preferred_element_type=jnp.float32)
        out_ref[k] = total * factor


def correlate(receivers, sources, cosine, sine):
    block, width = receivers.shape
    bins = width // 2
    count = sources.shape[0]
    lags = cosine.shape[1]
    group = 8
    columns = sources.T
    factor = 1.0 / math.sqrt(bins)
    flops = 2 * count * block * width * lags + 6 * count * bins * lags
    moved = 2 * block * width + 2 * count * width + 8 * lags * bins + 4 * count * block * lags
    return pl.pallas_call(
        functools.partial(correlate_kernel, factor, bins, group),
        out_shape=jax.ShapeDtypeStruct((count, block, lags), jnp.float32),
        grid=(count // group,),
        in_specs=[
            pl.BlockSpec((block, width), lambda s: (0, 0)),
            pl.BlockSpec((width, count), lambda s: (0, 0)),
            pl.BlockSpec((bins, lags), lambda s: (0, 0)),
            pl.BlockSpec((bins, lags), lambda s: (0, 0)),
        ],
        out_specs=pl.BlockSpec((group, block, lags), lambda s: (s, 0, 0)),
        compiler_params=pltpu.CompilerParams(dimension_semantics=("arbitrary",)),
        cost_estimate=pl.CostEstimate(flops=flops, bytes_accessed=moved, transcendentals=0),
    )(receivers, columns, cosine, sine)


def swap_tm(x):
    other = lax.ppermute(x, "tm", perm=[(0, 1), (1, 0)])
    first = lax.axis_index("tm") == 0
    return jnp.where(first, x, other), jnp.where(first, other, x)


def local(records, fir_taps, channel_map, source_owner, source_offset):
    n_chan = lax.axis_size("chan")
    n_tm = lax.axis_size("tm")
    assert n_tm == 2
    n_dev = n_chan * n_tm
    raw_rows, channels = records.shape
    block = channels // n_chan
    half = block // n_tm
    out_rows = raw_rows // STRIDE
    halo_rows = TAPS - STRIDE
    samples = out_rows * n_dev
    bins = samples // 2
    tm = lax.axis_index("tm")

    shift = [(b, b - 1) for b in range(1, n_dev)]
    halo = lax.ppermute(records[:halo_rows], ("chan", "tm"), perm=shift)

    taps_matrix = decimation_matrix(fir_taps, out_rows, raw_rows + halo_rows)
    parts = split_bf16(taps_matrix, 3)
    stacked = jnp.concatenate(parts, axis=0)
    dims = (((0,), (1,)), ((), ()))
    main = lax.dot_general(records, stacked[:, :raw_rows], dims, preferred_element_type=jnp.float32)
    tail = lax.dot_general(halo, stacked[:, raw_rows:], dims, preferred_element_type=jnp.float32)
    summed = main + tail
    decimated = (
        summed[:, :out_rows] + summed[:, out_rows : 2 * out_rows] + summed[:, 2 * out_rows :]
    ).astype(jnp.bfloat16)

    first, second = swap_tm(decimated)
    paired = jnp.concatenate([first, second], axis=1)

    first_rows = source_owner * block + source_offset
    own_first = lax.dynamic_index_in_dim(first_rows, tm, keepdims=False)
    source_raw = lax.dynamic_slice_in_dim(channel_map, own_first, SRC)
    halves = channel_map.reshape(n_chan, n_tm, half)
    half_raw = lax.dynamic_index_in_dim(halves, tm, axis=1, keepdims=False)
    index = jnp.concatenate(
        [half_raw, jnp.broadcast_to(source_raw[None], (n_chan, SRC))], axis=1
    )
    width = index.shape[1]
    rows = jnp.take(paired, index.reshape(-1), axis=0, mode="clip").reshape(n_chan, width, -1)
    chip = lax.axis_index("chan")
    arrived = [lax.dynamic_index_in_dim(rows, chip, keepdims=False)]
    for k in range(1, n_chan):
        outgoing = lax.dynamic_index_in_dim(rows, (chip + k) % n_chan, keepdims=False)
        perm = [(c, (c + k) % n_chan) for c in range(n_chan)]
        arrived.append(lax.ppermute(outgoing, "chan", perm=perm))
    series = jnp.concatenate(arrived, axis=1)
    chunk = 2 * out_rows
    origin = (chip - jnp.arange(n_chan, dtype=jnp.int32)) % n_chan
    time_index = (origin[:, None] * chunk + jnp.arange(chunk, dtype=jnp.int32)[None, :]).reshape(-1)

    white = whiten_series(series, time_index)
    low, high = swap_tm(white)
    receivers = jnp.concatenate([low[:half], high[:half]], axis=0)
    sources = jnp.concatenate([low[half:], high[half:]], axis=0)

    lag_share = LAGS // n_tm
    kernel = lag_kernel(samples, tm * lag_share, lag_share).astype(jnp.float32)
    result = correlate(receivers, sources, kernel[:bins], kernel[bins:])
    return result.reshape(STEPS, SRC, block, lag_share)


def solution(mesh):
    return jax.shard_map(
        local,
        mesh=mesh,
        in_specs=(P(("chan", "tm"), "parts"), P(), P("parts"), P("parts"), P("parts")),
        out_specs=P(None, None, ("parts", "chan"), "tm"),
        check_vma=False,
    )
```

```python
import functools
import math

import jax
import jax.numpy as jnp
from jax import lax
from jax.experimental import pallas as pl
from jax.experimental.pallas import tpu as pltpu
from jax.sharding import PartitionSpec as P

SRC = 16
STEPS = 2
LAGS = 512
TAPS = 32
STRIDE = 8
HALF_BAND = 32

two_pi = 2.0 * math.pi
epsilon = 1e-06


def split_bf16(x, parts):
    pieces = []
    rest = x
    for _ in range(parts):
        piece = rest.astype(jnp.bfloat16)
        pieces.append(piece)
        rest = rest - piece.astype(jnp.float32)
    return pieces


def decimation_matrix(fir_taps, out_rows, in_rows):
    rows = jnp.arange(out_rows, dtype=jnp.int32)[:, None, None]
    groups = jnp.arange(in_rows // STRIDE, dtype=jnp.int32)[None, :, None]
    lead = groups - rows
    matrix = jnp.zeros((out_rows, in_rows // STRIDE, STRIDE), jnp.float32)
    for lead_index in range(TAPS // STRIDE):
        taps = fir_taps[lead_index * STRIDE : (lead_index + 1) * STRIDE][None, None, :]
        matrix = matrix + jnp.where(lead == lead_index, taps, 0.0)
    return matrix.reshape(out_rows, in_rows)


def dft_table(samples, bins, time_index):
    inner = 32
    outer = samples // inner
    frequency = jnp.arange(bins, dtype=jnp.int32)[None, :]
    low = jnp.arange(inner, dtype=jnp.int32)[:, None]
    high = time_index.reshape(outer, inner)[:, :1]
    scale = two_pi / samples
    low_angle = ((low * frequency) % samples).astype(jnp.float32) * scale
    high_angle = ((high * frequency) % samples).astype(jnp.float32) * scale
    cl, sl = jnp.cos(low_angle)[None], jnp.sin(low_angle)[None]
    ch, sh = jnp.cos(high_angle)[:, None], jnp.sin(high_angle)[:, None]
    cosine = (ch * cl - sh * sl).reshape(samples, bins)
    sine = (sh * cl + ch * sl).reshape(samples, bins)
    return jnp.concatenate([cosine, -sine], axis=1)


def band_matrix(bins):
    g = jnp.arange(bins, dtype=jnp.int32)
    near = jnp.abs(g[:, None] - g[None, :]) <= HALF_BAND
    return near.astype(jnp.bfloat16)


def lag_kernel(samples, first_lag, lag_count):
    bin_count = samples // 2
    frequency = jnp.arange(bin_count, dtype=jnp.int32)
    shifts = first_lag + jnp.arange(lag_count, dtype=jnp.int32) - LAGS // 2
    phases = jnp.mod(frequency[:, None] * shifts[None, :], samples)
    angles = phases.astype(jnp.float32) * (two_pi / samples)
    return jnp.concatenate([jnp.cos(angles), -jnp.sin(angles)], axis=0).astype(jnp.bfloat16)


def whiten_series(series, time_index):
    samples = series.shape[1]
    bins = samples // 2
    table = dft_table(samples, bins, time_index)
    hi, lo = split_bf16(table, 2)
    both = jnp.dot(series, jnp.concatenate([hi, lo], axis=1), preferred_element_type=jnp.float32)
    spectrum = both[:, : 2 * bins] + both[:, 2 * bins :]
    real_part = spectrum[:, :bins]
    imag_part = spectrum[:, bins:]
    powers = real_part * real_part + imag_part * imag_part
    pieces = split_bf16(powers, 3)
    band = band_matrix(bins)
    window = jnp.dot(
        jnp.concatenate(pieces, axis=1),
        jnp.concatenate([band] * 3, axis=0),
        preferred_element_type=jnp.float32,
    )
    window_span = 2 * HALF_BAND + 1
    factor = 1.0 / jnp.sqrt(window / window_span + epsilon)
    return jnp.concatenate([real_part * factor, imag_part * factor], axis=1).astype(jnp.bfloat16)


def correlate_kernel(factor, bins, group, white_ref, src_ref, lag_ref, out_ref):
    real_rcv = white_ref[:, :bins]
    imag_rcv = white_ref[:, bins:]
    lag = lag_ref[...]
    for k in range(group):
        row = src_ref[pl.ds(pl.program_id(0) * group + k, 1), :]
        real_src = row[:, :bins]
        imag_src = row[:, bins:]
        cross = jnp.concatenate(
            [real_src * real_rcv + imag_src * imag_rcv, imag_src * real_rcv - real_src * imag_rcv],
            axis=1,
        ).astype(jnp.bfloat16)
        out_ref[k] = jnp.dot(cross, lag, preferred_element_type=jnp.float32) * factor


def correlate(receivers, sources, lag):
    block, width = receivers.shape
    bins = width // 2
    count = sources.shape[0]
    lags = lag.shape[1]
    group = 8
    factor = 1.0 / math.sqrt(bins)
    flops = 2 * count * block * width * lags + 6 * count * block * bins
    moved = 4 * block * width + 4 * count * width + 2 * lags * width + 4 * count * block * lags
    return pl.pallas_call(
        functools.partial(correlate_kernel, factor, bins, group),
        out_shape=jax.ShapeDtypeStruct((count, block, lags), jnp.float32),
        grid=(count // group,),
        in_specs=[
            pl.BlockSpec((block, width), lambda s: (0, 0)),
            pl.BlockSpec((count, width), lambda s: (0, 0)),
            pl.BlockSpec((width, lags), lambda s: (0, 0)),
        ],
        out_specs=pl.BlockSpec((group, block, lags), lambda s: (s, 0, 0)),
        compiler_params=pltpu.CompilerParams(dimension_semantics=("arbitrary",)),
        cost_estimate=pl.CostEstimate(flops=flops, bytes_accessed=moved, transcendentals=0),
    )(receivers, sources, lag)


def swap_tm(x):
    other = lax.ppermute(x, "tm", perm=[(0, 1), (1, 0)])
    first = lax.axis_index("tm") == 0
    return jnp.where(first, x, other), jnp.where(first, other, x)


def local(records, fir_taps, channel_map, source_owner, source_offset):
    n_chan = lax.axis_size("chan")
    n_tm = lax.axis_size("tm")
    assert n_tm == 2
    n_dev = n_chan * n_tm
    raw_rows, channels = records.shape
    block = channels // n_chan
    half = block // n_tm
    out_rows = raw_rows // STRIDE
    halo_rows = TAPS - STRIDE
    samples = out_rows * n_dev
    bins = samples // 2
    tm = lax.axis_index("tm")

    shift = [(b, b - 1) for b in range(1, n_dev)]
    halo = lax.ppermute(records[:halo_rows], ("chan", "tm"), perm=shift)

    taps_matrix = decimation_matrix(fir_taps, out_rows, raw_rows + halo_rows)
    parts = split_bf16(taps_matrix, 3)
    stacked = jnp.concatenate(parts, axis=0)
    dims = (((0,), (1,)), ((), ()))
    main = lax.dot_general(records, stacked[:, :raw_rows], dims, preferred_element_type=jnp.float32)
    tail = lax.dot_general(halo, stacked[:, raw_rows:], dims, preferred_element_type=jnp.float32)
    summed = main + tail
    decimated = (
        summed[:, :out_rows] + summed[:, out_rows : 2 * out_rows] + summed[:, 2 * out_rows :]
    ).astype(jnp.bfloat16)

    first, second = swap_tm(decimated)
    paired = jnp.concatenate([first, second], axis=1)

    first_rows = source_owner * block + source_offset
    own_first = lax.dynamic_index_in_dim(first_rows, tm, keepdims=False)
    source_raw = lax.dynamic_slice_in_dim(channel_map, own_first, SRC)
    halves = channel_map.reshape(n_chan, n_tm, half)
    half_raw = lax.dynamic_index_in_dim(halves, tm, axis=1, keepdims=False)
    index = jnp.concatenate(
        [half_raw, jnp.broadcast_to(source_raw[None], (n_chan, SRC))], axis=1
    )
    width = index.shape[1]
    rows = jnp.take(paired, index.reshape(-1), axis=0, mode="clip").reshape(n_chan, width, -1)
    series = lax.all_to_all(rows, "chan", 0, 2, tiled=True).reshape(width, samples)
    time_index = jnp.arange(samples, dtype=jnp.int32)

    white = whiten_series(series, time_index)
    low, high = swap_tm(white)
    receivers = jnp.concatenate([low[:half], high[:half]], axis=0).astype(jnp.float32)
    sources = jnp.concatenate([low[half:], high[half:]], axis=0).astype(jnp.float32)

    lag_share = LAGS // n_tm
    kernel = lag_kernel(samples, tm * lag_share, lag_share)
    result = correlate(receivers, sources, kernel)
    return result.reshape(STEPS, SRC, block, lag_share)


def solution(mesh):
    return jax.shard_map(
        local,
        mesh=mesh,
        in_specs=(P(("chan", "tm"), "parts"), P(), P("parts"), P("parts"), P("parts")),
        out_specs=P(None, None, ("parts", "chan"), "tm"),
        check_vma=False,
    )
```

```python
import functools
import math

import jax
import jax.numpy as jnp
from jax import lax
from jax.experimental import pallas as pl
from jax.experimental.pallas import tpu as pltpu
from jax.sharding import PartitionSpec as P

SRC = 16
STEPS = 2
LAGS = 512
TAPS = 32
STRIDE = 8
HALF_BAND = 32

two_pi = 2.0 * math.pi
epsilon = 1e-06


def split_bf16(x, parts):
    pieces = []
    rest = x
    for _ in range(parts):
        piece = rest.astype(jnp.bfloat16)
        pieces.append(piece)
        rest = rest - piece.astype(jnp.float32)
    return pieces


def decimation_matrix(fir_taps, out_rows, in_rows):
    leads = TAPS // STRIDE
    rows = jnp.arange(out_rows, dtype=jnp.int32)[:, None, None, None]
    groups = jnp.arange(in_rows // STRIDE, dtype=jnp.int32)[None, :, None, None]
    lead = jnp.arange(leads, dtype=jnp.int32)[None, None, :, None]
    taps = fir_taps.reshape(1, 1, leads, STRIDE)
    matrix = jnp.where(groups - rows == lead, taps, 0.0).sum(axis=2)
    return matrix.reshape(out_rows, in_rows)


def dft_table(samples, bins, time_index):
    inner = 32
    outer = samples // inner
    frequency = jnp.arange(bins, dtype=jnp.int32)[None, :]
    low = jnp.arange(inner, dtype=jnp.int32)[:, None]
    high = time_index.reshape(outer, inner)[:, :1]
    scale = two_pi / samples
    low_angle = ((low * frequency) % samples).astype(jnp.float32) * scale
    high_angle = ((high * frequency) % samples).astype(jnp.float32) * scale
    cl, sl = jnp.cos(low_angle)[None], jnp.sin(low_angle)[None]
    ch, sh = jnp.cos(high_angle)[:, None], jnp.sin(high_angle)[:, None]
    cosine = (ch * cl - sh * sl).reshape(samples, bins)
    sine = (sh * cl + ch * sl).reshape(samples, bins)
    return jnp.concatenate([cosine, -sine], axis=1)


def band_matrix(bins):
    g = jnp.arange(bins, dtype=jnp.int32)
    near = jnp.abs(g[:, None] - g[None, :]) <= HALF_BAND
    return near.astype(jnp.bfloat16)


def lag_kernel(samples, first_lag, lag_count):
    bin_count = samples // 2
    frequency = jnp.arange(bin_count, dtype=jnp.int32)
    shifts = first_lag + jnp.arange(lag_count, dtype=jnp.int32) - LAGS // 2
    phases = jnp.mod(frequency[:, None] * shifts[None, :], samples)
    angles = phases.astype(jnp.float32) * (two_pi / samples)
    return jnp.concatenate([jnp.cos(angles), -jnp.sin(angles)], axis=0).astype(jnp.bfloat16)


def whiten_series(series, table):
    samples = series.shape[1]
    bins = samples // 2
    hi, lo = split_bf16(table, 2)
    both = jnp.dot(series, jnp.concatenate([hi, lo], axis=1), preferred_element_type=jnp.float32)
    spectrum = both[:, : 2 * bins] + both[:, 2 * bins :]
    real_part = spectrum[:, :bins]
    imag_part = spectrum[:, bins:]
    powers = real_part * real_part + imag_part * imag_part
    pieces = split_bf16(powers, 3)
    band = band_matrix(bins)
    window = jnp.dot(
        jnp.concatenate(pieces, axis=1),
        jnp.concatenate([band] * 3, axis=0),
        preferred_element_type=jnp.float32,
    )
    window_span = 2 * HALF_BAND + 1
    factor = 1.0 / jnp.sqrt(window / window_span + epsilon)
    return jnp.concatenate([real_part * factor, imag_part * factor], axis=1).astype(jnp.bfloat16)


def correlate_kernel(factor, bins, group, half, low_ref, high_ref, lag_ref, out_ref):
    step = pl.program_id(0)
    lag = lag_ref[...]
    receivers = [low_ref[:half, :].astype(jnp.float32), high_ref[:half, :].astype(jnp.float32)]
    every = jnp.concatenate([low_ref[half:, :], high_ref[half:, :]], axis=0).astype(jnp.float32)
    picked = every[:group]
    for g in range(1, every.shape[0] // group):
        picked = jnp.where(step == g, every[g * group : (g + 1) * group], picked)
    for k in range(group):
        row = picked[k : k + 1]
        real_src = row[:, :bins]
        imag_src = row[:, bins:]
        for part, rcv in enumerate(receivers):
            real_rcv = rcv[:, :bins]
            imag_rcv = rcv[:, bins:]
            cross = jnp.concatenate(
                [real_src * real_rcv + imag_src * imag_rcv, imag_src * real_rcv - real_src * imag_rcv],
                axis=1,
            ).astype(jnp.bfloat16)
            out_ref[k, part * half : (part + 1) * half, :] = (
                jnp.dot(cross, lag, preferred_element_type=jnp.float32) * factor
            )


def correlate(low, high, half, lag):
    rows, width = low.shape
    bins = width // 2
    count = 2 * (rows - half)
    block = 2 * half
    lags = lag.shape[1]
    group = 8
    factor = 1.0 / math.sqrt(bins)
    flops = 2 * count * block * width * lags + 6 * count * block * bins
    moved = 4 * rows * width + 2 * lags * width + 4 * count * block * lags
    return pl.pallas_call(
        functools.partial(correlate_kernel, factor, bins, group, half),
        out_shape=jax.ShapeDtypeStruct((count, block, lags), jnp.float32),
        grid=(count // group,),
        in_specs=[
            pl.BlockSpec((rows, width), lambda s: (0, 0)),
            pl.BlockSpec((rows, width), lambda s: (0, 0)),
            pl.BlockSpec((width, lags), lambda s: (0, 0)),
        ],
        out_specs=pl.BlockSpec((group, block, lags), lambda s: (s, 0, 0)),
        compiler_params=pltpu.CompilerParams(dimension_semantics=("arbitrary",)),
        cost_estimate=pl.CostEstimate(flops=flops, bytes_accessed=moved, transcendentals=0),
    )(low, high, lag)


def swap_tm(x):
    other = lax.ppermute(x, "tm", perm=[(0, 1), (1, 0)])
    first = lax.axis_index("tm") == 0
    return jnp.where(first, x, other), jnp.where(first, other, x)


def local(records, fir_taps, channel_map, source_owner, source_offset):
    n_chan = lax.axis_size("chan")
    n_tm = lax.axis_size("tm")
    assert n_tm == 2
    n_dev = n_chan * n_tm
    raw_rows, channels = records.shape
    block = channels // n_chan
    half = block // n_tm
    out_rows = raw_rows // STRIDE
    halo_rows = TAPS - STRIDE
    samples = out_rows * n_dev
    bins = samples // 2
    tm = lax.axis_index("tm")

    shift = [(b, b - 1) for b in range(1, n_dev)]
    halo = lax.ppermute(records[:halo_rows], ("chan", "tm"), perm=shift)

    taps_matrix = decimation_matrix(fir_taps, out_rows, raw_rows + halo_rows)
    stacked = jnp.concatenate(split_bf16(taps_matrix, 2), axis=0)
    main = jnp.dot(stacked[:, :raw_rows], records, preferred_element_type=jnp.float32)
    tail = jnp.dot(stacked[:, raw_rows:], halo, preferred_element_type=jnp.float32)
    summed = main + tail
    decimated = (summed[:out_rows] + summed[out_rows:]).astype(jnp.bfloat16).T

    first, second = swap_tm(decimated)
    paired = jnp.concatenate([first, second], axis=1)

    owner = lax.dynamic_index_in_dim(source_owner, tm, keepdims=False)
    offset = lax.dynamic_index_in_dim(source_offset, tm, keepdims=False)
    source_raw = lax.dynamic_slice_in_dim(channel_map, owner * block + offset, SRC)
    half_raw = lax.dynamic_slice(channel_map.reshape(n_chan, block), (0, tm * half), (n_chan, half))
    index = jnp.concatenate(
        [half_raw, jnp.broadcast_to(source_raw[None], (n_chan, SRC))], axis=1
    )
    width = index.shape[1]
    rows = jnp.take(paired, index.reshape(-1), axis=0, mode="clip").reshape(n_chan, width, -1)
    series = lax.all_to_all(rows, "chan", 0, 2, tiled=True).reshape(width, samples)
    table = dft_table(samples, bins, jnp.arange(samples, dtype=jnp.int32))
    lag_share = LAGS // n_tm
    first_lag = (tm * lag_share - LAGS // 2) % samples
    lag = lax.dynamic_slice_in_dim(table, first_lag, lag_share).T.astype(jnp.bfloat16)

    white = whiten_series(series, table)
    low, high = swap_tm(white)
    result = correlate(low, high, half, lag)
    return result.reshape(STEPS, SRC, block, lag_share)


def solution(mesh):
    return jax.shard_map(
        local,
        mesh=mesh,
        in_specs=(P(("chan", "tm"), "parts"), P(), P("parts"), P("parts"), P("parts")),
        out_specs=P(None, None, ("parts", "chan"), "tm"),
        check_vma=False,
    )
```

```python
import functools
import math

import jax
import jax.numpy as jnp
from jax import lax
from jax.experimental import pallas as pl
from jax.experimental.pallas import tpu as pltpu
from jax.sharding import PartitionSpec as P

SRC = 16
STEPS = 2
LAGS = 512
TAPS = 32
STRIDE = 8
HALF_BAND = 32

two_pi = 2.0 * math.pi
epsilon = 1e-06


def split_bf16(x, parts):
    pieces = []
    rest = x
    for _ in range(parts):
        piece = rest.astype(jnp.bfloat16)
        pieces.append(piece)
        rest = rest - piece.astype(jnp.float32)
    return pieces


def decimation_matrix(fir_taps, out_rows, in_rows):
    leads = TAPS // STRIDE
    rows = jnp.arange(out_rows, dtype=jnp.int32)[:, None, None, None]
    groups = jnp.arange(in_rows // STRIDE, dtype=jnp.int32)[None, :, None, None]
    lead = jnp.arange(leads, dtype=jnp.int32)[None, None, :, None]
    taps = fir_taps.reshape(1, 1, leads, STRIDE)
    matrix = jnp.where(groups - rows == lead, taps, 0.0).sum(axis=2)
    return matrix.reshape(out_rows, in_rows)


def dft_table(samples, bins, time_index):
    inner = 32
    outer = samples // inner
    frequency = jnp.arange(bins, dtype=jnp.int32)[None, :]
    low = jnp.arange(inner, dtype=jnp.int32)[:, None]
    high = time_index.reshape(outer, inner)[:, :1]
    scale = two_pi / samples
    low_angle = ((low * frequency) % samples).astype(jnp.float32) * scale
    high_angle = ((high * frequency) % samples).astype(jnp.float32) * scale
    cl, sl = jnp.cos(low_angle)[None], jnp.sin(low_angle)[None]
    ch, sh = jnp.cos(high_angle)[:, None], jnp.sin(high_angle)[:, None]
    cosine = (ch * cl - sh * sl).reshape(samples, bins)
    sine = (sh * cl + ch * sl).reshape(samples, bins)
    return jnp.concatenate([cosine, -sine], axis=1)


def band_matrix(bins):
    g = jnp.arange(bins, dtype=jnp.int32)
    near = jnp.abs(g[:, None] - g[None, :]) <= HALF_BAND
    return near.astype(jnp.bfloat16)


def lag_kernel(samples, first_lag, lag_count):
    bin_count = samples // 2
    inner = 32
    frequency = jnp.arange(bin_count, dtype=jnp.int32)[:, None]
    low = jnp.arange(inner, dtype=jnp.int32)[None, :]
    high = first_lag - LAGS // 2 + jnp.arange(lag_count // inner, dtype=jnp.int32)[None, :] * inner
    scale = two_pi / samples
    low_angle = jnp.mod(frequency * low, samples).astype(jnp.float32) * scale
    high_angle = jnp.mod(frequency * high, samples).astype(jnp.float32) * scale
    cl, sl = jnp.cos(low_angle)[:, None, :], jnp.sin(low_angle)[:, None, :]
    ch, sh = jnp.cos(high_angle)[:, :, None], jnp.sin(high_angle)[:, :, None]
    cosine = (ch * cl - sh * sl).reshape(bin_count, lag_count)
    sine = (sh * cl + ch * sl).reshape(bin_count, lag_count)
    return jnp.concatenate([cosine, -sine], axis=0).astype(jnp.bfloat16)


def whiten_series(series, table):
    samples = series.shape[1]
    bins = samples // 2
    hi, lo = split_bf16(table, 2)
    both = jnp.dot(series, jnp.concatenate([hi, lo], axis=1), preferred_element_type=jnp.float32)
    spectrum = both[:, : 2 * bins] + both[:, 2 * bins :]
    real_part = spectrum[:, :bins]
    imag_part = spectrum[:, bins:]
    powers = real_part * real_part + imag_part * imag_part
    pieces = split_bf16(powers, 3)
    band = band_matrix(bins)
    window = jnp.dot(
        jnp.concatenate(pieces, axis=1),
        jnp.concatenate([band] * 3, axis=0),
        preferred_element_type=jnp.float32,
    )
    window_span = 2 * HALF_BAND + 1
    factor = 1.0 / jnp.sqrt(window / window_span + epsilon)
    return jnp.concatenate([real_part * factor, imag_part * factor], axis=1).astype(jnp.bfloat16)


def correlate_kernel(factor, bins, group, half, mine_ref, other_ref, lag_ref, out_ref):
    step = pl.program_id(0)
    first = lax.axis_index("tm") == 0
    lag = lag_ref[...]
    receivers = [mine_ref[:half, :].astype(jnp.float32), other_ref[:half, :].astype(jnp.float32)]
    places = [jnp.where(first, 0, half), jnp.where(first, half, 0)]
    mine_src = mine_ref[half:, :]
    other_src = other_ref[half:, :]
    every = jnp.where(
        first,
        jnp.concatenate([mine_src, other_src], axis=0),
        jnp.concatenate([other_src, mine_src], axis=0),
    ).astype(jnp.float32)
    picked = every[:group]
    for g in range(1, every.shape[0] // group):
        picked = jnp.where(step == g, every[g * group : (g + 1) * group], picked)
    for k in range(group):
        row = picked[k : k + 1]
        real_src = row[:, :bins]
        imag_src = row[:, bins:]
        for part, rcv in enumerate(receivers):
            real_rcv = rcv[:, :bins]
            imag_rcv = rcv[:, bins:]
            cross = jnp.concatenate(
                [real_src * real_rcv + imag_src * imag_rcv, imag_src * real_rcv - real_src * imag_rcv],
                axis=1,
            ).astype(jnp.bfloat16)
            out_ref[k, pl.ds(pl.multiple_of(places[part], 8), half), :] = (
                jnp.dot(cross, lag, preferred_element_type=jnp.float32) * factor
            )


def correlate(low, high, half, lag):
    rows, width = low.shape
    bins = width // 2
    count = 2 * (rows - half)
    block = 2 * half
    lags = lag.shape[1]
    group = 8
    factor = 1.0 / math.sqrt(bins)
    flops = 2 * count * block * width * lags + 6 * count * block * bins
    moved = 4 * rows * width + 2 * lags * width + 4 * count * block * lags
    return pl.pallas_call(
        functools.partial(correlate_kernel, factor, bins, group, half),
        out_shape=jax.ShapeDtypeStruct((count, block, lags), jnp.float32),
        grid=(count // group,),
        in_specs=[
            pl.BlockSpec((rows, width), lambda s: (0, 0)),
            pl.BlockSpec((rows, width), lambda s: (0, 0)),
            pl.BlockSpec((width, lags), lambda s: (0, 0)),
        ],
        out_specs=pl.BlockSpec((group, block, lags), lambda s: (s, 0, 0)),
        compiler_params=pltpu.CompilerParams(dimension_semantics=("arbitrary",)),
        cost_estimate=pl.CostEstimate(flops=flops, bytes_accessed=moved, transcendentals=0),
    )(low, high, lag)


def swap_tm(x):
    other = lax.ppermute(x, "tm", perm=[(0, 1), (1, 0)])
    first = lax.axis_index("tm") == 0
    return jnp.where(first, x, other), jnp.where(first, other, x)


def local(records, fir_taps, channel_map, source_owner, source_offset):
    n_chan = lax.axis_size("chan")
    n_tm = lax.axis_size("tm")
    assert n_tm == 2
    n_dev = n_chan * n_tm
    raw_rows, channels = records.shape
    block = channels // n_chan
    half = block // n_tm
    out_rows = raw_rows // STRIDE
    halo_rows = TAPS - STRIDE
    samples = out_rows * n_dev
    bins = samples // 2
    tm = lax.axis_index("tm")

    shift = [(b, b - 1) for b in range(1, n_dev)]
    halo = lax.ppermute(records[:halo_rows], ("chan", "tm"), perm=shift)

    taps_matrix = decimation_matrix(fir_taps, out_rows, raw_rows + halo_rows)
    stacked = jnp.concatenate(split_bf16(taps_matrix, 2), axis=0)
    main = jnp.dot(stacked[:, :raw_rows], records, preferred_element_type=jnp.float32)
    tail = jnp.dot(stacked[:, raw_rows:], halo, preferred_element_type=jnp.float32)
    summed = main + tail
    decimated = (summed[:out_rows] + summed[out_rows:]).astype(jnp.bfloat16).T

    first, second = swap_tm(decimated)
    paired = jnp.concatenate([first, second], axis=1)

    owner = lax.dynamic_index_in_dim(source_owner, tm, keepdims=False)
    offset = lax.dynamic_index_in_dim(source_offset, tm, keepdims=False)
    source_raw = lax.dynamic_slice_in_dim(channel_map, owner * block + offset, SRC)
    half_raw = lax.dynamic_slice(channel_map.reshape(n_chan, block), (0, tm * half), (n_chan, half))
    index = jnp.concatenate(
        [half_raw, jnp.broadcast_to(source_raw[None], (n_chan, SRC))], axis=1
    )
    width = index.shape[1]
    rows = jnp.take(paired, index.reshape(-1), axis=0, mode="clip").reshape(n_chan, width, -1)
    series = lax.all_to_all(rows, "chan", 0, 2, tiled=True).reshape(width, samples)
    table = dft_table(samples, bins, jnp.arange(samples, dtype=jnp.int32))
    lag_share = LAGS // n_tm
    lag = lag_kernel(samples, tm * lag_share, lag_share)

    white = whiten_series(series, table)
    other = lax.ppermute(white, "tm", perm=[(0, 1), (1, 0)])
    result = correlate(white, other, half, lag)
    return result.reshape(STEPS, SRC, block, lag_share)


def solution(mesh):
    return jax.shard_map(
        local,
        mesh=mesh,
        in_specs=(P(("chan", "tm"), "parts"), P(), P("parts"), P("parts"), P("parts")),
        out_specs=P(None, None, ("parts", "chan"), "tm"),
        check_vma=False,
    )
```

```python
import functools
import math

import jax
import jax.numpy as jnp
from jax import lax
from jax.experimental import pallas as pl
from jax.experimental.pallas import tpu as pltpu
from jax.sharding import PartitionSpec as P

SRC = 16
STEPS = 2
LAGS = 512
TAPS = 32
STRIDE = 8
HALF_BAND = 32

two_pi = 2.0 * math.pi
epsilon = 1e-06


def split_bf16(x, parts):
    pieces = []
    rest = x
    for _ in range(parts):
        piece = rest.astype(jnp.bfloat16)
        pieces.append(piece)
        rest = rest - piece.astype(jnp.float32)
    return pieces


def decimation_matrix(fir_taps, out_rows, in_rows):
    leads = TAPS // STRIDE
    rows = jnp.arange(out_rows, dtype=jnp.int32)[:, None, None, None]
    groups = jnp.arange(in_rows // STRIDE, dtype=jnp.int32)[None, :, None, None]
    lead = jnp.arange(leads, dtype=jnp.int32)[None, None, :, None]
    taps = fir_taps.reshape(1, 1, leads, STRIDE)
    matrix = jnp.where(groups - rows == lead, taps, 0.0).sum(axis=2)
    return matrix.reshape(out_rows, in_rows)


def dft_table(samples, bins, time_index):
    inner = 32
    outer = samples // inner
    frequency = jnp.arange(bins, dtype=jnp.int32)[None, :]
    low = jnp.arange(inner, dtype=jnp.int32)[:, None]
    high = time_index.reshape(outer, inner)[:, :1]
    scale = two_pi / samples
    low_angle = ((low * frequency) % samples).astype(jnp.float32) * scale
    high_angle = ((high * frequency) % samples).astype(jnp.float32) * scale
    cl, sl = jnp.cos(low_angle)[None], jnp.sin(low_angle)[None]
    ch, sh = jnp.cos(high_angle)[:, None], jnp.sin(high_angle)[:, None]
    cosine = (ch * cl - sh * sl).reshape(samples, bins)
    sine = (sh * cl + ch * sl).reshape(samples, bins)
    return jnp.concatenate([cosine, -sine], axis=1)


def band_matrix(bins):
    g = jnp.arange(bins, dtype=jnp.int32)
    near = jnp.abs(g[:, None] - g[None, :]) <= HALF_BAND
    return near.astype(jnp.bfloat16)


def lag_kernel(samples, first_lag, lag_count):
    bin_count = samples // 2
    inner = 32
    frequency = jnp.arange(bin_count, dtype=jnp.int32)[:, None]
    low = jnp.arange(inner, dtype=jnp.int32)[None, :]
    high = first_lag - LAGS // 2 + jnp.arange(lag_count // inner, dtype=jnp.int32)[None, :] * inner
    scale = two_pi / samples
    low_angle = jnp.mod(frequency * low, samples).astype(jnp.float32) * scale
    high_angle = jnp.mod(frequency * high, samples).astype(jnp.float32) * scale
    cl, sl = jnp.cos(low_angle)[:, None, :], jnp.sin(low_angle)[:, None, :]
    ch, sh = jnp.cos(high_angle)[:, :, None], jnp.sin(high_angle)[:, :, None]
    cosine = (ch * cl - sh * sl).reshape(bin_count, lag_count)
    sine = (sh * cl + ch * sl).reshape(bin_count, lag_count)
    return jnp.concatenate([cosine, -sine], axis=0).astype(jnp.bfloat16)


def whiten_series(series, table):
    samples = series.shape[1]
    bins = samples // 2
    hi, lo = split_bf16(table, 2)
    both = jnp.dot(series, jnp.concatenate([hi, lo], axis=1), preferred_element_type=jnp.float32)
    spectrum = both[:, : 2 * bins] + both[:, 2 * bins :]
    real_part = spectrum[:, :bins]
    imag_part = spectrum[:, bins:]
    powers = real_part * real_part + imag_part * imag_part
    pieces = split_bf16(powers, 3)
    band = band_matrix(bins)
    window = jnp.dot(
        jnp.concatenate(pieces, axis=1),
        jnp.concatenate([band] * 3, axis=0),
        preferred_element_type=jnp.float32,
    )
    window_span = 2 * HALF_BAND + 1
    factor = 1.0 / jnp.sqrt(window / window_span + epsilon)
    return jnp.concatenate([real_part * factor, imag_part * factor], axis=1).astype(jnp.bfloat16)


def correlate_kernel(factor, bins, group, half, mine_ref, other_ref, lag_ref, out_ref):
    step = pl.program_id(0)
    first = lax.axis_index("tm") == 0
    lag = lag_ref[...]
    receivers = [mine_ref[:half, :], other_ref[:half, :]]
    places = [jnp.where(first, 0, half), jnp.where(first, half, 0)]
    mine_src = mine_ref[half:, :]
    other_src = other_ref[half:, :]
    every = jnp.where(
        first,
        jnp.concatenate([mine_src, other_src], axis=0),
        jnp.concatenate([other_src, mine_src], axis=0),
    )
    picked = every[:group]
    for g in range(1, every.shape[0] // group):
        picked = jnp.where(step == g, every[g * group : (g + 1) * group], picked)
    for k in range(group):
        row = picked[k : k + 1]
        real_src = row[:, :bins]
        imag_src = row[:, bins:]
        for part, rcv in enumerate(receivers):
            real_rcv = rcv[:, :bins]
            imag_rcv = rcv[:, bins:]
            cross = jnp.concatenate(
                [real_src * real_rcv + imag_src * imag_rcv, imag_src * real_rcv - real_src * imag_rcv],
                axis=1,
            )
            out_ref[k, pl.ds(pl.multiple_of(places[part], 8), half), :] = (
                jnp.dot(cross, lag, preferred_element_type=jnp.float32) * factor
            )


def correlate(low, high, half, lag):
    rows, width = low.shape
    bins = width // 2
    count = 2 * (rows - half)
    block = 2 * half
    lags = lag.shape[1]
    group = 8
    factor = 1.0 / math.sqrt(bins)
    flops = 2 * count * block * width * lags + 6 * count * block * bins
    moved = 4 * rows * width + 2 * lags * width + 4 * count * block * lags
    return pl.pallas_call(
        functools.partial(correlate_kernel, factor, bins, group, half),
        out_shape=jax.ShapeDtypeStruct((count, block, lags), jnp.float32),
        grid=(count // group,),
        in_specs=[
            pl.BlockSpec((rows, width), lambda s: (0, 0)),
            pl.BlockSpec((rows, width), lambda s: (0, 0)),
            pl.BlockSpec((width, lags), lambda s: (0, 0)),
        ],
        out_specs=pl.BlockSpec((group, block, lags), lambda s: (s, 0, 0)),
        compiler_params=pltpu.CompilerParams(dimension_semantics=("arbitrary",)),
        cost_estimate=pl.CostEstimate(flops=flops, bytes_accessed=moved, transcendentals=0),
    )(low, high, lag)


def swap_tm(x):
    other = lax.ppermute(x, "tm", perm=[(0, 1), (1, 0)])
    first = lax.axis_index("tm") == 0
    return jnp.where(first, x, other), jnp.where(first, other, x)


def local(records, fir_taps, channel_map, source_owner, source_offset):
    n_chan = lax.axis_size("chan")
    n_tm = lax.axis_size("tm")
    assert n_tm == 2
    n_dev = n_chan * n_tm
    raw_rows, channels = records.shape
    block = channels // n_chan
    half = block // n_tm
    out_rows = raw_rows // STRIDE
    halo_rows = TAPS - STRIDE
    samples = out_rows * n_dev
    bins = samples // 2
    tm = lax.axis_index("tm")

    shift = [(b, b - 1) for b in range(1, n_dev)]
    halo = lax.ppermute(records[:halo_rows], ("chan", "tm"), perm=shift)

    taps_matrix = decimation_matrix(fir_taps, out_rows, raw_rows + halo_rows)
    stacked = jnp.concatenate(split_bf16(taps_matrix, 2), axis=0)
    main = jnp.dot(stacked[:, :raw_rows], records, preferred_element_type=jnp.float32)
    tail = jnp.dot(stacked[:, raw_rows:], halo, preferred_element_type=jnp.float32)
    summed = main + tail
    decimated = (summed[:out_rows] + summed[out_rows:]).astype(jnp.bfloat16).T

    first, second = swap_tm(decimated)
    paired = jnp.concatenate([first, second], axis=1)

    owner = lax.dynamic_index_in_dim(source_owner, tm, keepdims=False)
    offset = lax.dynamic_index_in_dim(source_offset, tm, keepdims=False)
    source_raw = lax.dynamic_slice_in_dim(channel_map, owner * block + offset, SRC)
    half_raw = lax.dynamic_slice(channel_map.reshape(n_chan, block), (0, tm * half), (n_chan, half))
    index = jnp.concatenate(
        [half_raw, jnp.broadcast_to(source_raw[None], (n_chan, SRC))], axis=1
    )
    width = index.shape[1]
    rows = jnp.take(paired, index.reshape(-1), axis=0, mode="clip").reshape(n_chan, width, -1)
    series = lax.all_to_all(rows, "chan", 0, 2, tiled=True).reshape(width, samples)
    table = dft_table(samples, bins, jnp.arange(samples, dtype=jnp.int32))
    lag_share = LAGS // n_tm
    lag = lag_kernel(samples, tm * lag_share, lag_share)

    white = whiten_series(series, table)
    other = lax.ppermute(white, "tm", perm=[(0, 1), (1, 0)])
    result = correlate(white, other, half, lag)
    return result.reshape(STEPS, SRC, block, lag_share)


def solution(mesh):
    return jax.shard_map(
        local,
        mesh=mesh,
        in_specs=(P(("chan", "tm"), "parts"), P(), P("parts"), P("parts"), P("parts")),
        out_specs=P(None, None, ("parts", "chan"), "tm"),
        check_vma=False,
    )
```

```python
import functools
import math

import jax
import jax.numpy as jnp
from jax import lax
from jax.experimental import pallas as pl
from jax.experimental.pallas import tpu as pltpu
from jax.sharding import PartitionSpec as P

SRC = 16
STEPS = 2
LAGS = 512
TAPS = 32
STRIDE = 8
HALF_BAND = 32

two_pi = 2.0 * math.pi
epsilon = 1e-06


def split_bf16(x, parts):
    pieces = []
    rest = x
    for _ in range(parts):
        piece = rest.astype(jnp.bfloat16)
        pieces.append(piece)
        rest = rest - piece.astype(jnp.float32)
    return pieces


def decimation_matrix(fir_taps, out_rows, in_rows):
    rows = jnp.arange(out_rows, dtype=jnp.int32)[:, None, None]
    cols = jnp.arange(in_rows, dtype=jnp.int32)[None, :, None]
    tap = jnp.arange(TAPS, dtype=jnp.int32)[None, None, :]
    return jnp.where(cols - STRIDE * rows == tap, fir_taps[None, None, :], 0.0).sum(axis=2)


def dft_table(samples, bins, time_index):
    inner = 32
    outer = samples // inner
    frequency = jnp.arange(bins, dtype=jnp.int32)[None, :]
    low = jnp.arange(inner, dtype=jnp.int32)[:, None]
    high = time_index.reshape(outer, inner)[:, :1]
    scale = two_pi / samples
    low_angle = ((low * frequency) % samples).astype(jnp.float32) * scale
    high_angle = ((high * frequency) % samples).astype(jnp.float32) * scale
    cl, sl = jnp.cos(low_angle)[None], jnp.sin(low_angle)[None]
    ch, sh = jnp.cos(high_angle)[:, None], jnp.sin(high_angle)[:, None]
    cosine = (ch * cl - sh * sl).reshape(samples, bins)
    sine = (sh * cl + ch * sl).reshape(samples, bins)
    return jnp.concatenate([cosine, -sine], axis=1)


def band_matrix(bins):
    g = jnp.arange(bins, dtype=jnp.int32)
    near = jnp.abs(g[:, None] - g[None, :]) <= HALF_BAND
    return near.astype(jnp.bfloat16)


def lag_kernel(samples, first_lag, lag_count):
    bin_count = samples // 2
    inner = 32
    frequency = jnp.arange(bin_count, dtype=jnp.int32)[:, None]
    low = jnp.arange(inner, dtype=jnp.int32)[None, :]
    high = first_lag - LAGS // 2 + jnp.arange(lag_count // inner, dtype=jnp.int32)[None, :] * inner
    scale = two_pi / samples
    low_angle = jnp.mod(frequency * low, samples).astype(jnp.float32) * scale
    high_angle = jnp.mod(frequency * high, samples).astype(jnp.float32) * scale
    cl, sl = jnp.cos(low_angle)[:, None, :], jnp.sin(low_angle)[:, None, :]
    ch, sh = jnp.cos(high_angle)[:, :, None], jnp.sin(high_angle)[:, :, None]
    cosine = (ch * cl - sh * sl).reshape(bin_count, lag_count)
    sine = (sh * cl + ch * sl).reshape(bin_count, lag_count)
    return jnp.concatenate([cosine, -sine], axis=0).astype(jnp.bfloat16)


def whiten_series(series, table):
    samples = series.shape[1]
    bins = samples // 2
    hi, lo = split_bf16(table, 2)
    both = jnp.dot(series, jnp.concatenate([hi, lo], axis=1), preferred_element_type=jnp.float32)
    spectrum = both[:, : 2 * bins] + both[:, 2 * bins :]
    real_part = spectrum[:, :bins]
    imag_part = spectrum[:, bins:]
    powers = real_part * real_part + imag_part * imag_part
    pieces = split_bf16(powers, 3)
    band = band_matrix(bins)
    window = jnp.dot(
        jnp.concatenate(pieces, axis=1),
        jnp.concatenate([band] * 3, axis=0),
        preferred_element_type=jnp.float32,
    )
    window_span = 2 * HALF_BAND + 1
    factor = 1.0 / jnp.sqrt(window / window_span + epsilon)
    return jnp.concatenate([real_part * factor, imag_part * factor], axis=1).astype(jnp.bfloat16)


def correlate_kernel(factor, bins, group, half, mine_ref, other_ref, lag_ref, out_ref):
    step = pl.program_id(0)
    first = lax.axis_index("tm") == 0
    lag = lag_ref[...]
    receivers = [mine_ref[:half, :].astype(jnp.float32), other_ref[:half, :].astype(jnp.float32)]
    places = [jnp.where(first, 0, half), jnp.where(first, half, 0)]
    mine_src = mine_ref[half:, :]
    other_src = other_ref[half:, :]
    every = jnp.where(
        first,
        jnp.concatenate([mine_src, other_src], axis=0),
        jnp.concatenate([other_src, mine_src], axis=0),
    ).astype(jnp.float32)
    picked = every[:group]
    for g in range(1, every.shape[0] // group):
        picked = jnp.where(step == g, every[g * group : (g + 1) * group], picked)
    for k in range(group):
        row = picked[k : k + 1]
        real_src = row[:, :bins]
        imag_src = row[:, bins:]
        for part, rcv in enumerate(receivers):
            real_rcv = rcv[:, :bins]
            imag_rcv = rcv[:, bins:]
            cross = jnp.concatenate(
                [real_src * real_rcv + imag_src * imag_rcv, imag_src * real_rcv - real_src * imag_rcv],
                axis=1,
            ).astype(jnp.bfloat16)
            out_ref[k, pl.ds(pl.multiple_of(places[part], 8), half), :] = (
                jnp.dot(cross, lag, preferred_element_type=jnp.float32) * factor
            )


def correlate(low, high, half, lag):
    rows, width = low.shape
    bins = width // 2
    count = 2 * (rows - half)
    block = 2 * half
    lags = lag.shape[1]
    group = 8
    factor = 1.0 / math.sqrt(bins)
    flops = 2 * count * block * width * lags + 6 * count * block * bins
    moved = 4 * rows * width + 2 * lags * width + 4 * count * block * lags
    return pl.pallas_call(
        functools.partial(correlate_kernel, factor, bins, group, half),
        out_shape=jax.ShapeDtypeStruct((count, block, lags), jnp.float32),
        grid=(count // group,),
        in_specs=[
            pl.BlockSpec((rows, width), lambda s: (0, 0)),
            pl.BlockSpec((rows, width), lambda s: (0, 0)),
            pl.BlockSpec((width, lags), lambda s: (0, 0)),
        ],
        out_specs=pl.BlockSpec((group, block, lags), lambda s: (s, 0, 0)),
        compiler_params=pltpu.CompilerParams(dimension_semantics=("arbitrary",)),
        cost_estimate=pl.CostEstimate(flops=flops, bytes_accessed=moved, transcendentals=0),
    )(low, high, lag)


def swap_tm(x):
    other = lax.ppermute(x, "tm", perm=[(0, 1), (1, 0)])
    first = lax.axis_index("tm") == 0
    return jnp.where(first, x, other), jnp.where(first, other, x)


def local(records, fir_taps, channel_map, source_owner, source_offset):
    n_chan = lax.axis_size("chan")
    n_tm = lax.axis_size("tm")
    assert n_tm == 2
    n_dev = n_chan * n_tm
    raw_rows, channels = records.shape
    block = channels // n_chan
    half = block // n_tm
    out_rows = raw_rows // STRIDE
    halo_rows = TAPS - STRIDE
    samples = out_rows * n_dev
    bins = samples // 2
    tm = lax.axis_index("tm")

    shift = [(b, b - 1) for b in range(1, n_dev)]
    halo = lax.ppermute(records[:halo_rows], ("chan", "tm"), perm=shift)

    taps_matrix = decimation_matrix(fir_taps, out_rows, raw_rows + halo_rows)
    stacked = jnp.concatenate(split_bf16(taps_matrix, 2), axis=0)
    main = jnp.dot(stacked[:, :raw_rows], records, preferred_element_type=jnp.float32)
    tail = jnp.dot(stacked[:, raw_rows:], halo, preferred_element_type=jnp.float32)
    summed = main + tail
    decimated = (summed[:out_rows] + summed[out_rows:]).astype(jnp.bfloat16)

    first, second = swap_tm(decimated)
    paired = jnp.concatenate([first, second], axis=0).T

    steps = jnp.arange(source_owner.shape[0], dtype=jnp.int32)
    own_first = jnp.sum(jnp.where(steps == tm, source_owner * block + source_offset, 0))
    source_raw = lax.dynamic_slice_in_dim(channel_map, own_first, SRC)
    half_raw = lax.dynamic_slice(channel_map.reshape(n_chan, block), (0, tm * half), (n_chan, half))
    index = jnp.concatenate(
        [half_raw, jnp.broadcast_to(source_raw[None], (n_chan, SRC))], axis=1
    )
    width = index.shape[1]
    rows = jnp.take(paired, index.reshape(-1), axis=0, mode="clip").reshape(n_chan, width, -1)
    series = lax.all_to_all(rows, "chan", 0, 2, tiled=True).reshape(width, samples)
    table = dft_table(samples, bins, jnp.arange(samples, dtype=jnp.int32))
    lag_share = LAGS // n_tm
    lag = lag_kernel(samples, tm * lag_share, lag_share)

    white = whiten_series(series, table)
    other = lax.ppermute(white, "tm", perm=[(0, 1), (1, 0)])
    result = correlate(white, other, half, lag)
    return result.reshape(STEPS, SRC, block, lag_share)


def solution(mesh):
    return jax.shard_map(
        local,
        mesh=mesh,
        in_specs=(P(("chan", "tm"), "parts"), P(), P("parts"), P("parts"), P("parts")),
        out_specs=P(None, None, ("parts", "chan"), "tm"),
        check_vma=False,
    )
```

```python
import functools
import math

import jax
import jax.numpy as jnp
from jax import lax
from jax.experimental import pallas as pl
from jax.experimental.pallas import tpu as pltpu
from jax.sharding import PartitionSpec as P

SRC = 16
STEPS = 2
LAGS = 512
TAPS = 32
STRIDE = 8
HALF_BAND = 32

two_pi = 2.0 * math.pi
epsilon = 1e-06


def split_bf16(x, parts):
    pieces = []
    rest = x
    for _ in range(parts):
        piece = rest.astype(jnp.bfloat16)
        pieces.append(piece)
        rest = rest - piece.astype(jnp.float32)
    return pieces


def decimation_matrix(fir_taps, out_rows, in_rows):
    rows = jnp.arange(out_rows, dtype=jnp.int32)[:, None, None]
    cols = jnp.arange(in_rows, dtype=jnp.int32)[None, :, None]
    tap = jnp.arange(TAPS, dtype=jnp.int32)[None, None, :]
    return jnp.where(cols - STRIDE * rows == tap, fir_taps[None, None, :], 0.0).sum(axis=2)


def dft_table(samples, bins, time_index):
    inner = 32
    outer = samples // inner
    frequency = jnp.arange(bins, dtype=jnp.int32)[None, :]
    low = jnp.arange(inner, dtype=jnp.int32)[:, None]
    high = time_index.reshape(outer, inner)[:, :1]
    scale = two_pi / samples
    low_angle = ((low * frequency) % samples).astype(jnp.float32) * scale
    high_angle = ((high * frequency) % samples).astype(jnp.float32) * scale
    cl, sl = jnp.cos(low_angle)[None], jnp.sin(low_angle)[None]
    ch, sh = jnp.cos(high_angle)[:, None], jnp.sin(high_angle)[:, None]
    cosine = (ch * cl - sh * sl).reshape(samples, bins)
    sine = (sh * cl + ch * sl).reshape(samples, bins)
    return jnp.concatenate([cosine, -sine], axis=1)


def band_matrix(bins):
    g = jnp.arange(bins, dtype=jnp.int32)
    near = jnp.abs(g[:, None] - g[None, :]) <= HALF_BAND
    return near.astype(jnp.bfloat16)


def lag_kernel(samples, first_lag, lag_count):
    bin_count = samples // 2
    inner = 32
    frequency = jnp.arange(bin_count, dtype=jnp.int32)[:, None]
    low = jnp.arange(inner, dtype=jnp.int32)[None, :]
    high = first_lag - LAGS // 2 + jnp.arange(lag_count // inner, dtype=jnp.int32)[None, :] * inner
    scale = two_pi / samples
    low_angle = jnp.mod(frequency * low, samples).astype(jnp.float32) * scale
    high_angle = jnp.mod(frequency * high, samples).astype(jnp.float32) * scale
    cl, sl = jnp.cos(low_angle)[:, None, :], jnp.sin(low_angle)[:, None, :]
    ch, sh = jnp.cos(high_angle)[:, :, None], jnp.sin(high_angle)[:, :, None]
    cosine = (ch * cl - sh * sl).reshape(bin_count, lag_count)
    sine = (sh * cl + ch * sl).reshape(bin_count, lag_count)
    return jnp.concatenate([cosine, -sine], axis=0).astype(jnp.bfloat16)


def whiten_series(series, table):
    samples = series.shape[1]
    bins = samples // 2
    hi, lo = split_bf16(table, 2)
    both = jnp.dot(series, jnp.concatenate([hi, lo], axis=1), preferred_element_type=jnp.float32)
    spectrum = both[:, : 2 * bins] + both[:, 2 * bins :]
    real_part = spectrum[:, :bins]
    imag_part = spectrum[:, bins:]
    powers = real_part * real_part + imag_part * imag_part
    pieces = split_bf16(powers, 3)
    band = band_matrix(bins)
    window = jnp.dot(
        jnp.concatenate(pieces, axis=1),
        jnp.concatenate([band] * 3, axis=0),
        preferred_element_type=jnp.float32,
    )
    window_span = 2 * HALF_BAND + 1
    factor = 1.0 / jnp.sqrt(window / window_span + epsilon)
    return jnp.concatenate([real_part * factor, imag_part * factor], axis=1).astype(jnp.bfloat16)


def correlate_kernel(factor, bins, group, half, mine_ref, other_ref, lag_ref, out_ref, cross_ref):
    step = pl.program_id(0)
    first = lax.axis_index("tm") == 0
    lag = lag_ref[...]
    receivers = [mine_ref[:half, :].astype(jnp.float32), other_ref[:half, :].astype(jnp.float32)]
    places = [jnp.where(first, 0, half), jnp.where(first, half, 0)]
    mine_src = mine_ref[half:, :]
    other_src = other_ref[half:, :]
    every = jnp.where(
        first,
        jnp.concatenate([mine_src, other_src], axis=0),
        jnp.concatenate([other_src, mine_src], axis=0),
    ).astype(jnp.float32)
    picked = every[:group]
    for g in range(1, every.shape[0] // group):
        picked = jnp.where(step == g, every[g * group : (g + 1) * group], picked)
    for k in range(group):
        row = picked[k : k + 1]
        real_src = row[:, :bins]
        imag_src = row[:, bins:]
        for part, rcv in enumerate(receivers):
            real_rcv = rcv[:, :bins]
            imag_rcv = rcv[:, bins:]
            at = pl.multiple_of(k * 2 * half + places[part], 8)
            cross_ref[pl.ds(at, half), :bins] = (real_src * real_rcv + imag_src * imag_rcv).astype(
                jnp.bfloat16
            )
            cross_ref[pl.ds(at, half), bins:] = (imag_src * real_rcv - real_src * imag_rcv).astype(
                jnp.bfloat16
            )
    total = jnp.dot(cross_ref[...], lag, preferred_element_type=jnp.float32) * factor
    out_ref[...] = total.reshape(out_ref.shape)


def correlate(low, high, half, lag):
    rows, width = low.shape
    bins = width // 2
    count = 2 * (rows - half)
    block = 2 * half
    lags = lag.shape[1]
    group = 8
    factor = 1.0 / math.sqrt(bins)
    flops = 2 * count * block * width * lags + 6 * count * block * bins
    moved = 4 * rows * width + 2 * lags * width + 4 * count * block * lags
    return pl.pallas_call(
        functools.partial(correlate_kernel, factor, bins, group, half),
        out_shape=jax.ShapeDtypeStruct((count, block, lags), jnp.float32),
        grid=(count // group,),
        in_specs=[
            pl.BlockSpec((rows, width), lambda s: (0, 0)),
            pl.BlockSpec((rows, width), lambda s: (0, 0)),
            pl.BlockSpec((width, lags), lambda s: (0, 0)),
        ],
        out_specs=pl.BlockSpec((group, block, lags), lambda s: (s, 0, 0)),
        scratch_shapes=[pltpu.VMEM((group * block, width), jnp.bfloat16)],
        compiler_params=pltpu.CompilerParams(
            dimension_semantics=("arbitrary",), vmem_limit_bytes=48 * 1024 * 1024
        ),
        cost_estimate=pl.CostEstimate(flops=flops, bytes_accessed=moved, transcendentals=0),
    )(low, high, lag)


def swap_tm(x):
    other = lax.ppermute(x, "tm", perm=[(0, 1), (1, 0)])
    first = lax.axis_index("tm") == 0
    return jnp.where(first, x, other), jnp.where(first, other, x)


def local(records, fir_taps, channel_map, source_owner, source_offset):
    n_chan = lax.axis_size("chan")
    n_tm = lax.axis_size("tm")
    assert n_tm == 2
    n_dev = n_chan * n_tm
    raw_rows, channels = records.shape
    block = channels // n_chan
    half = block // n_tm
    out_rows = raw_rows // STRIDE
    halo_rows = TAPS - STRIDE
    samples = out_rows * n_dev
    bins = samples // 2
    tm = lax.axis_index("tm")

    shift = [(b, b - 1) for b in range(1, n_dev)]
    halo = lax.ppermute(records[:halo_rows], ("chan", "tm"), perm=shift)

    taps_matrix = decimation_matrix(fir_taps, out_rows, raw_rows + halo_rows)
    stacked = jnp.concatenate(split_bf16(taps_matrix, 2), axis=0)
    main = jnp.dot(stacked[:, :raw_rows], records, preferred_element_type=jnp.float32)
    tail = jnp.dot(stacked[:, raw_rows:], halo, preferred_element_type=jnp.float32)
    summed = main + tail
    decimated = (summed[:out_rows] + summed[out_rows:]).astype(jnp.bfloat16)

    first, second = swap_tm(decimated)
    paired = jnp.concatenate([first, second], axis=0).T

    steps = jnp.arange(source_owner.shape[0], dtype=jnp.int32)
    own_first = jnp.sum(jnp.where(steps == tm, source_owner * block + source_offset, 0))
    source_raw = lax.dynamic_slice_in_dim(channel_map, own_first, SRC)
    half_raw = lax.dynamic_slice(channel_map.reshape(n_chan, block), (0, tm * half), (n_chan, half))
    index = jnp.concatenate(
        [half_raw, jnp.broadcast_to(source_raw[None], (n_chan, SRC))], axis=1
    )
    width = index.shape[1]
    rows = jnp.take(paired, index.reshape(-1), axis=0, mode="clip").reshape(n_chan, width, -1)
    series = lax.all_to_all(rows, "chan", 0, 2, tiled=True).reshape(width, samples)
    table = dft_table(samples, bins, jnp.arange(samples, dtype=jnp.int32))
    lag_share = LAGS // n_tm
    lag = lag_kernel(samples, tm * lag_share, lag_share)

    white = whiten_series(series, table)
    other = lax.ppermute(white, "tm", perm=[(0, 1), (1, 0)])
    result = correlate(white, other, half, lag)
    return result.reshape(STEPS, SRC, block, lag_share)


def solution(mesh):
    return jax.shard_map(
        local,
        mesh=mesh,
        in_specs=(P(("chan", "tm"), "parts"), P(), P("parts"), P("parts"), P("parts")),
        out_specs=P(None, None, ("parts", "chan"), "tm"),
        check_vma=False,
    )
```

```python
import functools
import math

import jax
import jax.numpy as jnp
from jax import lax
from jax.experimental import pallas as pl
from jax.experimental.pallas import tpu as pltpu
from jax.sharding import PartitionSpec as P

SRC = 16
STEPS = 2
LAGS = 512
TAPS = 32
STRIDE = 8
HALF_BAND = 32

two_pi = 2.0 * math.pi
epsilon = 1e-06


def split_bf16(x, parts):
    pieces = []
    rest = x
    for _ in range(parts):
        piece = rest.astype(jnp.bfloat16)
        pieces.append(piece)
        rest = rest - piece.astype(jnp.float32)
    return pieces


def decimation_matrix(fir_taps, out_rows, in_rows):
    rows = jnp.arange(out_rows, dtype=jnp.int32)[:, None, None]
    cols = jnp.arange(in_rows, dtype=jnp.int32)[None, :, None]
    tap = jnp.arange(TAPS, dtype=jnp.int32)[None, None, :]
    return jnp.where(cols - STRIDE * rows == tap, fir_taps[None, None, :], 0.0).sum(axis=2)


def dft_table(samples, bins, time_index):
    inner = 32
    outer = samples // inner
    frequency = jnp.arange(bins, dtype=jnp.int32)[None, :]
    low = jnp.arange(inner, dtype=jnp.int32)[:, None]
    high = time_index.reshape(outer, inner)[:, :1]
    scale = two_pi / samples
    low_angle = ((low * frequency) % samples).astype(jnp.float32) * scale
    high_angle = ((high * frequency) % samples).astype(jnp.float32) * scale
    cl, sl = jnp.cos(low_angle)[None], jnp.sin(low_angle)[None]
    ch, sh = jnp.cos(high_angle)[:, None], jnp.sin(high_angle)[:, None]
    cosine = (ch * cl - sh * sl).reshape(samples, bins)
    sine = (sh * cl + ch * sl).reshape(samples, bins)
    return jnp.concatenate([cosine, -sine], axis=1)


def band_matrix(bins):
    g = jnp.arange(bins, dtype=jnp.int32)
    near = jnp.abs(g[:, None] - g[None, :]) <= HALF_BAND
    return near.astype(jnp.bfloat16)


def lag_kernel(samples, first_lag, lag_count):
    bin_count = samples // 2
    inner = 32
    frequency = jnp.arange(bin_count, dtype=jnp.int32)[:, None]
    low = jnp.arange(inner, dtype=jnp.int32)[None, :]
    high = first_lag - LAGS // 2 + jnp.arange(lag_count // inner, dtype=jnp.int32)[None, :] * inner
    scale = two_pi / samples
    low_angle = jnp.mod(frequency * low, samples).astype(jnp.float32) * scale
    high_angle = jnp.mod(frequency * high, samples).astype(jnp.float32) * scale
    cl, sl = jnp.cos(low_angle)[:, None, :], jnp.sin(low_angle)[:, None, :]
    ch, sh = jnp.cos(high_angle)[:, :, None], jnp.sin(high_angle)[:, :, None]
    cosine = (ch * cl - sh * sl).reshape(bin_count, lag_count)
    sine = (sh * cl + ch * sl).reshape(bin_count, lag_count)
    return jnp.concatenate([cosine, -sine], axis=0).astype(jnp.bfloat16)


def whiten_series(series, table):
    samples = series.shape[1]
    bins = samples // 2
    spectrum = jnp.dot(series, table.astype(jnp.bfloat16), preferred_element_type=jnp.float32)
    real_part = spectrum[:, :bins]
    imag_part = spectrum[:, bins:]
    powers = real_part * real_part + imag_part * imag_part
    pieces = split_bf16(powers, 3)
    band = band_matrix(bins)
    window = jnp.dot(
        jnp.concatenate(pieces, axis=1),
        jnp.concatenate([band] * 3, axis=0),
        preferred_element_type=jnp.float32,
    )
    window_span = 2 * HALF_BAND + 1
    factor = 1.0 / jnp.sqrt(window / window_span + epsilon)
    return jnp.concatenate([real_part * factor, imag_part * factor], axis=1).astype(jnp.bfloat16)


def correlate_kernel(factor, bins, group, half, mine_ref, other_ref, lag_ref, out_ref):
    step = pl.program_id(0)
    first = lax.axis_index("tm") == 0
    lag = lag_ref[...]
    receivers = [mine_ref[:half, :].astype(jnp.float32), other_ref[:half, :].astype(jnp.float32)]
    places = [jnp.where(first, 0, half), jnp.where(first, half, 0)]
    mine_src = mine_ref[half:, :]
    other_src = other_ref[half:, :]
    every = jnp.where(
        first,
        jnp.concatenate([mine_src, other_src], axis=0),
        jnp.concatenate([other_src, mine_src], axis=0),
    ).astype(jnp.float32)
    picked = every[:group]
    for g in range(1, every.shape[0] // group):
        picked = jnp.where(step == g, every[g * group : (g + 1) * group], picked)
    for k in range(group):
        row = picked[k : k + 1]
        real_src = row[:, :bins]
        imag_src = row[:, bins:]
        for part, rcv in enumerate(receivers):
            real_rcv = rcv[:, :bins]
            imag_rcv = rcv[:, bins:]
            cross = jnp.concatenate(
                [real_src * real_rcv + imag_src * imag_rcv, imag_src * real_rcv - real_src * imag_rcv],
                axis=1,
            ).astype(jnp.bfloat16)
            out_ref[k, pl.ds(pl.multiple_of(places[part], 8), half), :] = (
                jnp.dot(cross, lag, preferred_element_type=jnp.float32) * factor
            )


def correlate(low, high, half, lag):
    rows, width = low.shape
    bins = width // 2
    count = 2 * (rows - half)
    block = 2 * half
    lags = lag.shape[1]
    group = 8
    factor = 1.0 / math.sqrt(bins)
    flops = 2 * count * block * width * lags + 6 * count * block * bins
    moved = 4 * rows * width + 2 * lags * width + 4 * count * block * lags
    return pl.pallas_call(
        functools.partial(correlate_kernel, factor, bins, group, half),
        out_shape=jax.ShapeDtypeStruct((count, block, lags), jnp.float32),
        grid=(count // group,),
        in_specs=[
            pl.BlockSpec((rows, width), lambda s: (0, 0)),
            pl.BlockSpec((rows, width), lambda s: (0, 0)),
            pl.BlockSpec((width, lags), lambda s: (0, 0)),
        ],
        out_specs=pl.BlockSpec((group, block, lags), lambda s: (s, 0, 0)),
        compiler_params=pltpu.CompilerParams(dimension_semantics=("arbitrary",)),
        cost_estimate=pl.CostEstimate(flops=flops, bytes_accessed=moved, transcendentals=0),
    )(low, high, lag)


def swap_tm(x):
    other = lax.ppermute(x, "tm", perm=[(0, 1), (1, 0)])
    first = lax.axis_index("tm") == 0
    return jnp.where(first, x, other), jnp.where(first, other, x)


def local(records, fir_taps, channel_map, source_owner, source_offset):
    n_chan = lax.axis_size("chan")
    n_tm = lax.axis_size("tm")
    assert n_tm == 2
    n_dev = n_chan * n_tm
    raw_rows, channels = records.shape
    block = channels // n_chan
    half = block // n_tm
    out_rows = raw_rows // STRIDE
    halo_rows = TAPS - STRIDE
    samples = out_rows * n_dev
    bins = samples // 2
    tm = lax.axis_index("tm")

    shift = [(b, b - 1) for b in range(1, n_dev)]
    halo = lax.ppermute(records[:halo_rows], ("chan", "tm"), perm=shift)

    taps_matrix = decimation_matrix(fir_taps, out_rows, raw_rows + halo_rows)
    stacked = jnp.concatenate(split_bf16(taps_matrix, 2), axis=0)
    main = jnp.dot(stacked[:, :raw_rows], records, preferred_element_type=jnp.float32)
    tail = jnp.dot(stacked[:, raw_rows:], halo, preferred_element_type=jnp.float32)
    summed = main + tail
    decimated = (summed[:out_rows] + summed[out_rows:]).astype(jnp.bfloat16)

    first, second = swap_tm(decimated)
    paired = jnp.concatenate([first, second], axis=0).T

    steps = jnp.arange(source_owner.shape[0], dtype=jnp.int32)
    own_first = jnp.sum(jnp.where(steps == tm, source_owner * block + source_offset, 0))
    source_raw = lax.dynamic_slice_in_dim(channel_map, own_first, SRC)
    half_raw = lax.dynamic_slice(channel_map.reshape(n_chan, block), (0, tm * half), (n_chan, half))
    index = jnp.concatenate(
        [half_raw, jnp.broadcast_to(source_raw[None], (n_chan, SRC))], axis=1
    )
    width = index.shape[1]
    rows = jnp.take(paired, index.reshape(-1), axis=0, mode="clip").reshape(n_chan, width, -1)
    series = lax.all_to_all(rows, "chan", 0, 2, tiled=True).reshape(width, samples)
    table = dft_table(samples, bins, jnp.arange(samples, dtype=jnp.int32))
    lag_share = LAGS // n_tm
    lag = lag_kernel(samples, tm * lag_share, lag_share)

    white = whiten_series(series, table)
    other = lax.ppermute(white, "tm", perm=[(0, 1), (1, 0)])
    result = correlate(white, other, half, lag)
    return result.reshape(STEPS, SRC, block, lag_share)


def solution(mesh):
    return jax.shard_map(
        local,
        mesh=mesh,
        in_specs=(P(("chan", "tm"), "parts"), P(), P("parts"), P("parts"), P("parts")),
        out_specs=P(None, None, ("parts", "chan"), "tm"),
        check_vma=False,
    )
```

```python
import functools
import math

import jax
import jax.numpy as jnp
from jax import lax
from jax.experimental import pallas as pl
from jax.experimental.pallas import tpu as pltpu
from jax.sharding import PartitionSpec as P

SRC = 16
STEPS = 2
LAGS = 512
TAPS = 32
STRIDE = 8
HALF_BAND = 32

two_pi = 2.0 * math.pi
epsilon = 1e-06


def decimation_matrix(fir_taps, out_rows, in_rows):
    leads = TAPS // STRIDE
    rows = jnp.arange(out_rows, dtype=jnp.int32)[:, None, None, None]
    groups = jnp.arange(in_rows // STRIDE, dtype=jnp.int32)[None, :, None, None]
    lead = jnp.arange(leads, dtype=jnp.int32)[None, None, :, None]
    taps = fir_taps.reshape(1, 1, leads, STRIDE)
    matrix = jnp.where(groups - rows == lead, taps, 0.0).sum(axis=2)
    return matrix.reshape(out_rows, in_rows)


def dft_table(samples, bins, time_index):
    inner = 32
    outer = samples // inner
    frequency = jnp.arange(bins, dtype=jnp.int32)[None, :]
    low = jnp.arange(inner, dtype=jnp.int32)[:, None]
    high = time_index.reshape(outer, inner)[:, :1]
    scale = two_pi / samples
    low_angle = ((low * frequency) % samples).astype(jnp.float32) * scale
    high_angle = ((high * frequency) % samples).astype(jnp.float32) * scale
    cl, sl = jnp.cos(low_angle)[None], jnp.sin(low_angle)[None]
    ch, sh = jnp.cos(high_angle)[:, None], jnp.sin(high_angle)[:, None]
    cosine = (ch * cl - sh * sl).reshape(samples, bins)
    sine = (sh * cl + ch * sl).reshape(samples, bins)
    return jnp.concatenate([cosine, -sine], axis=1)


def band_matrix(bins):
    g = jnp.arange(bins, dtype=jnp.int32)
    near = jnp.abs(g[:, None] - g[None, :]) <= HALF_BAND
    return near.astype(jnp.bfloat16)


def lag_kernel(samples, first_lag, lag_count):
    bin_count = samples // 2
    inner = 32
    frequency = jnp.arange(bin_count, dtype=jnp.int32)[:, None]
    low = jnp.arange(inner, dtype=jnp.int32)[None, :]
    high = first_lag - LAGS // 2 + jnp.arange(lag_count // inner, dtype=jnp.int32)[None, :] * inner
    scale = two_pi / samples
    low_angle = jnp.mod(frequency * low, samples).astype(jnp.float32) * scale
    high_angle = jnp.mod(frequency * high, samples).astype(jnp.float32) * scale
    cl, sl = jnp.cos(low_angle)[:, None, :], jnp.sin(low_angle)[:, None, :]
    ch, sh = jnp.cos(high_angle)[:, :, None], jnp.sin(high_angle)[:, :, None]
    cosine = (ch * cl - sh * sl).reshape(bin_count, lag_count)
    sine = (sh * cl + ch * sl).reshape(bin_count, lag_count)
    return jnp.concatenate([cosine, -sine], axis=0).astype(jnp.bfloat16)


def whiten_series(series, table):
    samples = series.shape[1]
    bins = samples // 2
    spectrum = jnp.dot(series, table.astype(jnp.bfloat16), preferred_element_type=jnp.float32)
    real_part = spectrum[:, :bins]
    imag_part = spectrum[:, bins:]
    powers = real_part * real_part + imag_part * imag_part
    window = jnp.dot(powers.astype(jnp.bfloat16), band_matrix(bins), preferred_element_type=jnp.float32)
    window_span = 2 * HALF_BAND + 1
    factor = 1.0 / jnp.sqrt(window / window_span + epsilon)
    return jnp.concatenate([real_part * factor, imag_part * factor], axis=1).astype(jnp.bfloat16)


def correlate_kernel(factor, bins, group, half, mine_ref, other_ref, lag_ref, out_ref):
    step = pl.program_id(0)
    first = lax.axis_index("tm") == 0
    lag = lag_ref[...]
    receivers = [mine_ref[:half, :].astype(jnp.float32), other_ref[:half, :].astype(jnp.float32)]
    places = [jnp.where(first, 0, half), jnp.where(first, half, 0)]
    mine_src = mine_ref[half:, :]
    other_src = other_ref[half:, :]
    every = jnp.where(
        first,
        jnp.concatenate([mine_src, other_src], axis=0),
        jnp.concatenate([other_src, mine_src], axis=0),
    ).astype(jnp.float32)
    picked = every[:group]
    for g in range(1, every.shape[0] // group):
        picked = jnp.where(step == g, every[g * group : (g + 1) * group], picked)
    for k in range(group):
        row = picked[k : k + 1]
        real_src = row[:, :bins]
        imag_src = row[:, bins:]
        for part, rcv in enumerate(receivers):
            real_rcv = rcv[:, :bins]
            imag_rcv = rcv[:, bins:]
            cross = jnp.concatenate(
                [real_src * real_rcv + imag_src * imag_rcv, imag_src * real_rcv - real_src * imag_rcv],
                axis=1,
            ).astype(jnp.bfloat16)
            out_ref[k, pl.ds(pl.multiple_of(places[part], 8), half), :] = (
                jnp.dot(cross, lag, preferred_element_type=jnp.float32) * factor
            )


def correlate(low, high, half, lag):
    rows, width = low.shape
    bins = width // 2
    count = 2 * (rows - half)
    block = 2 * half
    lags = lag.shape[1]
    group = 8
    factor = 1.0 / math.sqrt(bins)
    flops = 2 * count * block * width * lags + 6 * count * block * bins
    moved = 4 * rows * width + 2 * lags * width + 4 * count * block * lags
    return pl.pallas_call(
        functools.partial(correlate_kernel, factor, bins, group, half),
        out_shape=jax.ShapeDtypeStruct((count, block, lags), jnp.float32),
        grid=(count // group,),
        in_specs=[
            pl.BlockSpec((rows, width), lambda s: (0, 0)),
            pl.BlockSpec((rows, width), lambda s: (0, 0)),
            pl.BlockSpec((width, lags), lambda s: (0, 0)),
        ],
        out_specs=pl.BlockSpec((group, block, lags), lambda s: (s, 0, 0)),
        compiler_params=pltpu.CompilerParams(dimension_semantics=("arbitrary",)),
        cost_estimate=pl.CostEstimate(flops=flops, bytes_accessed=moved, transcendentals=0),
    )(low, high, lag)


def swap_tm(x):
    other = lax.ppermute(x, "tm", perm=[(0, 1), (1, 0)])
    first = lax.axis_index("tm") == 0
    return jnp.where(first, x, other), jnp.where(first, other, x)


def local(records, fir_taps, channel_map, source_owner, source_offset):
    n_chan = lax.axis_size("chan")
    n_tm = lax.axis_size("tm")
    assert n_tm == 2
    n_dev = n_chan * n_tm
    raw_rows, channels = records.shape
    block = channels // n_chan
    half = block // n_tm
    out_rows = raw_rows // STRIDE
    halo_rows = TAPS - STRIDE
    samples = out_rows * n_dev
    bins = samples // 2
    tm = lax.axis_index("tm")

    shift = [(b, b - 1) for b in range(1, n_dev)]
    halo = lax.ppermute(records[:halo_rows], ("chan", "tm"), perm=shift)

    taps_matrix = decimation_matrix(fir_taps, out_rows, raw_rows + halo_rows)
    taps_matrix = taps_matrix.astype(jnp.bfloat16)
    main = jnp.dot(taps_matrix[:, :raw_rows], records, preferred_element_type=jnp.float32)
    tail = jnp.dot(taps_matrix[:, raw_rows:], halo, preferred_element_type=jnp.float32)
    decimated = (main + tail).astype(jnp.bfloat16)

    first, second = swap_tm(decimated)
    paired = jnp.concatenate([first, second], axis=0).T

    steps = jnp.arange(source_owner.shape[0], dtype=jnp.int32)
    own_first = jnp.sum(jnp.where(steps == tm, source_owner * block + source_offset, 0))
    source_raw = lax.dynamic_slice_in_dim(channel_map, own_first, SRC)
    half_raw = lax.dynamic_slice(channel_map.reshape(n_chan, block), (0, tm * half), (n_chan, half))
    index = jnp.concatenate(
        [half_raw, jnp.broadcast_to(source_raw[None], (n_chan, SRC))], axis=1
    )
    width = index.shape[1]
    rows = jnp.take(paired, index.reshape(-1), axis=0, mode="clip").reshape(n_chan, width, -1)
    series = lax.all_to_all(rows, "chan", 0, 2, tiled=True).reshape(width, samples)
    table = dft_table(samples, bins, jnp.arange(samples, dtype=jnp.int32))
    lag_share = LAGS // n_tm
    lag = lag_kernel(samples, tm * lag_share, lag_share)

    white = whiten_series(series, table)
    other = lax.ppermute(white, "tm", perm=[(0, 1), (1, 0)])
    result = correlate(white, other, half, lag)
    return result.reshape(STEPS, SRC, block, lag_share)


def solution(mesh):
    return jax.shard_map(
        local,
        mesh=mesh,
        in_specs=(P(("chan", "tm"), "parts"), P(), P("parts"), P("parts"), P("parts")),
        out_specs=P(None, None, ("parts", "chan"), "tm"),
        check_vma=False,
    )
```

```python
import functools
import math

import jax
import jax.numpy as jnp
from jax import lax
from jax.experimental import pallas as pl
from jax.experimental.pallas import tpu as pltpu
from jax.sharding import PartitionSpec as P

SRC = 16
STEPS = 2
LAGS = 512
TAPS = 32
STRIDE = 8
HALF_BAND = 32

two_pi = 2.0 * math.pi
epsilon = 1e-06


def decimation_matrix(fir_taps, out_rows, in_rows):
    leads = TAPS // STRIDE
    rows = jnp.arange(out_rows, dtype=jnp.int32)[:, None, None, None]
    groups = jnp.arange(in_rows // STRIDE, dtype=jnp.int32)[None, :, None, None]
    lead = jnp.arange(leads, dtype=jnp.int32)[None, None, :, None]
    taps = fir_taps.reshape(1, 1, leads, STRIDE)
    matrix = jnp.where(groups - rows == lead, taps, 0.0).sum(axis=2)
    return matrix.reshape(out_rows, in_rows)


def dft_table(samples, bins, time_index):
    inner = 32
    outer = samples // inner
    frequency = jnp.arange(bins, dtype=jnp.int32)[None, :]
    low = jnp.arange(inner, dtype=jnp.int32)[:, None]
    high = time_index.reshape(outer, inner)[:, :1]
    scale = two_pi / samples
    low_angle = ((low * frequency) % samples).astype(jnp.float32) * scale
    high_angle = ((high * frequency) % samples).astype(jnp.float32) * scale
    cl, sl = jnp.cos(low_angle)[None], jnp.sin(low_angle)[None]
    ch, sh = jnp.cos(high_angle)[:, None], jnp.sin(high_angle)[:, None]
    cosine = (ch * cl - sh * sl).reshape(samples, bins)
    sine = (sh * cl + ch * sl).reshape(samples, bins)
    return jnp.concatenate([cosine, -sine], axis=1)


def band_matrix(bins):
    g = jnp.arange(bins, dtype=jnp.int32)
    near = jnp.abs(g[:, None] - g[None, :]) <= HALF_BAND
    return near.astype(jnp.bfloat16)


def lag_pieces(samples, first_lag, lag_count):
    bin_count = samples // 2
    inner = 32
    shifts = first_lag - LAGS // 2 + jnp.arange(lag_count, dtype=jnp.int32)[None, :]
    high = jnp.arange(bin_count // inner, dtype=jnp.int32)[:, None] * inner
    low = jnp.arange(inner, dtype=jnp.int32)[:, None]
    scale = two_pi / samples
    high_angle = jnp.mod(high * shifts, samples).astype(jnp.float32) * scale
    low_angle = jnp.mod(low * shifts, samples).astype(jnp.float32) * scale
    return jnp.cos(high_angle), jnp.sin(high_angle), jnp.cos(low_angle), jnp.sin(low_angle)


def whiten_series(series, table):
    samples = series.shape[1]
    bins = samples // 2
    spectrum = jnp.dot(series, table.astype(jnp.bfloat16), preferred_element_type=jnp.float32)
    real_part = spectrum[:, :bins]
    imag_part = spectrum[:, bins:]
    powers = real_part * real_part + imag_part * imag_part
    window = jnp.dot(powers.astype(jnp.bfloat16), band_matrix(bins), preferred_element_type=jnp.float32)
    window_span = 2 * HALF_BAND + 1
    factor = 1.0 / jnp.sqrt(window / window_span + epsilon)
    return jnp.concatenate([real_part * factor, imag_part * factor], axis=1).astype(jnp.bfloat16)


def correlate_kernel(
    factor, bins, group, half, mine_ref, other_ref, ch_ref, sh_ref, cl_ref, sl_ref, out_ref, lag_ref
):
    step = pl.program_id(0)
    first = lax.axis_index("tm") == 0

    @pl.when(step == 0)
    def _():
        inner = cl_ref.shape[0]
        cl = cl_ref[...]
        sl = sl_ref[...]
        for h in range(bins // inner):
            ch = ch_ref[h : h + 1, :]
            sh = sh_ref[h : h + 1, :]
            lag_ref[h * inner : (h + 1) * inner, :] = (ch * cl - sh * sl).astype(jnp.bfloat16)
            lag_ref[bins + h * inner : bins + (h + 1) * inner, :] = (-(sh * cl + ch * sl)).astype(
                jnp.bfloat16
            )

    lag = lag_ref[...]
    receivers = [mine_ref[:half, :].astype(jnp.float32), other_ref[:half, :].astype(jnp.float32)]
    places = [jnp.where(first, 0, half), jnp.where(first, half, 0)]
    mine_src = mine_ref[half:, :]
    other_src = other_ref[half:, :]
    every = jnp.where(
        first,
        jnp.concatenate([mine_src, other_src], axis=0),
        jnp.concatenate([other_src, mine_src], axis=0),
    ).astype(jnp.float32)
    picked = every[:group]
    for g in range(1, every.shape[0] // group):
        picked = jnp.where(step == g, every[g * group : (g + 1) * group], picked)
    for k in range(group):
        row = picked[k : k + 1]
        real_src = row[:, :bins]
        imag_src = row[:, bins:]
        for part, rcv in enumerate(receivers):
            real_rcv = rcv[:, :bins]
            imag_rcv = rcv[:, bins:]
            cross = jnp.concatenate(
                [real_src * real_rcv + imag_src * imag_rcv, imag_src * real_rcv - real_src * imag_rcv],
                axis=1,
            ).astype(jnp.bfloat16)
            out_ref[k, pl.ds(pl.multiple_of(places[part], 8), half), :] = (
                jnp.dot(cross, lag, preferred_element_type=jnp.float32) * factor
            )


def correlate(low, high, half, pieces):
    rows, width = low.shape
    bins = width // 2
    count = 2 * (rows - half)
    block = 2 * half
    lags = pieces[0].shape[1]
    group = 8
    factor = 1.0 / math.sqrt(bins)
    flops = 2 * count * block * width * lags + 6 * count * block * bins
    moved = 4 * rows * width + 4 * lags * (bins // 16 + 64) + 4 * count * block * lags
    return pl.pallas_call(
        functools.partial(correlate_kernel, factor, bins, group, half),
        out_shape=jax.ShapeDtypeStruct((count, block, lags), jnp.float32),
        grid=(count // group,),
        in_specs=[
            pl.BlockSpec((rows, width), lambda s: (0, 0)),
            pl.BlockSpec((rows, width), lambda s: (0, 0)),
        ]
        + [pl.BlockSpec(piece.shape, lambda s: (0, 0)) for piece in pieces],
        out_specs=pl.BlockSpec((group, block, lags), lambda s: (s, 0, 0)),
        scratch_shapes=[pltpu.VMEM((width, lags), jnp.bfloat16)],
        compiler_params=pltpu.CompilerParams(dimension_semantics=("arbitrary",)),
        cost_estimate=pl.CostEstimate(flops=flops, bytes_accessed=moved, transcendentals=0),
    )(low, high, *pieces)


def swap_tm(x):
    other = lax.ppermute(x, "tm", perm=[(0, 1), (1, 0)])
    first = lax.axis_index("tm") == 0
    return jnp.where(first, x, other), jnp.where(first, other, x)


def local(records, fir_taps, channel_map, source_owner, source_offset):
    n_chan = lax.axis_size("chan")
    n_tm = lax.axis_size("tm")
    assert n_tm == 2
    n_dev = n_chan * n_tm
    raw_rows, channels = records.shape
    block = channels // n_chan
    half = block // n_tm
    out_rows = raw_rows // STRIDE
    halo_rows = TAPS - STRIDE
    samples = out_rows * n_dev
    bins = samples // 2
    tm = lax.axis_index("tm")

    shift = [(b, b - 1) for b in range(1, n_dev)]
    halo = lax.ppermute(records[:halo_rows], ("chan", "tm"), perm=shift)

    taps_matrix = decimation_matrix(fir_taps, out_rows, raw_rows + halo_rows)
    taps_matrix = taps_matrix.astype(jnp.bfloat16)
    main = jnp.dot(taps_matrix[:, :raw_rows], records, preferred_element_type=jnp.float32)
    tail = jnp.dot(taps_matrix[:, raw_rows:], halo, preferred_element_type=jnp.float32)
    decimated = (main + tail).astype(jnp.bfloat16)

    first, second = swap_tm(decimated)
    paired = jnp.concatenate([first, second], axis=0).T

    steps = jnp.arange(source_owner.shape[0], dtype=jnp.int32)
    own_first = jnp.sum(jnp.where(steps == tm, source_owner * block + source_offset, 0))
    source_raw = lax.dynamic_slice_in_dim(channel_map, own_first, SRC)
    half_raw = lax.dynamic_slice(channel_map.reshape(n_chan, block), (0, tm * half), (n_chan, half))
    index = jnp.concatenate(
        [half_raw, jnp.broadcast_to(source_raw[None], (n_chan, SRC))], axis=1
    )
    width = index.shape[1]
    rows = jnp.take(paired, index.reshape(-1), axis=0, mode="clip").reshape(n_chan, width, -1)
    series = lax.all_to_all(rows, "chan", 0, 2, tiled=True).reshape(width, samples)
    table = dft_table(samples, bins, jnp.arange(samples, dtype=jnp.int32))
    lag_share = LAGS // n_tm
    pieces = lag_pieces(samples, tm * lag_share, lag_share)

    white = whiten_series(series, table)
    other = lax.ppermute(white, "tm", perm=[(0, 1), (1, 0)])
    result = correlate(white, other, half, pieces)
    return result.reshape(STEPS, SRC, block, lag_share)


def solution(mesh):
    return jax.shard_map(
        local,
        mesh=mesh,
        in_specs=(P(("chan", "tm"), "parts"), P(), P("parts"), P("parts"), P("parts")),
        out_specs=P(None, None, ("parts", "chan"), "tm"),
        check_vma=False,
    )
```

```python
import functools
import math

import jax
import jax.numpy as jnp
from jax import lax
from jax.experimental import pallas as pl
from jax.experimental.pallas import tpu as pltpu
from jax.sharding import PartitionSpec as P

SRC = 16
STEPS = 2
LAGS = 512
TAPS = 32
STRIDE = 8
HALF_BAND = 32

two_pi = 2.0 * math.pi
epsilon = 1e-06


def decimation_matrix(fir_taps, out_rows, in_rows):
    leads = TAPS // STRIDE
    rows = jnp.arange(out_rows, dtype=jnp.int32)[:, None, None, None]
    groups = jnp.arange(in_rows // STRIDE, dtype=jnp.int32)[None, :, None, None]
    lead = jnp.arange(leads, dtype=jnp.int32)[None, None, :, None]
    taps = fir_taps.reshape(1, 1, leads, STRIDE)
    matrix = jnp.where(groups - rows == lead, taps, 0.0).sum(axis=2)
    return matrix.reshape(out_rows, in_rows)


def dft_table(samples, bins, time_index):
    inner = 32
    outer = samples // inner
    frequency = jnp.arange(bins, dtype=jnp.int32)[None, :]
    low = jnp.arange(inner, dtype=jnp.int32)[:, None]
    high = time_index.reshape(outer, inner)[:, :1]
    scale = two_pi / samples
    low_angle = ((low * frequency) % samples).astype(jnp.float32) * scale
    high_angle = ((high * frequency) % samples).astype(jnp.float32) * scale
    cl, sl = jnp.cos(low_angle)[None], jnp.sin(low_angle)[None]
    ch, sh = jnp.cos(high_angle)[:, None], jnp.sin(high_angle)[:, None]
    cosine = (ch * cl - sh * sl).reshape(samples, bins)
    sine = (sh * cl + ch * sl).reshape(samples, bins)
    return jnp.concatenate([cosine, -sine], axis=1)


def band_matrix(bins):
    g = jnp.arange(bins, dtype=jnp.int32)
    near = jnp.abs(g[:, None] - g[None, :]) <= HALF_BAND
    return near.astype(jnp.bfloat16)


def lag_pieces(samples, first_lag, lag_count):
    bin_count = samples // 2
    inner = 32
    shifts = first_lag - LAGS // 2 + jnp.arange(lag_count, dtype=jnp.int32)[None, :]
    high = jnp.arange(bin_count // inner, dtype=jnp.int32)[:, None] * inner
    low = jnp.arange(inner, dtype=jnp.int32)[:, None]
    scale = two_pi / samples
    high_angle = jnp.mod(high * shifts, samples).astype(jnp.float32) * scale
    low_angle = jnp.mod(low * shifts, samples).astype(jnp.float32) * scale
    return jnp.cos(high_angle), jnp.sin(high_angle), jnp.cos(low_angle), jnp.sin(low_angle)


def whiten_series(series, table, band):
    samples = series.shape[1]
    bins = samples // 2
    spectrum = jnp.dot(series, table.astype(jnp.bfloat16), preferred_element_type=jnp.float32)
    real_part = spectrum[:, :bins]
    imag_part = spectrum[:, bins:]
    powers = real_part * real_part + imag_part * imag_part
    window = jnp.dot(powers.astype(jnp.bfloat16), band, preferred_element_type=jnp.float32)
    window_span = 2 * HALF_BAND + 1
    factor = 1.0 / jnp.sqrt(window / window_span + epsilon)
    return jnp.concatenate([real_part * factor, imag_part * factor], axis=1).astype(jnp.bfloat16)


def correlate_kernel(
    factor, bins, group, half, mine_ref, other_ref, ch_ref, sh_ref, cl_ref, sl_ref, out_ref, lag_ref
):
    step = pl.program_id(0)
    first = lax.axis_index("tm") == 0

    @pl.when(step == 0)
    def _():
        inner = cl_ref.shape[0]
        cl = cl_ref[...]
        sl = sl_ref[...]
        for h in range(bins // inner):
            ch = ch_ref[h : h + 1, :]
            sh = sh_ref[h : h + 1, :]
            lag_ref[h * inner : (h + 1) * inner, :] = (ch * cl - sh * sl).astype(jnp.bfloat16)
            lag_ref[bins + h * inner : bins + (h + 1) * inner, :] = (-(sh * cl + ch * sl)).astype(
                jnp.bfloat16
            )

    lag = lag_ref[...]
    receivers = [mine_ref[:half, :].astype(jnp.float32), other_ref[:half, :].astype(jnp.float32)]
    places = [jnp.where(first, 0, half), jnp.where(first, half, 0)]
    mine_src = mine_ref[half:, :]
    other_src = other_ref[half:, :]
    every = jnp.where(
        first,
        jnp.concatenate([mine_src, other_src], axis=0),
        jnp.concatenate([other_src, mine_src], axis=0),
    ).astype(jnp.float32)
    picked = every[:group]
    for g in range(1, every.shape[0] // group):
        picked = jnp.where(step == g, every[g * group : (g + 1) * group], picked)
    for k in range(group):
        row = picked[k : k + 1]
        real_src = row[:, :bins]
        imag_src = row[:, bins:]
        for part, rcv in enumerate(receivers):
            real_rcv = rcv[:, :bins]
            imag_rcv = rcv[:, bins:]
            cross = jnp.concatenate(
                [real_src * real_rcv + imag_src * imag_rcv, imag_src * real_rcv - real_src * imag_rcv],
                axis=1,
            ).astype(jnp.bfloat16)
            out_ref[k, pl.ds(pl.multiple_of(places[part], 8), half), :] = (
                jnp.dot(cross, lag, preferred_element_type=jnp.float32) * factor
            )


def correlate(low, high, half, pieces):
    rows, width = low.shape
    bins = width // 2
    count = 2 * (rows - half)
    block = 2 * half
    lags = pieces[0].shape[1]
    group = 8
    factor = 1.0 / math.sqrt(bins)
    flops = 2 * count * block * width * lags + 6 * count * block * bins
    moved = 4 * rows * width + 4 * lags * (bins // 16 + 64) + 4 * count * block * lags
    return pl.pallas_call(
        functools.partial(correlate_kernel, factor, bins, group, half),
        out_shape=jax.ShapeDtypeStruct((count, block, lags), jnp.float32),
        grid=(count // group,),
        in_specs=[
            pl.BlockSpec((rows, width), lambda s: (0, 0)),
            pl.BlockSpec((rows, width), lambda s: (0, 0)),
        ]
        + [pl.BlockSpec(piece.shape, lambda s: (0, 0)) for piece in pieces],
        out_specs=pl.BlockSpec((group, block, lags), lambda s: (s, 0, 0)),
        scratch_shapes=[pltpu.VMEM((width, lags), jnp.bfloat16)],
        compiler_params=pltpu.CompilerParams(dimension_semantics=("arbitrary",)),
        cost_estimate=pl.CostEstimate(flops=flops, bytes_accessed=moved, transcendentals=0),
    )(low, high, *pieces)


def swap_tm(x):
    other = lax.ppermute(x, "tm", perm=[(0, 1), (1, 0)])
    first = lax.axis_index("tm") == 0
    return jnp.where(first, x, other), jnp.where(first, other, x)


def local(records, fir_taps, channel_map, source_owner, source_offset):
    n_chan = lax.axis_size("chan")
    n_tm = lax.axis_size("tm")
    assert n_tm == 2
    n_dev = n_chan * n_tm
    raw_rows, channels = records.shape
    block = channels // n_chan
    half = block // n_tm
    out_rows = raw_rows // STRIDE
    halo_rows = TAPS - STRIDE
    samples = out_rows * n_dev
    bins = samples // 2
    tm = lax.axis_index("tm")

    shift = [(b, b - 1) for b in range(1, n_dev)]
    halo = lax.ppermute(records[:halo_rows], ("chan", "tm"), perm=shift)

    taps_matrix = decimation_matrix(fir_taps, out_rows, raw_rows + halo_rows)
    taps_matrix = taps_matrix.astype(jnp.bfloat16)
    main = jnp.dot(taps_matrix[:, :raw_rows], records, preferred_element_type=jnp.float32)
    tail = jnp.dot(taps_matrix[:, raw_rows:], halo, preferred_element_type=jnp.float32)
    decimated = (main + tail).astype(jnp.bfloat16)

    first, second = swap_tm(decimated)
    paired = jnp.concatenate([first, second], axis=0).T

    steps = jnp.arange(source_owner.shape[0], dtype=jnp.int32)
    own_first = jnp.sum(jnp.where(steps == tm, source_owner * block + source_offset, 0))
    source_raw = lax.dynamic_slice_in_dim(channel_map, own_first, SRC)
    half_raw = lax.dynamic_slice(channel_map.reshape(n_chan, block), (0, tm * half), (n_chan, half))
    index = jnp.concatenate(
        [half_raw, jnp.broadcast_to(source_raw[None], (n_chan, SRC))], axis=1
    )
    width = index.shape[1]
    rows = jnp.take(paired, index.reshape(-1), axis=0, mode="clip").reshape(n_chan, width, -1)
    series = lax.all_to_all(rows, "chan", 0, 2, tiled=True).reshape(width, samples)
    table = dft_table(samples, bins, jnp.arange(samples, dtype=jnp.int32))
    lag_share = LAGS // n_tm
    pieces = lag_pieces(samples, tm * lag_share, lag_share)

    series, table, band, pieces = lax.optimization_barrier(
        (series, table, band_matrix(bins), pieces)
    )
    white = whiten_series(series, table, band)
    other = lax.ppermute(white, "tm", perm=[(0, 1), (1, 0)])
    result = correlate(white, other, half, pieces)
    return result.reshape(STEPS, SRC, block, lag_share)


def solution(mesh):
    return jax.shard_map(
        local,
        mesh=mesh,
        in_specs=(P(("chan", "tm"), "parts"), P(), P("parts"), P("parts"), P("parts")),
        out_specs=P(None, None, ("parts", "chan"), "tm"),
        check_vma=False,
    )
```

```python
import functools
import math

import jax
import jax.numpy as jnp
from jax import lax
from jax.experimental import pallas as pl
from jax.experimental.pallas import tpu as pltpu
from jax.sharding import PartitionSpec as P

SRC = 16
STEPS = 2
LAGS = 512
TAPS = 32
STRIDE = 8
HALF_BAND = 32

two_pi = 2.0 * math.pi
epsilon = 1e-06


def decimation_matrix(fir_taps, out_rows, in_rows):
    leads = TAPS // STRIDE
    rows = jnp.arange(out_rows, dtype=jnp.int32)[:, None, None, None]
    groups = jnp.arange(in_rows // STRIDE, dtype=jnp.int32)[None, :, None, None]
    lead = jnp.arange(leads, dtype=jnp.int32)[None, None, :, None]
    taps = fir_taps.reshape(1, 1, leads, STRIDE)
    matrix = jnp.where(groups - rows == lead, taps, 0.0).sum(axis=2)
    return matrix.reshape(out_rows, in_rows)


def dft_table(samples, bins, time_index):
    inner = 32
    outer = samples // inner
    frequency = jnp.arange(bins, dtype=jnp.int32)[None, :]
    low = jnp.arange(inner, dtype=jnp.int32)[:, None]
    high = time_index.reshape(outer, inner)[:, :1]
    scale = two_pi / samples
    low_angle = ((low * frequency) % samples).astype(jnp.float32) * scale
    high_angle = ((high * frequency) % samples).astype(jnp.float32) * scale
    cl, sl = jnp.cos(low_angle)[None], jnp.sin(low_angle)[None]
    ch, sh = jnp.cos(high_angle)[:, None], jnp.sin(high_angle)[:, None]
    cosine = (ch * cl - sh * sl).reshape(samples, bins)
    sine = (sh * cl + ch * sl).reshape(samples, bins)
    return jnp.concatenate([cosine, -sine], axis=1)


def band_matrix(bins):
    g = jnp.arange(bins, dtype=jnp.int32)
    near = jnp.abs(g[:, None] - g[None, :]) <= HALF_BAND
    return near.astype(jnp.bfloat16)


def lag_kernel(samples, first_lag, lag_count):
    bin_count = samples // 2
    inner = 32
    frequency = jnp.arange(bin_count, dtype=jnp.int32)[:, None]
    low = jnp.arange(inner, dtype=jnp.int32)[None, :]
    high = first_lag - LAGS // 2 + jnp.arange(lag_count // inner, dtype=jnp.int32)[None, :] * inner
    scale = two_pi / samples
    low_angle = jnp.mod(frequency * low, samples).astype(jnp.float32) * scale
    high_angle = jnp.mod(frequency * high, samples).astype(jnp.float32) * scale
    cl, sl = jnp.cos(low_angle)[:, None, :], jnp.sin(low_angle)[:, None, :]
    ch, sh = jnp.cos(high_angle)[:, :, None], jnp.sin(high_angle)[:, :, None]
    cosine = (ch * cl - sh * sl).reshape(bin_count, lag_count)
    sine = (sh * cl + ch * sl).reshape(bin_count, lag_count)
    return jnp.concatenate([cosine, -sine], axis=0).astype(jnp.bfloat16)


def whiten_series(series, table):
    samples = series.shape[1]
    bins = samples // 2
    spectrum = jnp.dot(series, table.astype(jnp.bfloat16), preferred_element_type=jnp.float32)
    real_part = spectrum[:, :bins]
    imag_part = spectrum[:, bins:]
    powers = real_part * real_part + imag_part * imag_part
    window = jnp.dot(powers.astype(jnp.bfloat16), band_matrix(bins), preferred_element_type=jnp.float32)
    window_span = 2 * HALF_BAND + 1
    factor = 1.0 / jnp.sqrt(window / window_span + epsilon)
    return jnp.concatenate([real_part * factor, imag_part * factor], axis=1).astype(jnp.bfloat16)


def correlate_kernel(factor, bins, group, half, mine_ref, other_ref, lag_ref, out_ref):
    step = pl.program_id(0)
    first = lax.axis_index("tm") == 0
    lag = lag_ref[...]
    receivers = [mine_ref[:half, :].astype(jnp.float32), other_ref[:half, :].astype(jnp.float32)]
    places = [jnp.where(first, 0, half), jnp.where(first, half, 0)]
    mine_src = mine_ref[half:, :]
    other_src = other_ref[half:, :]
    every = jnp.where(
        first,
        jnp.concatenate([mine_src, other_src], axis=0),
        jnp.concatenate([other_src, mine_src], axis=0),
    ).astype(jnp.float32)
    picked = every[:group]
    for g in range(1, every.shape[0] // group):
        picked = jnp.where(step == g, every[g * group : (g + 1) * group], picked)
    for k in range(group):
        row = picked[k : k + 1]
        real_src = row[:, :bins]
        imag_src = row[:, bins:]
        for part, rcv in enumerate(receivers):
            real_rcv = rcv[:, :bins]
            imag_rcv = rcv[:, bins:]
            cross = jnp.concatenate(
                [real_src * real_rcv + imag_src * imag_rcv, imag_src * real_rcv - real_src * imag_rcv],
                axis=1,
            ).astype(jnp.bfloat16)
            out_ref[k, pl.ds(pl.multiple_of(places[part], 8), half), :] = (
                jnp.dot(cross, lag, preferred_element_type=jnp.float32) * factor
            )


def correlate(low, high, half, lag):
    rows, width = low.shape
    bins = width // 2
    count = 2 * (rows - half)
    block = 2 * half
    lags = lag.shape[1]
    group = 4
    factor = 1.0 / math.sqrt(bins)
    flops = 2 * count * block * width * lags + 6 * count * block * bins
    moved = 4 * rows * width + 2 * lags * width + 4 * count * block * lags
    return pl.pallas_call(
        functools.partial(correlate_kernel, factor, bins, group, half),
        out_shape=jax.ShapeDtypeStruct((count, block, lags), jnp.float32),
        grid=(count // group,),
        in_specs=[
            pl.BlockSpec((rows, width), lambda s: (0, 0)),
            pl.BlockSpec((rows, width), lambda s: (0, 0)),
            pl.BlockSpec((width, lags), lambda s: (0, 0)),
        ],
        out_specs=pl.BlockSpec((group, block, lags), lambda s: (s, 0, 0)),
        compiler_params=pltpu.CompilerParams(dimension_semantics=("arbitrary",)),
        cost_estimate=pl.CostEstimate(flops=flops, bytes_accessed=moved, transcendentals=0),
    )(low, high, lag)


def swap_tm(x):
    other = lax.ppermute(x, "tm", perm=[(0, 1), (1, 0)])
    first = lax.axis_index("tm") == 0
    return jnp.where(first, x, other), jnp.where(first, other, x)


def local(records, fir_taps, channel_map, source_owner, source_offset):
    n_chan = lax.axis_size("chan")
    n_tm = lax.axis_size("tm")
    assert n_tm == 2
    n_dev = n_chan * n_tm
    raw_rows, channels = records.shape
    block = channels // n_chan
    half = block // n_tm
    out_rows = raw_rows // STRIDE
    halo_rows = TAPS - STRIDE
    samples = out_rows * n_dev
    bins = samples // 2
    tm = lax.axis_index("tm")

    shift = [(b, b - 1) for b in range(1, n_dev)]
    halo = lax.ppermute(records[:halo_rows], ("chan", "tm"), perm=shift)

    taps_matrix = decimation_matrix(fir_taps, out_rows, raw_rows + halo_rows)
    taps_matrix = taps_matrix.astype(jnp.bfloat16)
    main = jnp.dot(taps_matrix[:, :raw_rows], records, preferred_element_type=jnp.float32)
    tail = jnp.dot(taps_matrix[:, raw_rows:], halo, preferred_element_type=jnp.float32)
    decimated = (main + tail).astype(jnp.bfloat16)

    first, second = swap_tm(decimated)
    paired = jnp.concatenate([first, second], axis=0).T

    steps = jnp.arange(source_owner.shape[0], dtype=jnp.int32)
    own_first = jnp.sum(jnp.where(steps == tm, source_owner * block + source_offset, 0))
    source_raw = lax.dynamic_slice_in_dim(channel_map, own_first, SRC)
    half_raw = lax.dynamic_slice(channel_map.reshape(n_chan, block), (0, tm * half), (n_chan, half))
    index = jnp.concatenate(
        [half_raw, jnp.broadcast_to(source_raw[None], (n_chan, SRC))], axis=1
    )
    width = index.shape[1]
    rows = jnp.take(paired, index.reshape(-1), axis=0, mode="clip").reshape(n_chan, width, -1)
    series = lax.all_to_all(rows, "chan", 0, 2, tiled=True).reshape(width, samples)
    table = dft_table(samples, bins, jnp.arange(samples, dtype=jnp.int32))
    lag_share = LAGS // n_tm
    lag = lag_kernel(samples, tm * lag_share, lag_share)

    white = whiten_series(series, table)
    other = lax.ppermute(white, "tm", perm=[(0, 1), (1, 0)])
    result = correlate(white, other, half, lag)
    return result.reshape(STEPS, SRC, block, lag_share)


def solution(mesh):
    return jax.shard_map(
        local,
        mesh=mesh,
        in_specs=(P(("chan", "tm"), "parts"), P(), P("parts"), P("parts"), P("parts")),
        out_specs=P(None, None, ("parts", "chan"), "tm"),
        check_vma=False,
    )
```

```python
import functools
import math

import jax
import jax.numpy as jnp
from jax import lax
from jax.experimental import pallas as pl
from jax.experimental.pallas import tpu as pltpu
from jax.sharding import PartitionSpec as P

SRC = 16
STEPS = 2
LAGS = 512
TAPS = 32
STRIDE = 8
HALF_BAND = 32

two_pi = 2.0 * math.pi
epsilon = 1e-06


def decimation_matrix(fir_taps, out_rows, in_rows):
    leads = TAPS // STRIDE
    rows = jnp.arange(out_rows, dtype=jnp.int32)[:, None, None, None]
    groups = jnp.arange(in_rows // STRIDE, dtype=jnp.int32)[None, :, None, None]
    lead = jnp.arange(leads, dtype=jnp.int32)[None, None, :, None]
    taps = fir_taps.reshape(1, 1, leads, STRIDE)
    matrix = jnp.where(groups - rows == lead, taps, 0.0).sum(axis=2)
    return matrix.reshape(out_rows, in_rows)


def dft_table(samples, bins, time_index):
    inner = 32
    outer = samples // inner
    frequency = jnp.arange(bins, dtype=jnp.int32)[None, :]
    low = jnp.arange(inner, dtype=jnp.int32)[:, None]
    high = time_index.reshape(outer, inner)[:, :1]
    scale = two_pi / samples
    low_angle = ((low * frequency) % samples).astype(jnp.float32) * scale
    high_angle = ((high * frequency) % samples).astype(jnp.float32) * scale
    cl, sl = jnp.cos(low_angle)[None], jnp.sin(low_angle)[None]
    ch, sh = jnp.cos(high_angle)[:, None], jnp.sin(high_angle)[:, None]
    cosine = (ch * cl - sh * sl).reshape(samples, bins)
    sine = (sh * cl + ch * sl).reshape(samples, bins)
    return jnp.concatenate([cosine, -sine], axis=1)


def band_matrix(bins):
    g = jnp.arange(bins, dtype=jnp.int32)
    near = jnp.abs(g[:, None] - g[None, :]) <= HALF_BAND
    return near.astype(jnp.bfloat16)


def lag_kernel(samples, first_lag, lag_count):
    bin_count = samples // 2
    inner = 32
    frequency = jnp.arange(bin_count, dtype=jnp.int32)[:, None]
    low = jnp.arange(inner, dtype=jnp.int32)[None, :]
    high = first_lag - LAGS // 2 + jnp.arange(lag_count // inner, dtype=jnp.int32)[None, :] * inner
    scale = two_pi / samples
    low_angle = jnp.mod(frequency * low, samples).astype(jnp.float32) * scale
    high_angle = jnp.mod(frequency * high, samples).astype(jnp.float32) * scale
    cl, sl = jnp.cos(low_angle)[:, None, :], jnp.sin(low_angle)[:, None, :]
    ch, sh = jnp.cos(high_angle)[:, :, None], jnp.sin(high_angle)[:, :, None]
    cosine = (ch * cl - sh * sl).reshape(bin_count, lag_count)
    sine = (sh * cl + ch * sl).reshape(bin_count, lag_count)
    return jnp.concatenate([cosine, -sine], axis=0).astype(jnp.bfloat16)


def whiten_series(series, table):
    samples = series.shape[1]
    bins = samples // 2
    spectrum = jnp.dot(series, table.astype(jnp.bfloat16), preferred_element_type=jnp.float32)
    real_part = spectrum[:, :bins]
    imag_part = spectrum[:, bins:]
    powers = real_part * real_part + imag_part * imag_part
    window = jnp.dot(powers.astype(jnp.bfloat16), band_matrix(bins), preferred_element_type=jnp.float32)
    window_span = 2 * HALF_BAND + 1
    factor = 1.0 / jnp.sqrt(window / window_span + epsilon)
    return jnp.concatenate([real_part * factor, imag_part * factor], axis=1).astype(jnp.bfloat16)


def correlate_kernel(factor, bins, group, half, mine_ref, other_ref, lag_ref, out_ref):
    step = pl.program_id(0)
    first = lax.axis_index("tm") == 0
    lag = lag_ref[...]
    receivers = [mine_ref[:half, :].astype(jnp.float32), other_ref[:half, :].astype(jnp.float32)]
    places = [jnp.where(first, 0, half), jnp.where(first, half, 0)]
    mine_src = mine_ref[half:, :]
    other_src = other_ref[half:, :]
    every = jnp.where(
        first,
        jnp.concatenate([mine_src, other_src], axis=0),
        jnp.concatenate([other_src, mine_src], axis=0),
    ).astype(jnp.float32)
    picked = every[:group]
    for g in range(1, every.shape[0] // group):
        picked = jnp.where(step == g, every[g * group : (g + 1) * group], picked)
    for k in range(group):
        row = picked[k : k + 1]
        real_src = row[:, :bins]
        imag_src = row[:, bins:]
        for part, rcv in enumerate(receivers):
            real_rcv = rcv[:, :bins]
            imag_rcv = rcv[:, bins:]
            cross = jnp.concatenate(
                [real_src * real_rcv + imag_src * imag_rcv, imag_src * real_rcv - real_src * imag_rcv],
                axis=1,
            ).astype(jnp.bfloat16)
            out_ref[k, pl.ds(pl.multiple_of(places[part], 8), half), :] = (
                jnp.dot(cross, lag, preferred_element_type=jnp.float32) * factor
            )


def correlate(low, high, half, lag):
    rows, width = low.shape
    bins = width // 2
    count = 2 * (rows - half)
    block = 2 * half
    lags = lag.shape[1]
    group = 16
    factor = 1.0 / math.sqrt(bins)
    flops = 2 * count * block * width * lags + 6 * count * block * bins
    moved = 4 * rows * width + 2 * lags * width + 4 * count * block * lags
    return pl.pallas_call(
        functools.partial(correlate_kernel, factor, bins, group, half),
        out_shape=jax.ShapeDtypeStruct((count, block, lags), jnp.float32),
        grid=(count // group,),
        in_specs=[
            pl.BlockSpec((rows, width), lambda s: (0, 0)),
            pl.BlockSpec((rows, width), lambda s: (0, 0)),
            pl.BlockSpec((width, lags), lambda s: (0, 0)),
        ],
        out_specs=pl.BlockSpec((group, block, lags), lambda s: (s, 0, 0)),
        compiler_params=pltpu.CompilerParams(dimension_semantics=("arbitrary",)),
        cost_estimate=pl.CostEstimate(flops=flops, bytes_accessed=moved, transcendentals=0),
    )(low, high, lag)


def swap_tm(x):
    other = lax.ppermute(x, "tm", perm=[(0, 1), (1, 0)])
    first = lax.axis_index("tm") == 0
    return jnp.where(first, x, other), jnp.where(first, other, x)


def local(records, fir_taps, channel_map, source_owner, source_offset):
    n_chan = lax.axis_size("chan")
    n_tm = lax.axis_size("tm")
    assert n_tm == 2
    n_dev = n_chan * n_tm
    raw_rows, channels = records.shape
    block = channels // n_chan
    half = block // n_tm
    out_rows = raw_rows // STRIDE
    halo_rows = TAPS - STRIDE
    samples = out_rows * n_dev
    bins = samples // 2
    tm = lax.axis_index("tm")

    shift = [(b, b - 1) for b in range(1, n_dev)]
    halo = lax.ppermute(records[:halo_rows], ("chan", "tm"), perm=shift)

    taps_matrix = decimation_matrix(fir_taps, out_rows, raw_rows + halo_rows)
    taps_matrix = taps_matrix.astype(jnp.bfloat16)
    main = jnp.dot(taps_matrix[:, :raw_rows], records, preferred_element_type=jnp.float32)
    tail = jnp.dot(taps_matrix[:, raw_rows:], halo, preferred_element_type=jnp.float32)
    decimated = (main + tail).astype(jnp.bfloat16)

    first, second = swap_tm(decimated)
    paired = jnp.concatenate([first, second], axis=0).T

    steps = jnp.arange(source_owner.shape[0], dtype=jnp.int32)
    own_first = jnp.sum(jnp.where(steps == tm, source_owner * block + source_offset, 0))
    source_raw = lax.dynamic_slice_in_dim(channel_map, own_first, SRC)
    half_raw = lax.dynamic_slice(channel_map.reshape(n_chan, block), (0, tm * half), (n_chan, half))
    index = jnp.concatenate(
        [half_raw, jnp.broadcast_to(source_raw[None], (n_chan, SRC))], axis=1
    )
    width = index.shape[1]
    rows = jnp.take(paired, index.reshape(-1), axis=0, mode="clip").reshape(n_chan, width, -1)
    series = lax.all_to_all(rows, "chan", 0, 2, tiled=True).reshape(width, samples)
    table = dft_table(samples, bins, jnp.arange(samples, dtype=jnp.int32))
    lag_share = LAGS // n_tm
    lag = lag_kernel(samples, tm * lag_share, lag_share)

    white = whiten_series(series, table)
    other = lax.ppermute(white, "tm", perm=[(0, 1), (1, 0)])
    result = correlate(white, other, half, lag)
    return result.reshape(STEPS, SRC, block, lag_share)


def solution(mesh):
    return jax.shard_map(
        local,
        mesh=mesh,
        in_specs=(P(("chan", "tm"), "parts"), P(), P("parts"), P("parts"), P("parts")),
        out_specs=P(None, None, ("parts", "chan"), "tm"),
        check_vma=False,
    )
```

```python
import functools
import math

import jax
import jax.numpy as jnp
from jax import lax
from jax.experimental import pallas as pl
from jax.experimental.pallas import tpu as pltpu
from jax.sharding import PartitionSpec as P

SRC = 16
STEPS = 2
LAGS = 512
TAPS = 32
STRIDE = 8
HALF_BAND = 32

two_pi = 2.0 * math.pi
epsilon = 1e-06


def decimation_matrix(fir_taps, out_rows, in_rows):
    leads = TAPS // STRIDE
    rows = jnp.arange(out_rows, dtype=jnp.int32)[:, None, None, None]
    groups = jnp.arange(in_rows // STRIDE, dtype=jnp.int32)[None, :, None, None]
    lead = jnp.arange(leads, dtype=jnp.int32)[None, None, :, None]
    taps = fir_taps.reshape(1, 1, leads, STRIDE)
    matrix = jnp.where(groups - rows == lead, taps, 0.0).sum(axis=2)
    return matrix.reshape(out_rows, in_rows)


def dft_table(samples, bins, time_index):
    inner = 32
    outer = samples // inner
    frequency = jnp.arange(bins, dtype=jnp.int32)[None, :]
    low = jnp.arange(inner, dtype=jnp.int32)[:, None]
    high = time_index.reshape(outer, inner)[:, :1]
    scale = two_pi / samples
    low_angle = ((low * frequency) % samples).astype(jnp.float32) * scale
    high_angle = ((high * frequency) % samples).astype(jnp.float32) * scale
    cl, sl = jnp.cos(low_angle)[None], jnp.sin(low_angle)[None]
    ch, sh = jnp.cos(high_angle)[:, None], jnp.sin(high_angle)[:, None]
    cosine = (ch * cl - sh * sl).reshape(samples, bins)
    sine = (sh * cl + ch * sl).reshape(samples, bins)
    return jnp.concatenate([cosine, -sine], axis=1)


def band_matrix(bins):
    g = jnp.arange(bins, dtype=jnp.int32)
    near = jnp.abs(g[:, None] - g[None, :]) <= HALF_BAND
    return near.astype(jnp.bfloat16)


def lag_kernel(samples, first_lag, lag_count):
    bin_count = samples // 2
    inner = 32
    frequency = jnp.arange(bin_count, dtype=jnp.int32)[:, None]
    low = jnp.arange(inner, dtype=jnp.int32)[None, :]
    high = first_lag - LAGS // 2 + jnp.arange(lag_count // inner, dtype=jnp.int32)[None, :] * inner
    scale = two_pi / samples
    low_angle = jnp.mod(frequency * low, samples).astype(jnp.float32) * scale
    high_angle = jnp.mod(frequency * high, samples).astype(jnp.float32) * scale
    cl, sl = jnp.cos(low_angle)[:, None, :], jnp.sin(low_angle)[:, None, :]
    ch, sh = jnp.cos(high_angle)[:, :, None], jnp.sin(high_angle)[:, :, None]
    cosine = (ch * cl - sh * sl).reshape(bin_count, lag_count)
    sine = (sh * cl + ch * sl).reshape(bin_count, lag_count)
    return jnp.concatenate([cosine, -sine], axis=0).astype(jnp.bfloat16)


def whiten_series(series, table):
    samples = series.shape[1]
    bins = samples // 2
    spectrum = jnp.dot(series, table.astype(jnp.bfloat16), preferred_element_type=jnp.float32)
    real_part = spectrum[:, :bins]
    imag_part = spectrum[:, bins:]
    powers = real_part * real_part + imag_part * imag_part
    window = jnp.dot(powers.astype(jnp.bfloat16), band_matrix(bins), preferred_element_type=jnp.float32)
    window_span = 2 * HALF_BAND + 1
    factor = 1.0 / jnp.sqrt(window / window_span + epsilon)
    return jnp.concatenate([real_part * factor, imag_part * factor], axis=1).astype(jnp.bfloat16)


def correlate_kernel(factor, bins, group, half, mine_ref, other_ref, lag_ref, out_ref, buf, sems):
    step = pl.program_id(0)
    last = pl.num_programs(0) - 1

    def copy(slot, index):
        return pltpu.make_async_copy(buf.at[slot], out_ref.at[index], sems.at[slot])

    first = lax.axis_index("tm") == 0
    lag = lag_ref[...]
    receivers = [mine_ref[:half, :].astype(jnp.float32), other_ref[:half, :].astype(jnp.float32)]
    places = [jnp.where(first, 0, half), jnp.where(first, half, 0)]
    mine_src = mine_ref[half:, :]
    other_src = other_ref[half:, :]
    every = jnp.where(
        first,
        jnp.concatenate([mine_src, other_src], axis=0),
        jnp.concatenate([other_src, mine_src], axis=0),
    ).astype(jnp.float32)
    picked = every[:group]
    for g in range(1, every.shape[0] // group):
        picked = jnp.where(step == g, every[g * group : (g + 1) * group], picked)
    for k in range(group):
        slot = k % 2
        if k >= 2:
            copy(slot, 0).wait()
        else:

            @pl.when(step > 0)
            def _():
                copy(slot, 0).wait()

        row = picked[k : k + 1]
        real_src = row[:, :bins]
        imag_src = row[:, bins:]
        for part, rcv in enumerate(receivers):
            real_rcv = rcv[:, :bins]
            imag_rcv = rcv[:, bins:]
            cross = jnp.concatenate(
                [real_src * real_rcv + imag_src * imag_rcv, imag_src * real_rcv - real_src * imag_rcv],
                axis=1,
            ).astype(jnp.bfloat16)
            buf[slot, pl.ds(pl.multiple_of(places[part], 8), half), :] = (
                jnp.dot(cross, lag, preferred_element_type=jnp.float32) * factor
            )
        copy(slot, step * group + k).start()

    @pl.when(step == last)
    def _():
        for slot in range(2):
            copy(slot, 0).wait()


def correlate(low, high, half, lag):
    rows, width = low.shape
    bins = width // 2
    count = 2 * (rows - half)
    block = 2 * half
    lags = lag.shape[1]
    group = 8
    factor = 1.0 / math.sqrt(bins)
    flops = 2 * count * block * width * lags + 6 * count * block * bins
    moved = 4 * rows * width + 2 * lags * width + 4 * count * block * lags
    return pl.pallas_call(
        functools.partial(correlate_kernel, factor, bins, group, half),
        out_shape=jax.ShapeDtypeStruct((count, block, lags), jnp.float32),
        grid=(count // group,),
        in_specs=[
            pl.BlockSpec((rows, width), lambda s: (0, 0)),
            pl.BlockSpec((rows, width), lambda s: (0, 0)),
            pl.BlockSpec((width, lags), lambda s: (0, 0)),
        ],
        out_specs=pl.BlockSpec(memory_space=pl.ANY),
        scratch_shapes=[pltpu.VMEM((2, block, lags), jnp.float32), pltpu.SemaphoreType.DMA((2,))],
        compiler_params=pltpu.CompilerParams(dimension_semantics=("arbitrary",)),
        cost_estimate=pl.CostEstimate(flops=flops, bytes_accessed=moved, transcendentals=0),
    )(low, high, lag)


def swap_tm(x):
    other = lax.ppermute(x, "tm", perm=[(0, 1), (1, 0)])
    first = lax.axis_index("tm") == 0
    return jnp.where(first, x, other), jnp.where(first, other, x)


def local(records, fir_taps, channel_map, source_owner, source_offset):
    n_chan = lax.axis_size("chan")
    n_tm = lax.axis_size("tm")
    assert n_tm == 2
    n_dev = n_chan * n_tm
    raw_rows, channels = records.shape
    block = channels // n_chan
    half = block // n_tm
    out_rows = raw_rows // STRIDE
    halo_rows = TAPS - STRIDE
    samples = out_rows * n_dev
    bins = samples // 2
    tm = lax.axis_index("tm")

    shift = [(b, b - 1) for b in range(1, n_dev)]
    halo = lax.ppermute(records[:halo_rows], ("chan", "tm"), perm=shift)

    taps_matrix = decimation_matrix(fir_taps, out_rows, raw_rows + halo_rows)
    taps_matrix = taps_matrix.astype(jnp.bfloat16)
    main = jnp.dot(taps_matrix[:, :raw_rows], records, preferred_element_type=jnp.float32)
    tail = jnp.dot(taps_matrix[:, raw_rows:], halo, preferred_element_type=jnp.float32)
    decimated = (main + tail).astype(jnp.bfloat16)

    first, second = swap_tm(decimated)
    paired = jnp.concatenate([first, second], axis=0).T

    steps = jnp.arange(source_owner.shape[0], dtype=jnp.int32)
    own_first = jnp.sum(jnp.where(steps == tm, source_owner * block + source_offset, 0))
    source_raw = lax.dynamic_slice_in_dim(channel_map, own_first, SRC)
    half_raw = lax.dynamic_slice(channel_map.reshape(n_chan, block), (0, tm * half), (n_chan, half))
    index = jnp.concatenate(
        [half_raw, jnp.broadcast_to(source_raw[None], (n_chan, SRC))], axis=1
    )
    width = index.shape[1]
    rows = jnp.take(paired, index.reshape(-1), axis=0, mode="clip").reshape(n_chan, width, -1)
    series = lax.all_to_all(rows, "chan", 0, 2, tiled=True).reshape(width, samples)
    table = dft_table(samples, bins, jnp.arange(samples, dtype=jnp.int32))
    lag_share = LAGS // n_tm
    lag = lag_kernel(samples, tm * lag_share, lag_share)

    white = whiten_series(series, table)
    other = lax.ppermute(white, "tm", perm=[(0, 1), (1, 0)])
    result = correlate(white, other, half, lag)
    return result.reshape(STEPS, SRC, block, lag_share)


def solution(mesh):
    return jax.shard_map(
        local,
        mesh=mesh,
        in_specs=(P(("chan", "tm"), "parts"), P(), P("parts"), P("parts"), P("parts")),
        out_specs=P(None, None, ("parts", "chan"), "tm"),
        check_vma=False,
    )
```

```python
import functools
import math

import jax
import jax.numpy as jnp
from jax import lax
from jax.experimental import pallas as pl
from jax.experimental.pallas import tpu as pltpu
from jax.sharding import PartitionSpec as P

SRC = 16
STEPS = 2
LAGS = 512
TAPS = 32
STRIDE = 8
HALF_BAND = 32

two_pi = 2.0 * math.pi
epsilon = 1e-06


def decimation_matrix(fir_taps, out_rows, in_rows):
    leads = TAPS // STRIDE
    rows = jnp.arange(out_rows, dtype=jnp.int32)[:, None, None, None]
    groups = jnp.arange(in_rows // STRIDE, dtype=jnp.int32)[None, :, None, None]
    lead = jnp.arange(leads, dtype=jnp.int32)[None, None, :, None]
    taps = fir_taps.reshape(1, 1, leads, STRIDE)
    matrix = jnp.where(groups - rows == lead, taps, 0.0).sum(axis=2)
    return matrix.reshape(out_rows, in_rows)


def dft_table(samples, bins, time_index):
    inner = 32
    outer = samples // inner
    frequency = jnp.arange(bins, dtype=jnp.int32)[None, :]
    low = jnp.arange(inner, dtype=jnp.int32)[:, None]
    high = time_index.reshape(outer, inner)[:, :1]
    scale = two_pi / samples
    low_angle = ((low * frequency) % samples).astype(jnp.float32) * scale
    high_angle = ((high * frequency) % samples).astype(jnp.float32) * scale
    cl, sl = jnp.cos(low_angle)[None], jnp.sin(low_angle)[None]
    ch, sh = jnp.cos(high_angle)[:, None], jnp.sin(high_angle)[:, None]
    cosine = (ch * cl - sh * sl).reshape(samples, bins)
    sine = (sh * cl + ch * sl).reshape(samples, bins)
    return jnp.concatenate([cosine, -sine], axis=1)


def band_matrix(bins):
    g = jnp.arange(bins, dtype=jnp.int32)
    near = jnp.abs(g[:, None] - g[None, :]) <= HALF_BAND
    return near.astype(jnp.bfloat16)


def lag_kernel(samples, first_lag, lag_count):
    bin_count = samples // 2
    inner = 32
    frequency = jnp.arange(bin_count, dtype=jnp.int32)[:, None]
    low = jnp.arange(inner, dtype=jnp.int32)[None, :]
    high = first_lag - LAGS // 2 + jnp.arange(lag_count // inner, dtype=jnp.int32)[None, :] * inner
    scale = two_pi / samples
    low_angle = jnp.mod(frequency * low, samples).astype(jnp.float32) * scale
    high_angle = jnp.mod(frequency * high, samples).astype(jnp.float32) * scale
    cl, sl = jnp.cos(low_angle)[:, None, :], jnp.sin(low_angle)[:, None, :]
    ch, sh = jnp.cos(high_angle)[:, :, None], jnp.sin(high_angle)[:, :, None]
    cosine = (ch * cl - sh * sl).reshape(bin_count, lag_count)
    sine = (sh * cl + ch * sl).reshape(bin_count, lag_count)
    return jnp.concatenate([cosine, -sine], axis=0).astype(jnp.bfloat16)


def whiten_series(series, table):
    samples = series.shape[1]
    bins = samples // 2
    spectrum = jnp.dot(series, table.astype(jnp.bfloat16), preferred_element_type=jnp.float32)
    real_part = spectrum[:, :bins]
    imag_part = spectrum[:, bins:]
    powers = real_part * real_part + imag_part * imag_part
    window = jnp.dot(powers.astype(jnp.bfloat16), band_matrix(bins), preferred_element_type=jnp.float32)
    window_span = 2 * HALF_BAND + 1
    factor = 1.0 / jnp.sqrt(window / window_span + epsilon)
    return jnp.concatenate([real_part * factor, imag_part * factor], axis=1).astype(jnp.bfloat16)


def correlate_kernel(factor, bins, group, half, mine_ref, other_ref, lag_ref, out_ref):
    step = pl.program_id(0)
    first = lax.axis_index("tm") == 0
    lag = lag_ref[...]
    receivers = [mine_ref[:half, :].astype(jnp.float32), other_ref[:half, :].astype(jnp.float32)]
    places = [jnp.where(first, 0, half), jnp.where(first, half, 0)]
    mine_src = mine_ref[half:, :]
    other_src = other_ref[half:, :]
    every = jnp.where(
        first,
        jnp.concatenate([mine_src, other_src], axis=0),
        jnp.concatenate([other_src, mine_src], axis=0),
    ).astype(jnp.float32)
    picked = every[:group]
    for g in range(1, every.shape[0] // group):
        picked = jnp.where(step == g, every[g * group : (g + 1) * group], picked)
    for k in range(group):
        row = picked[k : k + 1]
        real_src = row[:, :bins]
        imag_src = row[:, bins:]
        for part, rcv in enumerate(receivers):
            real_rcv = rcv[:, :bins]
            imag_rcv = rcv[:, bins:]
            cross = jnp.concatenate(
                [real_src * real_rcv + imag_src * imag_rcv, imag_src * real_rcv - real_src * imag_rcv],
                axis=1,
            ).astype(jnp.bfloat16)
            out_ref[k, pl.ds(pl.multiple_of(places[part], 8), half), :] = (
                jnp.dot(cross, lag, preferred_element_type=jnp.float32) * factor
            )


def correlate(low, high, half, lag):
    rows, width = low.shape
    bins = width // 2
    count = 2 * (rows - half)
    block = 2 * half
    lags = lag.shape[1]
    group = 8
    factor = 1.0 / math.sqrt(bins)
    flops = 2 * count * block * width * lags + 6 * count * block * bins
    moved = 4 * rows * width + 2 * lags * width + 4 * count * block * lags
    return pl.pallas_call(
        functools.partial(correlate_kernel, factor, bins, group, half),
        out_shape=jax.ShapeDtypeStruct((count, block, lags), jnp.float32),
        grid=(count // group,),
        in_specs=[
            pl.BlockSpec((rows, width), lambda s: (0, 0)),
            pl.BlockSpec((rows, width), lambda s: (0, 0)),
            pl.BlockSpec((width, lags), lambda s: (0, 0)),
        ],
        out_specs=pl.BlockSpec((group, block, lags), lambda s: (s, 0, 0)),
        compiler_params=pltpu.CompilerParams(dimension_semantics=("arbitrary",)),
        cost_estimate=pl.CostEstimate(flops=flops, bytes_accessed=moved, transcendentals=0),
    )(low, high, lag)


def swap_tm(x):
    other = lax.ppermute(x, "tm", perm=[(0, 1), (1, 0)])
    first = lax.axis_index("tm") == 0
    return jnp.where(first, x, other), jnp.where(first, other, x)


def local(records, fir_taps, channel_map, source_owner, source_offset):
    n_chan = lax.axis_size("chan")
    n_tm = lax.axis_size("tm")
    assert n_tm == 2
    n_dev = n_chan * n_tm
    raw_rows, channels = records.shape
    block = channels // n_chan
    half = block // n_tm
    out_rows = raw_rows // STRIDE
    halo_rows = TAPS - STRIDE
    samples = out_rows * n_dev
    bins = samples // 2
    tm = lax.axis_index("tm")

    taps_matrix = decimation_matrix(fir_taps, out_rows, raw_rows + halo_rows)
    taps_matrix = taps_matrix.astype(jnp.bfloat16)
    reach = halo_rows // STRIDE
    partial = jnp.dot(
        taps_matrix[out_rows - reach :, raw_rows:],
        records[:halo_rows],
        preferred_element_type=jnp.float32,
    )
    shift = [(b, b - 1) for b in range(1, n_dev)]
    tail = lax.ppermute(partial, ("chan", "tm"), perm=shift)
    main = jnp.dot(taps_matrix[:, :raw_rows], records, preferred_element_type=jnp.float32)
    decimated = (main + jnp.pad(tail, ((out_rows - reach, 0), (0, 0)))).astype(jnp.bfloat16)

    first, second = swap_tm(decimated)
    paired = jnp.concatenate([first, second], axis=0).T

    steps = jnp.arange(source_owner.shape[0], dtype=jnp.int32)
    own_first = jnp.sum(jnp.where(steps == tm, source_owner * block + source_offset, 0))
    source_raw = lax.dynamic_slice_in_dim(channel_map, own_first, SRC)
    half_raw = lax.dynamic_slice(channel_map.reshape(n_chan, block), (0, tm * half), (n_chan, half))
    index = jnp.concatenate(
        [half_raw, jnp.broadcast_to(source_raw[None], (n_chan, SRC))], axis=1
    )
    width = index.shape[1]
    rows = jnp.take(paired, index.reshape(-1), axis=0, mode="clip").reshape(n_chan, width, -1)
    series = lax.all_to_all(rows, "chan", 0, 2, tiled=True).reshape(width, samples)
    table = dft_table(samples, bins, jnp.arange(samples, dtype=jnp.int32))
    lag_share = LAGS // n_tm
    lag = lag_kernel(samples, tm * lag_share, lag_share)

    white = whiten_series(series, table)
    other = lax.ppermute(white, "tm", perm=[(0, 1), (1, 0)])
    result = correlate(white, other, half, lag)
    return result.reshape(STEPS, SRC, block, lag_share)


def solution(mesh):
    return jax.shard_map(
        local,
        mesh=mesh,
        in_specs=(P(("chan", "tm"), "parts"), P(), P("parts"), P("parts"), P("parts")),
        out_specs=P(None, None, ("parts", "chan"), "tm"),
        check_vma=False,
    )
```

```python
import functools
import math

import jax
import jax.numpy as jnp
from jax import lax
from jax.experimental import pallas as pl
from jax.experimental.pallas import tpu as pltpu
from jax.sharding import PartitionSpec as P

SRC = 16
STEPS = 2
LAGS = 512
TAPS = 32
STRIDE = 8
HALF_BAND = 32

two_pi = 2.0 * math.pi
epsilon = 1e-06


def decimation_matrix(fir_taps, out_rows, in_rows):
    leads = TAPS // STRIDE
    rows = jnp.arange(out_rows, dtype=jnp.int32)[:, None, None, None]
    groups = jnp.arange(in_rows // STRIDE, dtype=jnp.int32)[None, :, None, None]
    lead = jnp.arange(leads, dtype=jnp.int32)[None, None, :, None]
    taps = fir_taps.reshape(1, 1, leads, STRIDE)
    matrix = jnp.where(groups - rows == lead, taps, 0.0).sum(axis=2)
    return matrix.reshape(out_rows, in_rows)


def dft_table(samples, bins, time_index):
    inner = 32
    outer = samples // inner
    frequency = jnp.arange(bins, dtype=jnp.int32)[None, :]
    low = jnp.arange(inner, dtype=jnp.int32)[:, None]
    high = time_index.reshape(outer, inner)[:, :1]
    scale = two_pi / samples
    low_angle = ((low * frequency) % samples).astype(jnp.float32) * scale
    high_angle = ((high * frequency) % samples).astype(jnp.float32) * scale
    cl, sl = jnp.cos(low_angle)[None], jnp.sin(low_angle)[None]
    ch, sh = jnp.cos(high_angle)[:, None], jnp.sin(high_angle)[:, None]
    cosine = (ch * cl - sh * sl).reshape(samples, bins)
    sine = (sh * cl + ch * sl).reshape(samples, bins)
    return jnp.concatenate([cosine, -sine], axis=1)


def band_matrix(bins):
    g = jnp.arange(bins, dtype=jnp.int32)
    near = jnp.abs(g[:, None] - g[None, :]) <= HALF_BAND
    return near.astype(jnp.bfloat16)


def lag_kernel(samples, first_lag, lag_count):
    bin_count = samples // 2
    inner = 32
    frequency = jnp.arange(bin_count, dtype=jnp.int32)[:, None]
    low = jnp.arange(inner, dtype=jnp.int32)[None, :]
    high = first_lag - LAGS // 2 + jnp.arange(lag_count // inner, dtype=jnp.int32)[None, :] * inner
    scale = two_pi / samples
    low_angle = jnp.mod(frequency * low, samples).astype(jnp.float32) * scale
    high_angle = jnp.mod(frequency * high, samples).astype(jnp.float32) * scale
    cl, sl = jnp.cos(low_angle)[:, None, :], jnp.sin(low_angle)[:, None, :]
    ch, sh = jnp.cos(high_angle)[:, :, None], jnp.sin(high_angle)[:, :, None]
    cosine = (ch * cl - sh * sl).reshape(bin_count, lag_count)
    sine = (sh * cl + ch * sl).reshape(bin_count, lag_count)
    return jnp.concatenate([cosine, -sine], axis=0).astype(jnp.bfloat16)


def whiten_series(series, table):
    samples = series.shape[1]
    bins = samples // 2
    spectrum = jnp.dot(series, table.astype(jnp.bfloat16), preferred_element_type=jnp.float32)
    real_part = spectrum[:, :bins]
    imag_part = spectrum[:, bins:]
    powers = real_part * real_part + imag_part * imag_part
    window = jnp.dot(powers.astype(jnp.bfloat16), band_matrix(bins), preferred_element_type=jnp.float32)
    window_span = 2 * HALF_BAND + 1
    factor = 1.0 / jnp.sqrt(window / window_span + epsilon)
    return jnp.concatenate([real_part * factor, imag_part * factor], axis=1).astype(jnp.bfloat16)


def correlate_kernel(factor, bins, group, half, mine_ref, other_ref, lag_ref, out_ref):
    step = pl.program_id(0)
    first = lax.axis_index("tm") == 0
    lag = lag_ref[...]
    receivers = [mine_ref[:half, :].astype(jnp.float32), other_ref[:half, :].astype(jnp.float32)]
    places = [jnp.where(first, 0, half), jnp.where(first, half, 0)]
    mine_src = mine_ref[half:, :]
    other_src = other_ref[half:, :]
    every = jnp.where(
        first,
        jnp.concatenate([mine_src, other_src], axis=0),
        jnp.concatenate([other_src, mine_src], axis=0),
    ).astype(jnp.float32)
    picked = every[:group]
    for g in range(1, every.shape[0] // group):
        picked = jnp.where(step == g, every[g * group : (g + 1) * group], picked)
    for k in range(group):
        row = picked[k : k + 1]
        real_src = row[:, :bins]
        imag_src = row[:, bins:]
        for part, rcv in enumerate(receivers):
            real_rcv = rcv[:, :bins]
            imag_rcv = rcv[:, bins:]
            cross = jnp.concatenate(
                [real_src * real_rcv + imag_src * imag_rcv, imag_src * real_rcv - real_src * imag_rcv],
                axis=1,
            ).astype(jnp.bfloat16)
            out_ref[k, pl.ds(pl.multiple_of(places[part], 8), half), :] = (
                jnp.dot(cross, lag, preferred_element_type=jnp.float32) * factor
            )


def correlate(low, high, half, lag):
    rows, width = low.shape
    bins = width // 2
    count = 2 * (rows - half)
    block = 2 * half
    lags = lag.shape[1]
    group = 8
    factor = 1.0 / math.sqrt(bins)
    flops = 2 * count * block * width * lags + 6 * count * block * bins
    moved = 4 * rows * width + 2 * lags * width + 4 * count * block * lags
    return pl.pallas_call(
        functools.partial(correlate_kernel, factor, bins, group, half),
        out_shape=jax.ShapeDtypeStruct((count, block, lags), jnp.float32),
        grid=(count // group,),
        in_specs=[pl.BlockSpec(memory_space=pltpu.VMEM)] * 3,
        out_specs=pl.BlockSpec((group, block, lags), lambda s: (s, 0, 0)),
        compiler_params=pltpu.CompilerParams(dimension_semantics=("arbitrary",)),
        cost_estimate=pl.CostEstimate(flops=flops, bytes_accessed=moved, transcendentals=0),
    )(low, high, lag)


def swap_tm(x):
    other = lax.ppermute(x, "tm", perm=[(0, 1), (1, 0)])
    first = lax.axis_index("tm") == 0
    return jnp.where(first, x, other), jnp.where(first, other, x)


def local(records, fir_taps, channel_map, source_owner, source_offset):
    n_chan = lax.axis_size("chan")
    n_tm = lax.axis_size("tm")
    assert n_tm == 2
    n_dev = n_chan * n_tm
    raw_rows, channels = records.shape
    block = channels // n_chan
    half = block // n_tm
    out_rows = raw_rows // STRIDE
    halo_rows = TAPS - STRIDE
    samples = out_rows * n_dev
    bins = samples // 2
    tm = lax.axis_index("tm")

    shift = [(b, b - 1) for b in range(1, n_dev)]
    halo = lax.ppermute(records[:halo_rows], ("chan", "tm"), perm=shift)

    taps_matrix = decimation_matrix(fir_taps, out_rows, raw_rows + halo_rows)
    taps_matrix = taps_matrix.astype(jnp.bfloat16)
    main = jnp.dot(taps_matrix[:, :raw_rows], records, preferred_element_type=jnp.float32)
    tail = jnp.dot(taps_matrix[:, raw_rows:], halo, preferred_element_type=jnp.float32)
    decimated = (main + tail).astype(jnp.bfloat16)

    first, second = swap_tm(decimated)
    paired = jnp.concatenate([first, second], axis=0).T

    steps = jnp.arange(source_owner.shape[0], dtype=jnp.int32)
    own_first = jnp.sum(jnp.where(steps == tm, source_owner * block + source_offset, 0))
    source_raw = lax.dynamic_slice_in_dim(channel_map, own_first, SRC)
    half_raw = lax.dynamic_slice(channel_map.reshape(n_chan, block), (0, tm * half), (n_chan, half))
    index = jnp.concatenate(
        [half_raw, jnp.broadcast_to(source_raw[None], (n_chan, SRC))], axis=1
    )
    width = index.shape[1]
    rows = jnp.take(paired, index.reshape(-1), axis=0, mode="clip").reshape(n_chan, width, -1)
    series = lax.all_to_all(rows, "chan", 0, 2, tiled=True).reshape(width, samples)
    table = dft_table(samples, bins, jnp.arange(samples, dtype=jnp.int32))
    lag_share = LAGS // n_tm
    lag = lag_kernel(samples, tm * lag_share, lag_share)

    white = whiten_series(series, table)
    other = lax.ppermute(white, "tm", perm=[(0, 1), (1, 0)])
    result = correlate(white, other, half, lag)
    return result.reshape(STEPS, SRC, block, lag_share)


def solution(mesh):
    return jax.shard_map(
        local,
        mesh=mesh,
        in_specs=(P(("chan", "tm"), "parts"), P(), P("parts"), P("parts"), P("parts")),
        out_specs=P(None, None, ("parts", "chan"), "tm"),
        check_vma=False,
    )
```

```python
import functools
import math

import jax
import jax.numpy as jnp
from jax import lax
from jax.experimental import pallas as pl
from jax.experimental.pallas import tpu as pltpu
from jax.sharding import PartitionSpec as P

SRC = 16
STEPS = 2
LAGS = 512
TAPS = 32
STRIDE = 8
HALF_BAND = 32

two_pi = 2.0 * math.pi
epsilon = 1e-06


def decimation_matrix(fir_taps, out_rows, in_rows):
    leads = TAPS // STRIDE
    rows = jnp.arange(out_rows, dtype=jnp.int32)[:, None, None, None]
    groups = jnp.arange(in_rows // STRIDE, dtype=jnp.int32)[None, :, None, None]
    lead = jnp.arange(leads, dtype=jnp.int32)[None, None, :, None]
    taps = fir_taps.reshape(1, 1, leads, STRIDE)
    matrix = jnp.where(groups - rows == lead, taps, 0.0).sum(axis=2)
    return matrix.reshape(out_rows, in_rows)


def dft_table(samples, bins, time_index):
    inner = 32
    outer = samples // inner
    frequency = jnp.arange(bins, dtype=jnp.int32)[None, :]
    low = jnp.arange(inner, dtype=jnp.int32)[:, None]
    high = time_index.reshape(outer, inner)[:, :1]
    scale = two_pi / samples
    low_angle = ((low * frequency) % samples).astype(jnp.float32) * scale
    high_angle = ((high * frequency) % samples).astype(jnp.float32) * scale
    cl, sl = jnp.cos(low_angle)[None], jnp.sin(low_angle)[None]
    ch, sh = jnp.cos(high_angle)[:, None], jnp.sin(high_angle)[:, None]
    cosine = (ch * cl - sh * sl).reshape(samples, bins)
    sine = (sh * cl + ch * sl).reshape(samples, bins)
    return jnp.concatenate([cosine, -sine], axis=1)


def band_matrix(bins):
    g = jnp.arange(bins, dtype=jnp.int32)
    near = jnp.abs(g[:, None] - g[None, :]) <= HALF_BAND
    return near.astype(jnp.bfloat16)


def lag_kernel(samples, first_lag, lag_count):
    bin_count = samples // 2
    inner = 32
    frequency = jnp.arange(bin_count, dtype=jnp.int32)[:, None]
    low = jnp.arange(inner, dtype=jnp.int32)[None, :]
    high = first_lag - LAGS // 2 + jnp.arange(lag_count // inner, dtype=jnp.int32)[None, :] * inner
    scale = two_pi / samples
    low_angle = jnp.mod(frequency * low, samples).astype(jnp.float32) * scale
    high_angle = jnp.mod(frequency * high, samples).astype(jnp.float32) * scale
    cl, sl = jnp.cos(low_angle)[:, None, :], jnp.sin(low_angle)[:, None, :]
    ch, sh = jnp.cos(high_angle)[:, :, None], jnp.sin(high_angle)[:, :, None]
    cosine = (ch * cl - sh * sl).reshape(bin_count, lag_count)
    sine = (sh * cl + ch * sl).reshape(bin_count, lag_count)
    return jnp.concatenate([cosine, -sine], axis=0).astype(jnp.bfloat16)


def whiten_series(series, table):
    samples = series.shape[1]
    bins = samples // 2
    spectrum = jnp.dot(series, table.astype(jnp.bfloat16), preferred_element_type=jnp.float32)
    real_part = spectrum[:, :bins]
    imag_part = spectrum[:, bins:]
    powers = real_part * real_part + imag_part * imag_part
    window = jnp.dot(powers.astype(jnp.bfloat16), band_matrix(bins), preferred_element_type=jnp.float32)
    window_span = 2 * HALF_BAND + 1
    factor = 1.0 / jnp.sqrt(window / window_span + epsilon)
    return jnp.concatenate([real_part * factor, imag_part * factor], axis=1).astype(jnp.bfloat16)


def correlate_kernel(factor, bins, group, half, mine_ref, other_ref, lag_ref, out_ref):
    step = pl.program_id(0)
    first = lax.axis_index("tm") == 0
    lag = lag_ref[...]
    receivers = [mine_ref[:half, :].astype(jnp.float32), other_ref[:half, :].astype(jnp.float32)]
    places = [jnp.where(first, 0, half), jnp.where(first, half, 0)]
    mine_src = mine_ref[half:, :]
    other_src = other_ref[half:, :]
    every = jnp.where(
        first,
        jnp.concatenate([mine_src, other_src], axis=0),
        jnp.concatenate([other_src, mine_src], axis=0),
    ).astype(jnp.float32)
    picked = every[:group]
    for g in range(1, every.shape[0] // group):
        picked = jnp.where(step == g, every[g * group : (g + 1) * group], picked)
    for k in range(group):
        row = picked[k : k + 1]
        real_src = row[:, :bins]
        imag_src = row[:, bins:]
        for part, rcv in enumerate(receivers):
            real_rcv = rcv[:, :bins]
            imag_rcv = rcv[:, bins:]
            cross = jnp.concatenate(
                [real_src * real_rcv + imag_src * imag_rcv, imag_src * real_rcv - real_src * imag_rcv],
                axis=1,
            ).astype(jnp.bfloat16)
            out_ref[k, pl.ds(pl.multiple_of(places[part], 8), half), :] = (
                jnp.dot(cross, lag, preferred_element_type=jnp.float32) * factor
            )


def correlate(low, high, half, lag):
    rows, width = low.shape
    bins = width // 2
    count = 2 * (rows - half)
    block = 2 * half
    lags = lag.shape[1]
    group = 8
    factor = 1.0 / math.sqrt(bins)
    flops = 2 * count * block * width * lags + 6 * count * block * bins
    moved = 4 * rows * width + 2 * lags * width + 4 * count * block * lags
    return pl.pallas_call(
        functools.partial(correlate_kernel, factor, bins, group, half),
        out_shape=jax.ShapeDtypeStruct((count, block, lags), jnp.float32),
        grid=(count // group,),
        in_specs=[
            pl.BlockSpec((rows, width), lambda s: (0, 0)),
            pl.BlockSpec((rows, width), lambda s: (0, 0)),
            pl.BlockSpec((width, lags), lambda s: (0, 0)),
        ],
        out_specs=pl.BlockSpec((group, block, lags), lambda s: (s, 0, 0)),
        compiler_params=pltpu.CompilerParams(dimension_semantics=("arbitrary",)),
        cost_estimate=pl.CostEstimate(flops=flops, bytes_accessed=moved, transcendentals=0),
    )(low, high, lag)


def swap_tm(x):
    other = lax.ppermute(x, "tm", perm=[(0, 1), (1, 0)])
    first = lax.axis_index("tm") == 0
    return jnp.where(first, x, other), jnp.where(first, other, x)


def local(records, fir_taps, channel_map, source_owner, source_offset):
    n_chan = lax.axis_size("chan")
    n_tm = lax.axis_size("tm")
    assert n_tm == 2
    n_dev = n_chan * n_tm
    raw_rows, channels = records.shape
    block = channels // n_chan
    half = block // n_tm
    out_rows = raw_rows // STRIDE
    halo_rows = TAPS - STRIDE
    samples = out_rows * n_dev
    bins = samples // 2
    tm = lax.axis_index("tm")

    shift = [(b, b - 1) for b in range(1, n_dev)]
    halo = lax.ppermute(records[:halo_rows], ("chan", "tm"), perm=shift)

    taps_matrix = decimation_matrix(fir_taps, out_rows, raw_rows + halo_rows)
    taps_matrix = taps_matrix.astype(jnp.bfloat16)
    main = jnp.dot(taps_matrix[:, :raw_rows], records, preferred_element_type=jnp.float32)
    tail = jnp.dot(taps_matrix[:, raw_rows:], halo, preferred_element_type=jnp.float32)
    decimated = (main + tail).astype(jnp.bfloat16)

    first, second = swap_tm(decimated)
    paired = jnp.concatenate([first, second], axis=0).T

    steps = jnp.arange(source_owner.shape[0], dtype=jnp.int32)
    own_first = jnp.sum(jnp.where(steps == tm, source_owner * block + source_offset, 0))
    source_raw = lax.dynamic_slice_in_dim(channel_map, own_first, SRC)
    half_raw = lax.dynamic_slice(channel_map.reshape(n_chan, block), (0, tm * half), (n_chan, half))
    index = jnp.concatenate(
        [half_raw, jnp.broadcast_to(source_raw[None], (n_chan, SRC))], axis=1
    )
    width = index.shape[1]
    rows = jnp.take(paired, index.reshape(-1), axis=0, mode="clip").reshape(n_chan, width, -1)
    arrived = lax.all_to_all(rows, "chan", 0, 0, tiled=True)
    series = arrived.transpose(1, 0, 2).reshape(width, samples)
    table = dft_table(samples, bins, jnp.arange(samples, dtype=jnp.int32))
    lag_share = LAGS // n_tm
    lag = lag_kernel(samples, tm * lag_share, lag_share)

    white = whiten_series(series, table)
    other = lax.ppermute(white, "tm", perm=[(0, 1), (1, 0)])
    result = correlate(white, other, half, lag)
    return result.reshape(STEPS, SRC, block, lag_share)


def solution(mesh):
    return jax.shard_map(
        local,
        mesh=mesh,
        in_specs=(P(("chan", "tm"), "parts"), P(), P("parts"), P("parts"), P("parts")),
        out_specs=P(None, None, ("parts", "chan"), "tm"),
        check_vma=False,
    )
```

```python
import functools
import math

import jax
import jax.numpy as jnp
import ml_dtypes
import numpy as np
from jax import lax
from jax.experimental import pallas as pl
from jax.experimental.pallas import tpu as pltpu
from jax.sharding import PartitionSpec as P

SRC = 16
STEPS = 2
LAGS = 512
TAPS = 32
STRIDE = 8
HALF_BAND = 32

two_pi = 2.0 * math.pi
epsilon = 1e-06


def decimation_matrix(fir_taps, out_rows, in_rows):
    leads = TAPS // STRIDE
    rows = jnp.arange(out_rows, dtype=jnp.int32)[:, None, None, None]
    groups = jnp.arange(in_rows // STRIDE, dtype=jnp.int32)[None, :, None, None]
    lead = jnp.arange(leads, dtype=jnp.int32)[None, None, :, None]
    taps = fir_taps.reshape(1, 1, leads, STRIDE)
    matrix = jnp.where(groups - rows == lead, taps, 0.0).sum(axis=2)
    return matrix.reshape(out_rows, in_rows)


def dft_table(samples, bins, time_index):
    inner = 32
    outer = samples // inner
    frequency = jnp.arange(bins, dtype=jnp.int32)[None, :]
    low = jnp.arange(inner, dtype=jnp.int32)[:, None]
    high = time_index.reshape(outer, inner)[:, :1]
    scale = two_pi / samples
    low_angle = ((low * frequency) % samples).astype(jnp.float32) * scale
    high_angle = ((high * frequency) % samples).astype(jnp.float32) * scale
    cl, sl = jnp.cos(low_angle)[None], jnp.sin(low_angle)[None]
    ch, sh = jnp.cos(high_angle)[:, None], jnp.sin(high_angle)[:, None]
    cosine = (ch * cl - sh * sl).reshape(samples, bins)
    sine = (sh * cl + ch * sl).reshape(samples, bins)
    return jnp.concatenate([cosine, -sine], axis=1)


def band_matrix(bins):
    g = jnp.arange(bins, dtype=jnp.int32)
    near = jnp.abs(g[:, None] - g[None, :]) <= HALF_BAND
    return near.astype(jnp.bfloat16)


def lag_tables(samples, cores):
    bin_count = samples // 2
    share = LAGS // cores
    frequency = np.arange(bin_count, dtype=np.int64)[:, None]
    tables = []
    for core in range(cores):
        shifts = core * share + np.arange(share, dtype=np.int64)[None, :] - LAGS // 2
        phases = np.mod(frequency * shifts, samples).astype(np.float32)
        angles = phases * np.float32(two_pi / samples)
        tables.append(np.concatenate([np.cos(angles), -np.sin(angles)], axis=0))
    return np.stack(tables).astype(ml_dtypes.bfloat16)


def whiten_series(series, table):
    samples = series.shape[1]
    bins = samples // 2
    spectrum = jnp.dot(series, table.astype(jnp.bfloat16), preferred_element_type=jnp.float32)
    real_part = spectrum[:, :bins]
    imag_part = spectrum[:, bins:]
    powers = real_part * real_part + imag_part * imag_part
    window = jnp.dot(powers.astype(jnp.bfloat16), band_matrix(bins), preferred_element_type=jnp.float32)
    window_span = 2 * HALF_BAND + 1
    factor = 1.0 / jnp.sqrt(window / window_span + epsilon)
    return jnp.concatenate([real_part * factor, imag_part * factor], axis=1).astype(jnp.bfloat16)


def correlate_kernel(factor, bins, group, half, tm_ref, mine_ref, other_ref, lag_ref, out_ref):
    step = pl.program_id(0)
    first = tm_ref[0] == 0
    lag = lag_ref[0]
    receivers = [mine_ref[:half, :].astype(jnp.float32), other_ref[:half, :].astype(jnp.float32)]
    places = [jnp.where(first, 0, half), jnp.where(first, half, 0)]
    mine_src = mine_ref[half:, :]
    other_src = other_ref[half:, :]
    every = jnp.where(
        first,
        jnp.concatenate([mine_src, other_src], axis=0),
        jnp.concatenate([other_src, mine_src], axis=0),
    ).astype(jnp.float32)
    picked = every[:group]
    for g in range(1, every.shape[0] // group):
        picked = jnp.where(step == g, every[g * group : (g + 1) * group], picked)
    for k in range(group):
        row = picked[k : k + 1]
        real_src = row[:, :bins]
        imag_src = row[:, bins:]
        for part, rcv in enumerate(receivers):
            real_rcv = rcv[:, :bins]
            imag_rcv = rcv[:, bins:]
            cross = jnp.concatenate(
                [real_src * real_rcv + imag_src * imag_rcv, imag_src * real_rcv - real_src * imag_rcv],
                axis=1,
            ).astype(jnp.bfloat16)
            out_ref[k, pl.ds(pl.multiple_of(places[part], 8), half), :] = (
                jnp.dot(cross, lag, preferred_element_type=jnp.float32) * factor
            )


def correlate(tm, low, high, half, lag):
    rows, width = low.shape
    bins = width // 2
    count = 2 * (rows - half)
    block = 2 * half
    lags = lag.shape[2]
    group = 8
    factor = 1.0 / math.sqrt(bins)
    flops = 2 * count * block * width * lags + 6 * count * block * bins
    moved = 4 * rows * width + 2 * lags * width + 4 * count * block * lags
    return pl.pallas_call(
        functools.partial(correlate_kernel, factor, bins, group, half),
        out_shape=jax.ShapeDtypeStruct((count, block, lags), jnp.float32),
        grid_spec=pltpu.PrefetchScalarGridSpec(
            num_scalar_prefetch=1,
            grid=(count // group,),
            in_specs=[
                pl.BlockSpec((rows, width), lambda s, tm_ref: (0, 0)),
                pl.BlockSpec((rows, width), lambda s, tm_ref: (0, 0)),
                pl.BlockSpec((1, width, lags), lambda s, tm_ref: (tm_ref[0], 0, 0)),
            ],
            out_specs=pl.BlockSpec((group, block, lags), lambda s, tm_ref: (s, 0, 0)),
        ),
        compiler_params=pltpu.CompilerParams(dimension_semantics=("arbitrary",)),
        cost_estimate=pl.CostEstimate(flops=flops, bytes_accessed=moved, transcendentals=0),
    )(tm, low, high, lag)


def swap_tm(x):
    other = lax.ppermute(x, "tm", perm=[(0, 1), (1, 0)])
    first = lax.axis_index("tm") == 0
    return jnp.where(first, x, other), jnp.where(first, other, x)


def local(records, fir_taps, channel_map, source_owner, source_offset):
    n_chan = lax.axis_size("chan")
    n_tm = lax.axis_size("tm")
    assert n_tm == 2
    n_dev = n_chan * n_tm
    raw_rows, channels = records.shape
    block = channels // n_chan
    half = block // n_tm
    out_rows = raw_rows // STRIDE
    halo_rows = TAPS - STRIDE
    samples = out_rows * n_dev
    bins = samples // 2
    tm = lax.axis_index("tm")

    shift = [(b, b - 1) for b in range(1, n_dev)]
    halo = lax.ppermute(records[:halo_rows], ("chan", "tm"), perm=shift)

    taps_matrix = decimation_matrix(fir_taps, out_rows, raw_rows + halo_rows)
    taps_matrix = taps_matrix.astype(jnp.bfloat16)
    main = jnp.dot(taps_matrix[:, :raw_rows], records, preferred_element_type=jnp.float32)
    tail = jnp.dot(taps_matrix[:, raw_rows:], halo, preferred_element_type=jnp.float32)
    decimated = (main + tail).astype(jnp.bfloat16)

    first, second = swap_tm(decimated)
    paired = jnp.concatenate([first, second], axis=0).T

    steps = jnp.arange(source_owner.shape[0], dtype=jnp.int32)
    own_first = jnp.sum(jnp.where(steps == tm, source_owner * block + source_offset, 0))
    source_raw = lax.dynamic_slice_in_dim(channel_map, own_first, SRC)
    half_raw = lax.dynamic_slice(channel_map.reshape(n_chan, block), (0, tm * half), (n_chan, half))
    index = jnp.concatenate(
        [half_raw, jnp.broadcast_to(source_raw[None], (n_chan, SRC))], axis=1
    )
    width = index.shape[1]
    rows = jnp.take(paired, index.reshape(-1), axis=0, mode="clip").reshape(n_chan, width, -1)
    series = lax.all_to_all(rows, "chan", 0, 2, tiled=True).reshape(width, samples)
    table = dft_table(samples, bins, jnp.arange(samples, dtype=jnp.int32))
    lag_share = LAGS // n_tm
    lag = jnp.asarray(lag_tables(samples, n_tm))

    white = whiten_series(series, table)
    other = lax.ppermute(white, "tm", perm=[(0, 1), (1, 0)])
    result = correlate(jnp.reshape(tm, (1,)).astype(jnp.int32), white, other, half, lag)
    return result.reshape(STEPS, SRC, block, lag_share)


def solution(mesh):
    return jax.shard_map(
        local,
        mesh=mesh,
        in_specs=(P(("chan", "tm"), "parts"), P(), P("parts"), P("parts"), P("parts")),
        out_specs=P(None, None, ("parts", "chan"), "tm"),
        check_vma=False,
    )
```

```python
import functools
import math

import jax
import jax.numpy as jnp
import ml_dtypes
import numpy as np
from jax import lax
from jax.experimental import pallas as pl
from jax.experimental.pallas import tpu as pltpu
from jax.sharding import PartitionSpec as P

SRC = 16
STEPS = 2
LAGS = 512
TAPS = 32
STRIDE = 8
HALF_BAND = 32

two_pi = 2.0 * math.pi
epsilon = 1e-06


def decimation_matrix(fir_taps, out_rows, in_rows):
    leads = TAPS // STRIDE
    rows = jnp.arange(out_rows, dtype=jnp.int32)[:, None, None, None]
    groups = jnp.arange(in_rows // STRIDE, dtype=jnp.int32)[None, :, None, None]
    lead = jnp.arange(leads, dtype=jnp.int32)[None, None, :, None]
    taps = fir_taps.reshape(1, 1, leads, STRIDE)
    matrix = jnp.where(groups - rows == lead, taps, 0.0).sum(axis=2)
    return matrix.reshape(out_rows, in_rows)


def dft_table(samples, bins, time_index):
    inner = 32
    outer = samples // inner
    frequency = jnp.arange(bins, dtype=jnp.int32)[None, :]
    low = jnp.arange(inner, dtype=jnp.int32)[:, None]
    high = time_index.reshape(outer, inner)[:, :1]
    scale = two_pi / samples
    low_angle = ((low * frequency) % samples).astype(jnp.float32) * scale
    high_angle = ((high * frequency) % samples).astype(jnp.float32) * scale
    cl, sl = jnp.cos(low_angle)[None], jnp.sin(low_angle)[None]
    ch, sh = jnp.cos(high_angle)[:, None], jnp.sin(high_angle)[:, None]
    cosine = (ch * cl - sh * sl).reshape(samples, bins)
    sine = (sh * cl + ch * sl).reshape(samples, bins)
    return jnp.concatenate([cosine, -sine], axis=1)


def band_matrix(bins):
    g = jnp.arange(bins, dtype=jnp.int32)
    near = jnp.abs(g[:, None] - g[None, :]) <= HALF_BAND
    return near.astype(jnp.bfloat16)


def lag_tables(samples, cores):
    bin_count = samples // 2
    share = LAGS // cores
    frequency = np.arange(bin_count, dtype=np.int64)[:, None]
    tables = []
    for core in range(cores):
        shifts = core * share + np.arange(share, dtype=np.int64)[None, :] - LAGS // 2
        phases = np.mod(frequency * shifts, samples).astype(np.float32)
        angles = phases * np.float32(two_pi / samples)
        tables.append(np.concatenate([np.cos(angles), -np.sin(angles)], axis=0))
    return np.stack(tables).astype(ml_dtypes.bfloat16)


def whiten_series(series, table):
    samples = series.shape[1]
    bins = samples // 2
    spectrum = jnp.dot(series, table.astype(jnp.bfloat16), preferred_element_type=jnp.float32)
    real_part = spectrum[:, :bins]
    imag_part = spectrum[:, bins:]
    powers = real_part * real_part + imag_part * imag_part
    window = jnp.dot(powers.astype(jnp.bfloat16), band_matrix(bins), preferred_element_type=jnp.float32)
    window_span = 2 * HALF_BAND + 1
    factor = 1.0 / jnp.sqrt(window / window_span + epsilon)
    return jnp.concatenate([real_part * factor, imag_part * factor], axis=1).astype(jnp.bfloat16)


def correlate_kernel(factor, bins, group, tm_ref, rcv_ref, mine_ref, other_ref, lag_ref, *rest):
    out_ref = rest[-1]
    step = pl.program_id(0)
    first = tm_ref[0] == 0
    lag = lag_ref[0]
    rcv = rcv_ref[...].astype(jnp.float32)
    real_rcv = rcv[:, :bins]
    imag_rcv = rcv[:, bins:]
    mine_src = mine_ref[...]
    other_src = other_ref[...]
    every = jnp.where(
        first,
        jnp.concatenate([mine_src, other_src], axis=0),
        jnp.concatenate([other_src, mine_src], axis=0),
    ).astype(jnp.float32)
    picked = every[:group]
    for g in range(1, every.shape[0] // group):
        picked = jnp.where(step == g, every[g * group : (g + 1) * group], picked)
    for k in range(group):
        row = picked[k : k + 1]
        real_src = row[:, :bins]
        imag_src = row[:, bins:]
        cross = jnp.concatenate(
            [real_src * real_rcv + imag_src * imag_rcv, imag_src * real_rcv - real_src * imag_rcv],
            axis=1,
        ).astype(jnp.bfloat16)
        out_ref[k] = jnp.dot(cross, lag, preferred_element_type=jnp.float32) * factor


def correlate(tm, receivers, mine_src, other_src, lag, own, previous):
    half, width = receivers.shape
    bins = width // 2
    count = 2 * mine_src.shape[0]
    block = 2 * half
    lags = lag.shape[2]
    group = 8
    factor = 1.0 / math.sqrt(bins)
    flops = 2 * count * half * width * lags + 6 * count * half * bins
    moved = 2 * half * width + 2 * lags * width + 4 * count * half * lags

    def out_index(s, tm_ref):
        core = tm_ref[0] if own else 1 - tm_ref[0]
        return (s, core, 0)

    operands = [tm, receivers, mine_src, other_src, lag]
    in_specs = [
        pl.BlockSpec(receivers.shape, lambda s, tm_ref: (0, 0)),
        pl.BlockSpec(mine_src.shape, lambda s, tm_ref: (0, 0)),
        pl.BlockSpec(other_src.shape, lambda s, tm_ref: (0, 0)),
        pl.BlockSpec((1, width, lags), lambda s, tm_ref: (tm_ref[0], 0, 0)),
    ]
    aliases = {}
    if previous is not None:
        operands.append(previous)
        in_specs.append(pl.BlockSpec(memory_space=pl.ANY))
        aliases = {len(operands) - 1: 0}
    return pl.pallas_call(
        functools.partial(correlate_kernel, factor, bins, group),
        out_shape=jax.ShapeDtypeStruct((count, block, lags), jnp.float32),
        grid_spec=pltpu.PrefetchScalarGridSpec(
            num_scalar_prefetch=1,
            grid=(count // group,),
            in_specs=in_specs,
            out_specs=pl.BlockSpec((group, half, lags), out_index),
        ),
        input_output_aliases=aliases,
        compiler_params=pltpu.CompilerParams(dimension_semantics=("arbitrary",)),
        cost_estimate=pl.CostEstimate(flops=flops, bytes_accessed=moved, transcendentals=0),
    )(*operands)


def swap_tm(x):
    other = lax.ppermute(x, "tm", perm=[(0, 1), (1, 0)])
    first = lax.axis_index("tm") == 0
    return jnp.where(first, x, other), jnp.where(first, other, x)


def local(records, fir_taps, channel_map, source_owner, source_offset):
    n_chan = lax.axis_size("chan")
    n_tm = lax.axis_size("tm")
    assert n_tm == 2
    n_dev = n_chan * n_tm
    raw_rows, channels = records.shape
    block = channels // n_chan
    half = block // n_tm
    out_rows = raw_rows // STRIDE
    halo_rows = TAPS - STRIDE
    samples = out_rows * n_dev
    bins = samples // 2
    tm = lax.axis_index("tm")

    shift = [(b, b - 1) for b in range(1, n_dev)]
    halo = lax.ppermute(records[:halo_rows], ("chan", "tm"), perm=shift)

    taps_matrix = decimation_matrix(fir_taps, out_rows, raw_rows + halo_rows)
    taps_matrix = taps_matrix.astype(jnp.bfloat16)
    main = jnp.dot(taps_matrix[:, :raw_rows], records, preferred_element_type=jnp.float32)
    tail = jnp.dot(taps_matrix[:, raw_rows:], halo, preferred_element_type=jnp.float32)
    decimated = (main + tail).astype(jnp.bfloat16)

    first, second = swap_tm(decimated)
    paired = jnp.concatenate([first, second], axis=0).T

    steps = jnp.arange(source_owner.shape[0], dtype=jnp.int32)
    own_first = jnp.sum(jnp.where(steps == tm, source_owner * block + source_offset, 0))
    source_raw = lax.dynamic_slice_in_dim(channel_map, own_first, SRC)
    half_raw = lax.dynamic_slice(channel_map.reshape(n_chan, block), (0, tm * half), (n_chan, half))
    index = jnp.concatenate(
        [half_raw, jnp.broadcast_to(source_raw[None], (n_chan, SRC))], axis=1
    )
    width = index.shape[1]
    rows = jnp.take(paired, index.reshape(-1), axis=0, mode="clip").reshape(n_chan, width, -1)
    series = lax.all_to_all(rows, "chan", 0, 2, tiled=True).reshape(width, samples)
    table = dft_table(samples, bins, jnp.arange(samples, dtype=jnp.int32))
    lag_share = LAGS // n_tm
    lag = jnp.asarray(lag_tables(samples, n_tm))

    white = whiten_series(series, table)
    swap = [(0, 1), (1, 0)]
    other_src = lax.ppermute(white[half:], "tm", perm=swap)
    other_rcv = lax.ppermute(white[:half], "tm", perm=swap)
    core = jnp.reshape(tm, (1,)).astype(jnp.int32)
    result = correlate(core, white[:half], white[half:], other_src, lag, True, None)
    result = correlate(core, other_rcv, white[half:], other_src, lag, False, result)
    return result.reshape(STEPS, SRC, block, lag_share)


def solution(mesh):
    return jax.shard_map(
        local,
        mesh=mesh,
        in_specs=(P(("chan", "tm"), "parts"), P(), P("parts"), P("parts"), P("parts")),
        out_specs=P(None, None, ("parts", "chan"), "tm"),
        check_vma=False,
    )
```

```python
import functools
import math

import jax
import jax.numpy as jnp
from jax import lax
from jax.experimental import pallas as pl
from jax.experimental.pallas import tpu as pltpu
from jax.sharding import PartitionSpec as P

SRC = 16
STEPS = 2
LAGS = 512
TAPS = 32
STRIDE = 8
HALF_BAND = 32

two_pi = 2.0 * math.pi
epsilon = 1e-06


def decimation_matrix(fir_taps, out_rows, in_rows):
    leads = TAPS // STRIDE
    rows = jnp.arange(out_rows, dtype=jnp.int32)[:, None, None, None]
    groups = jnp.arange(in_rows // STRIDE, dtype=jnp.int32)[None, :, None, None]
    lead = jnp.arange(leads, dtype=jnp.int32)[None, None, :, None]
    taps = fir_taps.reshape(1, 1, leads, STRIDE)
    matrix = jnp.where(groups - rows == lead, taps, 0.0).sum(axis=2)
    return matrix.reshape(out_rows, in_rows)


def dft_table(samples, bins, time_index):
    inner = 32
    outer = samples // inner
    frequency = jnp.arange(bins, dtype=jnp.int32)[None, :]
    low = jnp.arange(inner, dtype=jnp.int32)[:, None]
    high = time_index.reshape(outer, inner)[:, :1]
    scale = two_pi / samples
    low_angle = ((low * frequency) % samples).astype(jnp.float32) * scale
    high_angle = ((high * frequency) % samples).astype(jnp.float32) * scale
    cl, sl = jnp.cos(low_angle)[None], jnp.sin(low_angle)[None]
    ch, sh = jnp.cos(high_angle)[:, None], jnp.sin(high_angle)[:, None]
    cosine = (ch * cl - sh * sl).reshape(samples, bins)
    sine = (sh * cl + ch * sl).reshape(samples, bins)
    return jnp.concatenate([cosine, -sine], axis=1)


def band_matrix(bins):
    g = jnp.arange(bins, dtype=jnp.int32)
    near = jnp.abs(g[:, None] - g[None, :]) <= HALF_BAND
    return near.astype(jnp.bfloat16)


def lag_kernel(samples, first_lag, lag_count):
    bin_count = samples // 2
    inner = 32
    frequency = jnp.arange(bin_count, dtype=jnp.int32)[:, None]
    low = jnp.arange(inner, dtype=jnp.int32)[None, :]
    high = first_lag - LAGS // 2 + jnp.arange(lag_count // inner, dtype=jnp.int32)[None, :] * inner
    scale = two_pi / samples
    low_angle = jnp.mod(frequency * low, samples).astype(jnp.float32) * scale
    high_angle = jnp.mod(frequency * high, samples).astype(jnp.float32) * scale
    cl, sl = jnp.cos(low_angle)[:, None, :], jnp.sin(low_angle)[:, None, :]
    ch, sh = jnp.cos(high_angle)[:, :, None], jnp.sin(high_angle)[:, :, None]
    cosine = (ch * cl - sh * sl).reshape(bin_count, lag_count)
    sine = (sh * cl + ch * sl).reshape(bin_count, lag_count)
    return jnp.concatenate([cosine, -sine], axis=0).astype(jnp.bfloat16)


def whiten_series(series, table):
    samples = series.shape[1]
    bins = samples // 2
    spectrum = jnp.dot(series, table.astype(jnp.bfloat16), preferred_element_type=jnp.float32)
    real_part = spectrum[:, :bins]
    imag_part = spectrum[:, bins:]
    powers = real_part * real_part + imag_part * imag_part
    window = jnp.dot(powers.astype(jnp.bfloat16), band_matrix(bins), preferred_element_type=jnp.float32)
    window_span = 2 * HALF_BAND + 1
    factor = 1.0 / jnp.sqrt(window / window_span + epsilon)
    return jnp.concatenate([real_part * factor, imag_part * factor], axis=1).astype(jnp.bfloat16)


def correlate_kernel(factor, bins, group, half, mine_ref, other_ref, lag_ref, out_ref):
    step = pl.program_id(0)
    first = lax.axis_index("tm") == 0
    lag = lag_ref[...]
    receivers = [mine_ref[:half, :].astype(jnp.float32), other_ref[:half, :].astype(jnp.float32)]
    places = [jnp.where(first, 0, half), jnp.where(first, half, 0)]
    mine_src = mine_ref[half:, :]
    other_src = other_ref[half:, :]
    every = jnp.where(
        first,
        jnp.concatenate([mine_src, other_src], axis=0),
        jnp.concatenate([other_src, mine_src], axis=0),
    ).astype(jnp.float32)
    picked = every[:group]
    for g in range(1, every.shape[0] // group):
        picked = jnp.where(step == g, every[g * group : (g + 1) * group], picked)
    for k in range(group):
        row = picked[k : k + 1]
        real_src = row[:, :bins]
        imag_src = row[:, bins:]
        for part, rcv in enumerate(receivers):
            real_rcv = rcv[:, :bins]
            imag_rcv = rcv[:, bins:]
            cross = jnp.concatenate(
                [real_src * real_rcv + imag_src * imag_rcv, imag_src * real_rcv - real_src * imag_rcv],
                axis=1,
            ).astype(jnp.bfloat16)
            out_ref[k, pl.ds(pl.multiple_of(places[part], 8), half), :] = (
                jnp.dot(cross, lag, preferred_element_type=jnp.float32) * factor
            )


def correlate(low, high, half, lag):
    rows, width = low.shape
    bins = width // 2
    count = 2 * (rows - half)
    block = 2 * half
    lags = lag.shape[1]
    group = 8
    factor = 1.0 / math.sqrt(bins)
    flops = 2 * count * block * width * lags + 6 * count * block * bins
    moved = 4 * rows * width + 2 * lags * width + 4 * count * block * lags
    return pl.pallas_call(
        functools.partial(correlate_kernel, factor, bins, group, half),
        out_shape=jax.ShapeDtypeStruct((count, block, lags), jnp.float32),
        grid=(count // group,),
        in_specs=[
            pl.BlockSpec((rows, width), lambda s: (0, 0)),
            pl.BlockSpec((rows, width), lambda s: (0, 0)),
            pl.BlockSpec((width, lags), lambda s: (0, 0)),
        ],
        out_specs=pl.BlockSpec((group, block, lags), lambda s: (s, 0, 0)),
        compiler_params=pltpu.CompilerParams(dimension_semantics=("arbitrary",)),
        cost_estimate=pl.CostEstimate(flops=flops, bytes_accessed=moved, transcendentals=0),
    )(low, high, lag)


def swap_tm(x):
    other = lax.ppermute(x, "tm", perm=[(0, 1), (1, 0)])
    first = lax.axis_index("tm") == 0
    return jnp.where(first, x, other), jnp.where(first, other, x)


def local(records, fir_taps, channel_map, source_owner, source_offset):
    n_chan = lax.axis_size("chan")
    n_tm = lax.axis_size("tm")
    assert n_tm == 2
    n_dev = n_chan * n_tm
    raw_rows, channels = records.shape
    block = channels // n_chan
    half = block // n_tm
    out_rows = raw_rows // STRIDE
    halo_rows = TAPS
    samples = out_rows * n_dev
    bins = samples // 2
    tm = lax.axis_index("tm")

    shift = [(b, b - 1) for b in range(1, n_dev)]
    halo = lax.ppermute(records[:halo_rows], ("chan", "tm"), perm=shift)

    taps_matrix = decimation_matrix(fir_taps, out_rows, raw_rows + halo_rows)
    taps_matrix = taps_matrix.astype(jnp.bfloat16)
    main = jnp.dot(taps_matrix[:, :raw_rows], records, preferred_element_type=jnp.float32)
    tail = jnp.dot(taps_matrix[:, raw_rows:], halo, preferred_element_type=jnp.float32)
    decimated = (main + tail).astype(jnp.bfloat16)

    first, second = swap_tm(decimated)
    paired = jnp.concatenate([first, second], axis=0).T

    steps = jnp.arange(source_owner.shape[0], dtype=jnp.int32)
    own_first = jnp.sum(jnp.where(steps == tm, source_owner * block + source_offset, 0))
    source_raw = lax.dynamic_slice_in_dim(channel_map, own_first, SRC)
    half_raw = lax.dynamic_slice(channel_map.reshape(n_chan, block), (0, tm * half), (n_chan, half))
    index = jnp.concatenate(
        [half_raw, jnp.broadcast_to(source_raw[None], (n_chan, SRC))], axis=1
    )
    width = index.shape[1]
    rows = jnp.take(paired, index.reshape(-1), axis=0, mode="clip").reshape(n_chan, width, -1)
    series = lax.all_to_all(rows, "chan", 0, 2, tiled=True).reshape(width, samples)
    table = dft_table(samples, bins, jnp.arange(samples, dtype=jnp.int32))
    lag_share = LAGS // n_tm
    lag = lag_kernel(samples, tm * lag_share, lag_share)

    white = whiten_series(series, table)
    other = lax.ppermute(white, "tm", perm=[(0, 1), (1, 0)])
    result = correlate(white, other, half, lag)
    return result.reshape(STEPS, SRC, block, lag_share)


def solution(mesh):
    return jax.shard_map(
        local,
        mesh=mesh,
        in_specs=(P(("chan", "tm"), "parts"), P(), P("parts"), P("parts"), P("parts")),
        out_specs=P(None, None, ("parts", "chan"), "tm"),
        check_vma=False,
    )
```

```python
import functools
import math

import jax
import jax.numpy as jnp
from jax import lax
from jax.experimental import pallas as pl
from jax.experimental.pallas import tpu as pltpu
from jax.sharding import PartitionSpec as P

SRC = 16
STEPS = 2
LAGS = 512
TAPS = 32
STRIDE = 8
HALF_BAND = 32

two_pi = 2.0 * math.pi
epsilon = 1e-06


def decimation_matrix(fir_taps, out_rows, in_rows):
    rows = jnp.arange(out_rows, dtype=jnp.int32)[:, None, None]
    cols = jnp.arange(in_rows, dtype=jnp.int32)[None, :, None]
    tap = jnp.arange(TAPS, dtype=jnp.int32)[None, None, :]
    onehot = (cols - STRIDE * rows == tap).astype(jnp.bfloat16)
    matrix = jnp.dot(onehot, fir_taps.astype(jnp.bfloat16), preferred_element_type=jnp.float32)
    return matrix.astype(jnp.bfloat16)


def dft_table(samples, bins, time_index):
    inner = 32
    outer = samples // inner
    frequency = jnp.arange(bins, dtype=jnp.int32)[None, :]
    low = jnp.arange(inner, dtype=jnp.int32)[:, None]
    high = time_index.reshape(outer, inner)[:, :1]
    scale = two_pi / samples
    low_angle = ((low * frequency) % samples).astype(jnp.float32) * scale
    high_angle = ((high * frequency) % samples).astype(jnp.float32) * scale
    cl, sl = jnp.cos(low_angle)[None], jnp.sin(low_angle)[None]
    ch, sh = jnp.cos(high_angle)[:, None], jnp.sin(high_angle)[:, None]
    cosine = (ch * cl - sh * sl).reshape(samples, bins)
    sine = (sh * cl + ch * sl).reshape(samples, bins)
    return jnp.concatenate([cosine, -sine], axis=1)


def band_matrix(bins):
    g = jnp.arange(bins, dtype=jnp.int32)
    near = jnp.abs(g[:, None] - g[None, :]) <= HALF_BAND
    return near.astype(jnp.bfloat16)


def lag_kernel(samples, first_lag, lag_count):
    bin_count = samples // 2
    inner = 32
    frequency = jnp.arange(bin_count, dtype=jnp.int32)[:, None]
    low = jnp.arange(inner, dtype=jnp.int32)[None, :]
    high = first_lag - LAGS // 2 + jnp.arange(lag_count // inner, dtype=jnp.int32)[None, :] * inner
    scale = two_pi / samples
    low_angle = jnp.mod(frequency * low, samples).astype(jnp.float32) * scale
    high_angle = jnp.mod(frequency * high, samples).astype(jnp.float32) * scale
    cl, sl = jnp.cos(low_angle)[:, None, :], jnp.sin(low_angle)[:, None, :]
    ch, sh = jnp.cos(high_angle)[:, :, None], jnp.sin(high_angle)[:, :, None]
    cosine = (ch * cl - sh * sl).reshape(bin_count, lag_count)
    sine = (sh * cl + ch * sl).reshape(bin_count, lag_count)
    return jnp.concatenate([cosine, -sine], axis=0).astype(jnp.bfloat16)


def whiten_series(series, table):
    samples = series.shape[1]
    bins = samples // 2
    spectrum = jnp.dot(series, table.astype(jnp.bfloat16), preferred_element_type=jnp.float32)
    real_part = spectrum[:, :bins]
    imag_part = spectrum[:, bins:]
    powers = real_part * real_part + imag_part * imag_part
    window = jnp.dot(powers.astype(jnp.bfloat16), band_matrix(bins), preferred_element_type=jnp.float32)
    window_span = 2 * HALF_BAND + 1
    factor = 1.0 / jnp.sqrt(window / window_span + epsilon)
    return jnp.concatenate([real_part * factor, imag_part * factor], axis=1).astype(jnp.bfloat16)


def correlate_kernel(factor, bins, group, half, mine_ref, other_ref, lag_ref, out_ref):
    step = pl.program_id(0)
    first = lax.axis_index("tm") == 0
    lag = lag_ref[...]
    receivers = [mine_ref[:half, :].astype(jnp.float32), other_ref[:half, :].astype(jnp.float32)]
    places = [jnp.where(first, 0, half), jnp.where(first, half, 0)]
    mine_src = mine_ref[half:, :]
    other_src = other_ref[half:, :]
    every = jnp.where(
        first,
        jnp.concatenate([mine_src, other_src], axis=0),
        jnp.concatenate([other_src, mine_src], axis=0),
    ).astype(jnp.float32)
    picked = every[:group]
    for g in range(1, every.shape[0] // group):
        picked = jnp.where(step == g, every[g * group : (g + 1) * group], picked)
    for k in range(group):
        row = picked[k : k + 1]
        real_src = row[:, :bins]
        imag_src = row[:, bins:]
        for part, rcv in enumerate(receivers):
            real_rcv = rcv[:, :bins]
            imag_rcv = rcv[:, bins:]
            cross = jnp.concatenate(
                [real_src * real_rcv + imag_src * imag_rcv, imag_src * real_rcv - real_src * imag_rcv],
                axis=1,
            ).astype(jnp.bfloat16)
            out_ref[k, pl.ds(pl.multiple_of(places[part], 8), half), :] = (
                jnp.dot(cross, lag, preferred_element_type=jnp.float32) * factor
            )


def correlate(low, high, half, lag):
    rows, width = low.shape
    bins = width // 2
    count = 2 * (rows - half)
    block = 2 * half
    lags = lag.shape[1]
    group = 8
    factor = 1.0 / math.sqrt(bins)
    flops = 2 * count * block * width * lags + 6 * count * block * bins
    moved = 4 * rows * width + 2 * lags * width + 4 * count * block * lags
    return pl.pallas_call(
        functools.partial(correlate_kernel, factor, bins, group, half),
        out_shape=jax.ShapeDtypeStruct((count, block, lags), jnp.float32),
        grid=(count // group,),
        in_specs=[
            pl.BlockSpec((rows, width), lambda s: (0, 0)),
            pl.BlockSpec((rows, width), lambda s: (0, 0)),
            pl.BlockSpec((width, lags), lambda s: (0, 0)),
        ],
        out_specs=pl.BlockSpec((group, block, lags), lambda s: (s, 0, 0)),
        compiler_params=pltpu.CompilerParams(dimension_semantics=("arbitrary",)),
        cost_estimate=pl.CostEstimate(flops=flops, bytes_accessed=moved, transcendentals=0),
    )(low, high, lag)


def swap_tm(x):
    other = lax.ppermute(x, "tm", perm=[(0, 1), (1, 0)])
    first = lax.axis_index("tm") == 0
    return jnp.where(first, x, other), jnp.where(first, other, x)


def local(records, fir_taps, channel_map, source_owner, source_offset):
    n_chan = lax.axis_size("chan")
    n_tm = lax.axis_size("tm")
    assert n_tm == 2
    n_dev = n_chan * n_tm
    raw_rows, channels = records.shape
    block = channels // n_chan
    half = block // n_tm
    out_rows = raw_rows // STRIDE
    halo_rows = TAPS - STRIDE
    samples = out_rows * n_dev
    bins = samples // 2
    tm = lax.axis_index("tm")

    shift = [(b, b - 1) for b in range(1, n_dev)]
    halo = lax.ppermute(records[:halo_rows], ("chan", "tm"), perm=shift)

    taps_matrix = decimation_matrix(fir_taps, out_rows, raw_rows + halo_rows)
    main = jnp.dot(taps_matrix[:, :raw_rows], records, preferred_element_type=jnp.float32)
    tail = jnp.dot(taps_matrix[:, raw_rows:], halo, preferred_element_type=jnp.float32)
    decimated = (main + tail).astype(jnp.bfloat16)

    first, second = swap_tm(decimated)
    paired = jnp.concatenate([first, second], axis=0).T

    steps = jnp.arange(source_owner.shape[0], dtype=jnp.int32)
    own_first = jnp.sum(jnp.where(steps == tm, source_owner * block + source_offset, 0))
    source_raw = lax.dynamic_slice_in_dim(channel_map, own_first, SRC)
    half_raw = lax.dynamic_slice(channel_map.reshape(n_chan, block), (0, tm * half), (n_chan, half))
    index = jnp.concatenate(
        [half_raw, jnp.broadcast_to(source_raw[None], (n_chan, SRC))], axis=1
    )
    width = index.shape[1]
    rows = jnp.take(paired, index.reshape(-1), axis=0, mode="clip").reshape(n_chan, width, -1)
    series = lax.all_to_all(rows, "chan", 0, 2, tiled=True).reshape(width, samples)
    table = dft_table(samples, bins, jnp.arange(samples, dtype=jnp.int32))
    lag_share = LAGS // n_tm
    lag = lag_kernel(samples, tm * lag_share, lag_share)

    white = whiten_series(series, table)
    other = lax.ppermute(white, "tm", perm=[(0, 1), (1, 0)])
    result = correlate(white, other, half, lag)
    return result.reshape(STEPS, SRC, block, lag_share)


def solution(mesh):
    return jax.shard_map(
        local,
        mesh=mesh,
        in_specs=(P(("chan", "tm"), "parts"), P(), P("parts"), P("parts"), P("parts")),
        out_specs=P(None, None, ("parts", "chan"), "tm"),
        check_vma=False,
    )
```

```python
import functools
import math

import jax
import jax.numpy as jnp
from jax import lax
from jax.experimental import pallas as pl
from jax.experimental.pallas import tpu as pltpu
from jax.sharding import PartitionSpec as P

SRC = 16
STEPS = 2
LAGS = 512
TAPS = 32
STRIDE = 8
HALF_BAND = 32

two_pi = 2.0 * math.pi
epsilon = 1e-06


def decimation_matrix(fir_taps, out_rows, in_rows):
    leads = TAPS // STRIDE
    rows = jnp.arange(out_rows, dtype=jnp.int32)[:, None, None, None]
    groups = jnp.arange(in_rows // STRIDE, dtype=jnp.int32)[None, :, None, None]
    lead = jnp.arange(leads, dtype=jnp.int32)[None, None, :, None]
    taps = fir_taps.reshape(1, 1, leads, STRIDE)
    matrix = jnp.where(groups - rows == lead, taps, 0.0).sum(axis=2)
    return matrix.reshape(out_rows, in_rows)


def dft_table(samples, bins, time_index):
    inner = 32
    outer = samples // inner
    frequency = jnp.arange(bins, dtype=jnp.int32)[None, :]
    low = jnp.arange(inner, dtype=jnp.int32)[:, None]
    high = time_index.reshape(outer, inner)[:, :1]
    scale = two_pi / samples
    low_angle = ((low * frequency) % samples).astype(jnp.float32) * scale
    high_angle = ((high * frequency) % samples).astype(jnp.float32) * scale
    cl, sl = jnp.cos(low_angle)[None], jnp.sin(low_angle)[None]
    ch, sh = jnp.cos(high_angle)[:, None], jnp.sin(high_angle)[:, None]
    cosine = (ch * cl - sh * sl).reshape(samples, bins)
    sine = (sh * cl + ch * sl).reshape(samples, bins)
    return jnp.concatenate([cosine, -sine], axis=1)


def band_matrix(bins):
    g = jnp.arange(bins, dtype=jnp.int32)
    near = jnp.abs(g[:, None] - g[None, :]) <= HALF_BAND
    return near.astype(jnp.bfloat16)


def lag_kernel(samples, first_lag, lag_count):
    bin_count = samples // 2
    inner = 32
    frequency = jnp.arange(bin_count, dtype=jnp.int32)[:, None]
    low = jnp.arange(inner, dtype=jnp.int32)[None, :]
    high = first_lag - LAGS // 2 + jnp.arange(lag_count // inner, dtype=jnp.int32)[None, :] * inner
    scale = two_pi / samples
    low_angle = jnp.mod(frequency * low, samples).astype(jnp.float32) * scale
    high_angle = jnp.mod(frequency * high, samples).astype(jnp.float32) * scale
    cl, sl = jnp.cos(low_angle)[:, None, :], jnp.sin(low_angle)[:, None, :]
    ch, sh = jnp.cos(high_angle)[:, :, None], jnp.sin(high_angle)[:, :, None]
    cosine = (ch * cl - sh * sl).reshape(bin_count, lag_count)
    sine = (sh * cl + ch * sl).reshape(bin_count, lag_count)
    return jnp.concatenate([cosine, -sine], axis=0).astype(jnp.bfloat16)


def whiten_series(series, table):
    samples = series.shape[1]
    bins = samples // 2
    spectrum = jnp.dot(series, table.astype(jnp.bfloat16), preferred_element_type=jnp.float32)
    real_part = spectrum[:, :bins]
    imag_part = spectrum[:, bins:]
    powers = real_part * real_part + imag_part * imag_part
    window = jnp.dot(powers.astype(jnp.bfloat16), band_matrix(bins), preferred_element_type=jnp.float32)
    window_span = 2 * HALF_BAND + 1
    factor = 1.0 / jnp.sqrt(window / window_span + epsilon)
    return jnp.concatenate([real_part * factor, imag_part * factor], axis=1).astype(jnp.bfloat16)


def correlate_kernel(factor, bins, group, half, mine_ref, other_ref, lag_ref, out_ref):
    step = pl.program_id(0)
    first = lax.axis_index("tm") == 0
    lag = lag_ref[...]
    receivers = [mine_ref[:half, :].astype(jnp.float32), other_ref[:half, :].astype(jnp.float32)]
    places = [jnp.where(first, 0, half), jnp.where(first, half, 0)]
    mine_src = mine_ref[half:, :]
    other_src = other_ref[half:, :]
    every = jnp.where(
        first,
        jnp.concatenate([mine_src, other_src], axis=0),
        jnp.concatenate([other_src, mine_src], axis=0),
    ).astype(jnp.float32)
    picked = every[:group]
    for g in range(1, every.shape[0] // group):
        picked = jnp.where(step == g, every[g * group : (g + 1) * group], picked)
    for k in range(group):
        row = picked[k : k + 1]
        real_src = row[:, :bins]
        imag_src = row[:, bins:]
        for part, rcv in enumerate(receivers):
            real_rcv = rcv[:, :bins]
            imag_rcv = rcv[:, bins:]
            cross = jnp.concatenate(
                [real_src * real_rcv + imag_src * imag_rcv, imag_src * real_rcv - real_src * imag_rcv],
                axis=1,
            ).astype(jnp.bfloat16)
            out_ref[k, pl.ds(pl.multiple_of(places[part], 8), half), :] = (
                jnp.dot(cross, lag, preferred_element_type=jnp.float32) * factor
            )


def correlate(low, high, half, lag):
    rows, width = low.shape
    bins = width // 2
    count = 2 * (rows - half)
    block = 2 * half
    lags = lag.shape[1]
    group = 8
    factor = 1.0 / math.sqrt(bins)
    flops = 2 * count * block * width * lags + 6 * count * block * bins
    moved = 4 * rows * width + 2 * lags * width + 4 * count * block * lags
    return pl.pallas_call(
        functools.partial(correlate_kernel, factor, bins, group, half),
        out_shape=jax.ShapeDtypeStruct((count, block, lags), jnp.float32),
        grid=(count // group,),
        in_specs=[
            pl.BlockSpec((rows, width), lambda s: (0, 0)),
            pl.BlockSpec((rows, width), lambda s: (0, 0)),
            pl.BlockSpec((width, lags), lambda s: (0, 0)),
        ],
        out_specs=pl.BlockSpec((group, block, lags), lambda s: (s, 0, 0)),
        compiler_params=pltpu.CompilerParams(dimension_semantics=("arbitrary",)),
        cost_estimate=pl.CostEstimate(flops=flops, bytes_accessed=moved, transcendentals=0),
    )(low, high, lag)


def swap_tm(x):
    other = lax.ppermute(x, "tm", perm=[(0, 1), (1, 0)])
    first = lax.axis_index("tm") == 0
    return jnp.where(first, x, other), jnp.where(first, other, x)


def local(records, fir_taps, channel_map, source_owner, source_offset):
    n_chan = lax.axis_size("chan")
    n_tm = lax.axis_size("tm")
    assert n_tm == 2
    n_dev = n_chan * n_tm
    raw_rows, channels = records.shape
    block = channels // n_chan
    half = block // n_tm
    out_rows = raw_rows // STRIDE
    halo_rows = TAPS - STRIDE
    samples = out_rows * n_dev
    bins = samples // 2
    tm = lax.axis_index("tm")

    shift = [(b, b - 1) for b in range(1, n_dev)]
    halo = lax.ppermute(records[:halo_rows], ("chan", "tm"), perm=shift)

    taps_matrix = decimation_matrix(fir_taps, out_rows, raw_rows + halo_rows)
    taps_matrix = taps_matrix.astype(jnp.bfloat16)
    dims = (((0,), (1,)), ((), ()))
    main = lax.dot_general(records, taps_matrix[:, :raw_rows], dims, preferred_element_type=jnp.float32)
    tail = lax.dot_general(halo, taps_matrix[:, raw_rows:], dims, preferred_element_type=jnp.float32)
    decimated = (main + tail).astype(jnp.bfloat16)

    first, second = swap_tm(decimated)
    paired = jnp.concatenate([first, second], axis=1)

    steps = jnp.arange(source_owner.shape[0], dtype=jnp.int32)
    own_first = jnp.sum(jnp.where(steps == tm, source_owner * block + source_offset, 0))
    source_raw = lax.dynamic_slice_in_dim(channel_map, own_first, SRC)
    half_raw = lax.dynamic_slice(channel_map.reshape(n_chan, block), (0, tm * half), (n_chan, half))
    index = jnp.concatenate(
        [half_raw, jnp.broadcast_to(source_raw[None], (n_chan, SRC))], axis=1
    )
    width = index.shape[1]
    rows = jnp.take(paired, index.reshape(-1), axis=0, mode="clip").reshape(n_chan, width, -1)
    series = lax.all_to_all(rows, "chan", 0, 2, tiled=True).reshape(width, samples)
    table = dft_table(samples, bins, jnp.arange(samples, dtype=jnp.int32))
    lag_share = LAGS // n_tm
    lag = lag_kernel(samples, tm * lag_share, lag_share)

    white = whiten_series(series, table)
    other = lax.ppermute(white, "tm", perm=[(0, 1), (1, 0)])
    result = correlate(white, other, half, lag)
    return result.reshape(STEPS, SRC, block, lag_share)


def solution(mesh):
    return jax.shard_map(
        local,
        mesh=mesh,
        in_specs=(P(("chan", "tm"), "parts"), P(), P("parts"), P("parts"), P("parts")),
        out_specs=P(None, None, ("parts", "chan"), "tm"),
        check_vma=False,
    )
```

```python
import functools
import math

import jax
import jax.numpy as jnp
from jax import lax
from jax.experimental import pallas as pl
from jax.experimental.pallas import tpu as pltpu
from jax.sharding import PartitionSpec as P

SRC = 16
STEPS = 2
LAGS = 512
TAPS = 32
STRIDE = 8
HALF_BAND = 32

two_pi = 2.0 * math.pi
epsilon = 1e-06


def decimation_matrix(fir_taps, out_rows, in_rows):
    leads = TAPS // STRIDE
    rows = jnp.arange(out_rows, dtype=jnp.int32)[:, None, None, None]
    groups = jnp.arange(in_rows // STRIDE, dtype=jnp.int32)[None, :, None, None]
    lead = jnp.arange(leads, dtype=jnp.int32)[None, None, :, None]
    taps = fir_taps.reshape(1, 1, leads, STRIDE)
    matrix = jnp.where(groups - rows == lead, taps, 0.0).sum(axis=2)
    return matrix.reshape(out_rows, in_rows)


def dft_table(samples, bins, time_index):
    inner = 32
    outer = samples // inner
    frequency = jnp.arange(bins, dtype=jnp.int32)[None, :]
    low = jnp.arange(inner, dtype=jnp.int32)[:, None]
    high = time_index.reshape(outer, inner)[:, :1]
    scale = two_pi / samples
    low_angle = ((low * frequency) % samples).astype(jnp.float32) * scale
    high_angle = ((high * frequency) % samples).astype(jnp.float32) * scale
    cl, sl = jnp.cos(low_angle)[None], jnp.sin(low_angle)[None]
    ch, sh = jnp.cos(high_angle)[:, None], jnp.sin(high_angle)[:, None]
    cosine = (ch * cl - sh * sl).reshape(samples, bins)
    sine = (sh * cl + ch * sl).reshape(samples, bins)
    return jnp.concatenate([cosine, -sine], axis=1)


def band_matrix(bins):
    g = jnp.arange(bins, dtype=jnp.int32)
    near = jnp.abs(g[:, None] - g[None, :]) <= HALF_BAND
    return near.astype(jnp.bfloat16)


def lag_kernel(samples, first_lag, lag_count):
    bin_count = samples // 2
    inner = 32
    frequency = jnp.arange(bin_count, dtype=jnp.int32)[:, None]
    low = jnp.arange(inner, dtype=jnp.int32)[None, :]
    high = first_lag - LAGS // 2 + jnp.arange(lag_count // inner, dtype=jnp.int32)[None, :] * inner
    scale = two_pi / samples
    low_angle = jnp.mod(frequency * low, samples).astype(jnp.float32) * scale
    high_angle = jnp.mod(frequency * high, samples).astype(jnp.float32) * scale
    cl, sl = jnp.cos(low_angle)[:, None, :], jnp.sin(low_angle)[:, None, :]
    ch, sh = jnp.cos(high_angle)[:, :, None], jnp.sin(high_angle)[:, :, None]
    cosine = (ch * cl - sh * sl).reshape(bin_count, lag_count)
    sine = (sh * cl + ch * sl).reshape(bin_count, lag_count)
    return jnp.concatenate([cosine, -sine], axis=0).astype(jnp.bfloat16)


def whiten_series(series, table):
    samples = series.shape[1]
    bins = samples // 2
    spectrum = jnp.dot(series, table.astype(jnp.bfloat16), preferred_element_type=jnp.float32)
    real_part = spectrum[:, :bins]
    imag_part = spectrum[:, bins:]
    powers = real_part * real_part + imag_part * imag_part
    window = jnp.dot(powers.astype(jnp.bfloat16), band_matrix(bins), preferred_element_type=jnp.float32)
    window_span = 2 * HALF_BAND + 1
    factor = 1.0 / jnp.sqrt(window / window_span + epsilon)
    return jnp.concatenate([real_part * factor, imag_part * factor], axis=1).astype(jnp.bfloat16)


def correlate_kernel(factor, bins, group, half, mine_ref, other_ref, lag_ref, out_ref):
    step = pl.program_id(0)
    first = lax.axis_index("tm") == 0
    lag = lag_ref[...]
    receivers = [mine_ref[:half, :].astype(jnp.float32), other_ref[:half, :].astype(jnp.float32)]
    places = [jnp.where(first, 0, half), jnp.where(first, half, 0)]
    mine_src = mine_ref[half:, :]
    other_src = other_ref[half:, :]
    every = jnp.where(
        first,
        jnp.concatenate([mine_src, other_src], axis=0),
        jnp.concatenate([other_src, mine_src], axis=0),
    ).astype(jnp.float32)
    picked = every[:group]
    for g in range(1, every.shape[0] // group):
        picked = jnp.where(step == g, every[g * group : (g + 1) * group], picked)
    for k in range(group):
        row = picked[k : k + 1]
        real_src = row[:, :bins]
        imag_src = row[:, bins:]
        for part, rcv in enumerate(receivers):
            real_rcv = rcv[:, :bins]
            imag_rcv = rcv[:, bins:]
            cross = jnp.concatenate(
                [real_src * real_rcv + imag_src * imag_rcv, imag_src * real_rcv - real_src * imag_rcv],
                axis=1,
            ).astype(jnp.bfloat16)
            out_ref[k, pl.ds(pl.multiple_of(places[part], 8), half), :] = (
                jnp.dot(cross, lag, preferred_element_type=jnp.float32) * factor
            )


def correlate(low, high, half, lag):
    rows, width = low.shape
    bins = width // 2
    count = 2 * (rows - half)
    block = 2 * half
    lags = lag.shape[1]
    group = 8
    factor = 1.0 / math.sqrt(bins)
    flops = 2 * count * block * width * lags + 6 * count * block * bins
    moved = 4 * rows * width + 2 * lags * width + 4 * count * block * lags
    return pl.pallas_call(
        functools.partial(correlate_kernel, factor, bins, group, half),
        out_shape=jax.ShapeDtypeStruct((count, block, lags), jnp.float32),
        grid=(count // group,),
        in_specs=[
            pl.BlockSpec((rows, width), lambda s: (0, 0)),
            pl.BlockSpec((rows, width), lambda s: (0, 0)),
            pl.BlockSpec((width, lags), lambda s: (0, 0)),
        ],
        out_specs=pl.BlockSpec((group, block, lags), lambda s: (s, 0, 0)),
        compiler_params=pltpu.CompilerParams(dimension_semantics=("arbitrary",)),
        cost_estimate=pl.CostEstimate(flops=flops, bytes_accessed=moved, transcendentals=0),
    )(low, high, lag)


def swap_tm(x):
    other = lax.ppermute(x, "tm", perm=[(0, 1), (1, 0)])
    first = lax.axis_index("tm") == 0
    return jnp.where(first, x, other), jnp.where(first, other, x)


def local(records, fir_taps, channel_map, source_owner, source_offset):
    n_chan = lax.axis_size("chan")
    n_tm = lax.axis_size("tm")
    assert n_tm == 2
    n_dev = n_chan * n_tm
    raw_rows, channels = records.shape
    block = channels // n_chan
    half = block // n_tm
    out_rows = raw_rows // STRIDE
    halo_rows = TAPS - STRIDE
    samples = out_rows * n_dev
    bins = samples // 2
    tm = lax.axis_index("tm")

    shift = [(b, b - 1) for b in range(1, n_dev)]
    halo = lax.ppermute(records[:halo_rows], ("chan", "tm"), perm=shift)

    taps_matrix = decimation_matrix(fir_taps, out_rows, raw_rows + halo_rows)
    taps_matrix = taps_matrix.astype(jnp.bfloat16)
    main = jnp.dot(taps_matrix[:, :raw_rows], records, preferred_element_type=jnp.float32)
    tail = jnp.dot(taps_matrix[:, raw_rows:], halo, preferred_element_type=jnp.float32)
    decimated = (main + tail).astype(jnp.bfloat16)

    other = lax.ppermute(decimated, "tm", perm=[(0, 1), (1, 0)])
    paired = jnp.concatenate([decimated, other], axis=0).T

    steps = jnp.arange(source_owner.shape[0], dtype=jnp.int32)
    own_first = jnp.sum(jnp.where(steps == tm, source_owner * block + source_offset, 0))
    source_raw = lax.dynamic_slice_in_dim(channel_map, own_first, SRC)
    half_raw = lax.dynamic_slice(channel_map.reshape(n_chan, block), (0, tm * half), (n_chan, half))
    index = jnp.concatenate(
        [half_raw, jnp.broadcast_to(source_raw[None], (n_chan, SRC))], axis=1
    )
    width = index.shape[1]
    rows = jnp.take(paired, index.reshape(-1), axis=0, mode="clip").reshape(n_chan, width, -1)
    series = lax.all_to_all(rows, "chan", 0, 2, tiled=True).reshape(width, samples)
    chunk = 2 * out_rows
    column = jnp.arange(samples, dtype=jnp.int32)
    time_index = column - column % chunk + (column % chunk + tm * out_rows) % chunk
    table = dft_table(samples, bins, time_index)
    lag_share = LAGS // n_tm
    lag = lag_kernel(samples, tm * lag_share, lag_share)

    white = whiten_series(series, table)
    other = lax.ppermute(white, "tm", perm=[(0, 1), (1, 0)])
    result = correlate(white, other, half, lag)
    return result.reshape(STEPS, SRC, block, lag_share)


def solution(mesh):
    return jax.shard_map(
        local,
        mesh=mesh,
        in_specs=(P(("chan", "tm"), "parts"), P(), P("parts"), P("parts"), P("parts")),
        out_specs=P(None, None, ("parts", "chan"), "tm"),
        check_vma=False,
    )
```

```python
import functools
import math

import jax
import jax.numpy as jnp
from jax import lax
from jax.experimental import pallas as pl
from jax.experimental.pallas import tpu as pltpu
from jax.sharding import PartitionSpec as P

SRC = 16
STEPS = 2
LAGS = 512
TAPS = 32
STRIDE = 8
HALF_BAND = 32

two_pi = 2.0 * math.pi
epsilon = 1e-06


def decimation_matrix(fir_taps, out_rows, in_rows):
    leads = TAPS // STRIDE
    rows = jnp.arange(out_rows, dtype=jnp.int32)[:, None, None, None]
    groups = jnp.arange(in_rows // STRIDE, dtype=jnp.int32)[None, :, None, None]
    lead = jnp.arange(leads, dtype=jnp.int32)[None, None, :, None]
    taps = fir_taps.reshape(1, 1, leads, STRIDE)
    matrix = jnp.where(groups - rows == lead, taps, 0.0).sum(axis=2)
    return matrix.reshape(out_rows, in_rows)


def dft_table(samples, bins, time_index):
    inner = 32
    outer = samples // inner
    frequency = jnp.arange(bins, dtype=jnp.int32)[None, :]
    low = jnp.arange(inner, dtype=jnp.int32)[:, None]
    high = time_index.reshape(outer, inner)[:, :1]
    scale = two_pi / samples
    low_angle = ((low * frequency) % samples).astype(jnp.float32) * scale
    high_angle = ((high * frequency) % samples).astype(jnp.float32) * scale
    cl, sl = jnp.cos(low_angle)[None], jnp.sin(low_angle)[None]
    ch, sh = jnp.cos(high_angle)[:, None], jnp.sin(high_angle)[:, None]
    cosine = (ch * cl - sh * sl).reshape(samples, bins)
    sine = (sh * cl + ch * sl).reshape(samples, bins)
    return jnp.concatenate([cosine, -sine], axis=1)


def band_matrix(bins):
    g = jnp.arange(bins, dtype=jnp.int32)
    near = jnp.abs(g[:, None] - g[None, :]) <= HALF_BAND
    return near.astype(jnp.bfloat16)


def lag_kernel(samples, first_lag, lag_count):
    bin_count = samples // 2
    inner = 32
    frequency = jnp.arange(bin_count, dtype=jnp.int32)[:, None]
    low = jnp.arange(inner, dtype=jnp.int32)[None, :]
    high = first_lag - LAGS // 2 + jnp.arange(lag_count // inner, dtype=jnp.int32)[None, :] * inner
    scale = two_pi / samples
    low_angle = jnp.mod(frequency * low, samples).astype(jnp.float32) * scale
    high_angle = jnp.mod(frequency * high, samples).astype(jnp.float32) * scale
    cl, sl = jnp.cos(low_angle)[:, None, :], jnp.sin(low_angle)[:, None, :]
    ch, sh = jnp.cos(high_angle)[:, :, None], jnp.sin(high_angle)[:, :, None]
    cosine = (ch * cl - sh * sl).reshape(bin_count, lag_count)
    sine = (sh * cl + ch * sl).reshape(bin_count, lag_count)
    return jnp.concatenate([cosine, -sine], axis=0).astype(jnp.bfloat16)


def whiten_series(series, table):
    samples = series.shape[1]
    bins = samples // 2
    spectrum = jnp.dot(series, table.astype(jnp.bfloat16), preferred_element_type=jnp.float32)
    real_part = spectrum[:, :bins]
    imag_part = spectrum[:, bins:]
    powers = real_part * real_part + imag_part * imag_part
    window = jnp.dot(powers.astype(jnp.bfloat16), band_matrix(bins), preferred_element_type=jnp.float32)
    window_span = 2 * HALF_BAND + 1
    factor = 1.0 / jnp.sqrt(window / window_span + epsilon)
    return jnp.concatenate([real_part * factor, imag_part * factor], axis=1).astype(jnp.bfloat16)


def correlate_kernel(factor, bins, group, half, mine_ref, other_ref, lag_ref, out_ref):
    step = pl.program_id(0)
    first = lax.axis_index("tm") == 0
    lag = lag_ref[...]
    receivers = [mine_ref[:half, :].astype(jnp.float32), other_ref[:half, :].astype(jnp.float32)]
    places = [jnp.where(first, 0, half), jnp.where(first, half, 0)]
    mine_src = mine_ref[half:, :]
    other_src = other_ref[half:, :]
    every = jnp.where(
        first,
        jnp.concatenate([mine_src, other_src], axis=0),
        jnp.concatenate([other_src, mine_src], axis=0),
    ).astype(jnp.float32)
    picked = every[:group]
    for g in range(1, every.shape[0] // group):
        picked = jnp.where(step == g, every[g * group : (g + 1) * group], picked)
    for k in range(group):
        row = picked[k : k + 1]
        real_src = row[:, :bins]
        imag_src = row[:, bins:]
        for part, rcv in enumerate(receivers):
            real_rcv = rcv[:, :bins]
            imag_rcv = rcv[:, bins:]
            cross = jnp.concatenate(
                [real_src * real_rcv + imag_src * imag_rcv, imag_src * real_rcv - real_src * imag_rcv],
                axis=1,
            ).astype(jnp.bfloat16)
            out_ref[k, pl.ds(pl.multiple_of(places[part], 8), half), :] = (
                jnp.dot(cross, lag, preferred_element_type=jnp.float32) * factor
            )


def correlate(low, high, half, lag):
    rows, width = low.shape
    bins = width // 2
    count = 2 * (rows - half)
    block = 2 * half
    lags = lag.shape[1]
    group = 8
    factor = 1.0 / math.sqrt(bins)
    flops = 2 * count * block * width * lags + 6 * count * block * bins
    moved = 4 * rows * width + 2 * lags * width + 4 * count * block * lags
    return pl.pallas_call(
        functools.partial(correlate_kernel, factor, bins, group, half),
        out_shape=jax.ShapeDtypeStruct((count, block, lags), jnp.float32),
        grid=(count // group,),
        in_specs=[
            pl.BlockSpec((rows, width), lambda s: (0, 0)),
            pl.BlockSpec((rows, width), lambda s: (0, 0)),
            pl.BlockSpec((width, lags), lambda s: (0, 0)),
        ],
        out_specs=pl.BlockSpec((group, block, lags), lambda s: (s, 0, 0)),
        compiler_params=pltpu.CompilerParams(dimension_semantics=("arbitrary",)),
        cost_estimate=pl.CostEstimate(flops=flops, bytes_accessed=moved, transcendentals=0),
    )(low, high, lag)


def swap_tm(x):
    other = lax.ppermute(x, "tm", perm=[(0, 1), (1, 0)])
    first = lax.axis_index("tm") == 0
    return jnp.where(first, x, other), jnp.where(first, other, x)


def local(records, fir_taps, channel_map, source_owner, source_offset):
    n_chan = lax.axis_size("chan")
    n_tm = lax.axis_size("tm")
    assert n_tm == 2
    n_dev = n_chan * n_tm
    raw_rows, channels = records.shape
    block = channels // n_chan
    half = block // n_tm
    out_rows = raw_rows // STRIDE
    halo_rows = TAPS - STRIDE
    samples = out_rows * n_dev
    bins = samples // 2
    tm = lax.axis_index("tm")

    shift = [(b, b - 1) for b in range(1, n_dev)]
    halo = lax.ppermute(records[:halo_rows], ("chan", "tm"), perm=shift)

    taps_matrix = decimation_matrix(fir_taps, out_rows, raw_rows + halo_rows)
    taps_matrix = taps_matrix.astype(jnp.bfloat16)
    main = jnp.dot(taps_matrix[:, :raw_rows], records, preferred_element_type=jnp.float32)
    tail = jnp.dot(taps_matrix[:, raw_rows:], halo, preferred_element_type=jnp.float32)
    decimated = (main + tail).astype(jnp.bfloat16)

    first, second = swap_tm(decimated)
    paired = jnp.concatenate([first, second], axis=0).T

    steps = jnp.arange(source_owner.shape[0], dtype=jnp.int32)
    own_first = jnp.sum(jnp.where(steps == tm, source_owner * block + source_offset, 0))
    source_raw = lax.dynamic_slice_in_dim(channel_map, own_first, SRC)
    half_raw = lax.dynamic_slice(channel_map.reshape(n_chan, block), (0, tm * half), (n_chan, half))
    index = jnp.concatenate(
        [half_raw, jnp.broadcast_to(source_raw[None], (n_chan, SRC))], axis=1
    )
    width = index.shape[1]
    rows = paired.at[index.reshape(-1)].get(mode="promise_in_bounds").reshape(n_chan, width, -1)
    series = lax.all_to_all(rows, "chan", 0, 2, tiled=True).reshape(width, samples)
    table = dft_table(samples, bins, jnp.arange(samples, dtype=jnp.int32))
    lag_share = LAGS // n_tm
    lag = lag_kernel(samples, tm * lag_share, lag_share)

    white = whiten_series(series, table)
    other = lax.ppermute(white, "tm", perm=[(0, 1), (1, 0)])
    result = correlate(white, other, half, lag)
    return result.reshape(STEPS, SRC, block, lag_share)


def solution(mesh):
    return jax.shard_map(
        local,
        mesh=mesh,
        in_specs=(P(("chan", "tm"), "parts"), P(), P("parts"), P("parts"), P("parts")),
        out_specs=P(None, None, ("parts", "chan"), "tm"),
        check_vma=False,
    )
```
